32 devices in a mesh: clip: 2 (over x), gx: 8 (over z, y), gy: 2 (over core).
Axes of the slice: x: 2, y: 2, z: 4, core: 2. Of those that a mesh axis runs over, the one named last changes fastest.
Arguments:
- e_field: float32 [3, 128, 128, 128], P(None, ('clip', 'gx'), 'gy'), parts along dimension 1, may hold values from -6 to 6
- h_field: float32 [3, 128, 128, 128], P(None, ('clip', 'gx'), 'gy'), parts along dimension 1, may hold values from -6 to 6
- material: int32 [128, 128, 128], P(('clip', 'gx'), 'gy'), parts along dimension 0, may hold values from 0 to 5
- eps_table: float32 [6], replicated, may hold values from 0.8 to 1.2
- sigma_table: float32 [6], replicated, may hold values from 0 to 2
- angle_orders: int32 [64, 2], replicated, may hold values from -8 to 8
Outputs:
- e_out: float32 [3, 128, 128, 128], P(None, ('clip', 'gx'), 'gy'), parts along dimension 1
- h_out: float32 [3, 128, 128, 128], P(None, ('clip', 'gx'), 'gy'), parts along dimension 1
- far_field: float32 [128, 4], P(('clip', 'gx')), parts along dimension 0
The draws below stay inside these ranges and needn't reach their ends.
There are 2 independent parts, one for each index of `clip`. The reference program is written for one: setup_inputs(seed, part) draws one part's arguments, and reference() takes and returns one part's arrays. A program takes and returns all parts, laid end to end along the dimension named above; an argument that names none is the same for every part. Nothing has to cross between parts.
All inputs are finite; a program needn't handle non-finite values.
Results may differ from the reference program's by a relative error of at most 0.00021.
Values sent between devices are 32-bit elements; how exact they have to be, the bound alone decides.
No kernel may reach another device: no remote copies, remote signals or barrier semaphores. Data moves between devices by JAX's collectives and lax.ppermute only.
A program may use at most 64 MiB of HBM per device.

```python
import math
import jax
import jax.numpy as jnp
from jax import lax

NZ = 128
BILAYERS = 18
MATS = 6
ANGLES = 64
ITERS = 4
NX = 64
NY = 128


def draw_material(key, part):
    key_pattern = jax.random.fold_in(key, 11)
    key_mixing = jax.random.fold_in(key, 12)
    key_random = jax.random.fold_in(key, 13)
    depth = jnp.arange(NZ, dtype=jnp.int32)
    period = depth % 6
    stack_ids = jnp.where(period < 2, 1, jnp.where(period == 2, 4, 2))
    summit = 6 * BILAYERS
    column = jnp.where(depth < summit, stack_ids, jnp.where(depth < summit + 2, 3, jnp.where(depth < summit + 10, 5, 0)))
    pattern = jax.random.randint(key_pattern, (NX, NY), 0, 2)
    pattern = pattern.at[0].set(1)
    absorber_band = (depth >= summit + 2) & (depth < summit + 10)
    layered = jnp.where(absorber_band[None, None, :] & (pattern[:, :, None] == 0), 0, column[None, None, :])
    mixing = jax.random.randint(key_mixing, (NX, NY, NZ), 0, 4)
    random_ids = jax.random.randint(key_random, (NX, NY, NZ), 0, MATS)
    return jnp.where(mixing == 0, random_ids, layered).astype(jnp.int32)


def place_ends(result, key, smallest, high):
    longest = result.shape.index(max(result.shape))
    spots = []
    for shift in (0, 1):
        where = [jax.random.randint(jax.random.fold_in(key, axis), (), 0, length) for axis, length in enumerate(result.shape)]
        where[longest] = (where[longest] + shift) % result.shape[longest]
        spots.append(tuple(where))
    return result.at[spots[0]].set(smallest).at[spots[1]].set(high)


def levels(key, shape, cuts, low, high):
    level = 1.0
    for axis_at, blocks in cuts:
        steps = jax.random.uniform(jax.random.fold_in(jax.random.fold_in(key, 6), axis_at), (blocks,), jnp.float32, low / len(cuts), high / len(cuts))
        level = level * jnp.repeat(jnp.exp(steps), shape[axis_at] // blocks).reshape((-1,) + (1,) * (len(shape) - 1 - axis_at))
    return level


def noise(stream_key, extent, spread, limit, shards=(), kind=jnp.bfloat16):
    factor_of = levels(stream_key, extent, shards, -0.22, 0.18) if shards else 1.0
    values = jax.random.normal(stream_key, extent, jnp.float32) * spread * factor_of
    return jnp.minimum(jnp.maximum(values, -limit), limit).astype(kind)


def setup_inputs(seed: int = 0, part: int = 0) -> dict:
    key_of = jax.random.split(jax.random.key(seed), 7)
    part_keys = jax.random.split(jax.random.fold_in(key_of[6], part), 7)
    return {
        "e_field": noise(part_keys[0], (3, NX, NY, NZ), 1.0, 6.0, ((1, 8), (2, 2)), jnp.float32),
        "h_field": noise(part_keys[1], (3, NX, NY, NZ), 1.0, 6.0, ((1, 8), (2, 2)), jnp.float32),
        "material": draw_material(jax.random.fold_in(jax.random.fold_in(key_of[6], part), 71), part),
        "eps_table": jnp.clip(jax.random.uniform(key_of[3], (MATS,), jnp.float32, 0.8, 1.2), 0.8, 1.2),
        "sigma_table": jnp.clip(jax.random.uniform(key_of[4], (MATS,), jnp.float32, 0.0, 2.0), 0.0, 2.0),
        "angle_orders": place_ends(jax.random.randint(key_of[5], (ANGLES, 2), -8, 9), jax.random.fold_in(key_of[5], 1), -8, 8).astype(jnp.int32),
    }


TIME_STEP = 0.5
PHASE_STEP = 0.9

def forward(field, axis):
    if axis == 2:
        upper = jnp.concatenate([field[..., 1:], jnp.zeros_like(field[..., :1])], axis=-1)
    else:
        upper = jnp.roll(field, -1, axis)
    return upper - field

def backward(field, axis):
    if axis == 2:
        lower = jnp.concatenate([jnp.zeros_like(field[..., :1]), field[..., :-1]], axis=-1)
    else:
        lower = jnp.roll(field, 1, axis)
    return field - lower

def reference(e_field, h_field, material, eps_table, sigma_table, angle_orders):
    permit = eps_table[material]
    conduct = sigma_table[material]
    loss = conduct * TIME_STEP / (2.0 * permit)
    keep = (1.0 - loss) / (1.0 + loss)
    drive = TIME_STEP / (permit * (1.0 + loss))
    elec_x, elec_y, elec_z = (e_field[0], e_field[1], e_field[2])
    magn_x, magn_y, magn_z = (h_field[0], h_field[1], h_field[2])
    mon_real = jnp.zeros((2, NX, NY), jnp.float32)
    mon_imag = jnp.zeros((2, NX, NY), jnp.float32)
    for number in range(ITERS):
        magn_x = magn_x - TIME_STEP * (forward(elec_z, 1) - forward(elec_y, 2))
        magn_y = magn_y - TIME_STEP * (forward(elec_x, 2) - forward(elec_z, 0))
        magn_z = magn_z - TIME_STEP * (forward(elec_y, 0) - forward(elec_x, 1))
        elec_x = keep * elec_x + drive * (backward(magn_z, 1) - backward(magn_y, 2))
        elec_y = keep * elec_y + drive * (backward(magn_x, 2) - backward(magn_z, 0))
        elec_z = keep * elec_z + drive * (backward(magn_y, 0) - backward(magn_x, 1))
        plane = jnp.stack([elec_x[:, :, NZ - 3], elec_y[:, :, NZ - 3]])
        mon_real = mon_real + math.cos(PHASE_STEP * (number + 1)) * plane
        mon_imag = mon_imag - math.sin(PHASE_STEP * (number + 1)) * plane
    pos_x = jnp.arange(NX, dtype=jnp.int32)
    pos_y = jnp.arange(NY, dtype=jnp.int32)
    order_x = angle_orders[:, 0].astype(jnp.int32)
    order_y = angle_orders[:, 1].astype(jnp.int32)
    phase_int = (order_x[:, None, None] * pos_x[None, :, None] * NY + order_y[:, None, None] * pos_y[None, None, :] * NX) % (NX * NY)
    theta = phase_int.astype(jnp.float32) * (2.0 * math.pi / (NX * NY))
    cosine = jnp.cos(theta).reshape(ANGLES, NX * NY)
    sine = jnp.sin(theta).reshape(ANGLES, NX * NY)
    flat_real = mon_real.reshape(2, NX * NY).T
    flat_imag = mon_imag.reshape(2, NX * NY).T
    high = lax.Precision.HIGHEST
    real_part = jnp.dot(cosine, flat_real, precision=high, preferred_element_type=jnp.float32) + jnp.dot(sine, flat_imag, precision=high, preferred_element_type=jnp.float32)
    imag_part = jnp.dot(cosine, flat_imag, precision=high, preferred_element_type=jnp.float32) - jnp.dot(sine, flat_real, precision=high, preferred_element_type=jnp.float32)
    far_field = jnp.stack([real_part[:, 0], imag_part[:, 0], real_part[:, 1], imag_part[:, 1]], axis=1) * (1.0 / math.sqrt(NX * NY))
    e_out = jnp.stack([elec_x, elec_y, elec_z])
    h_out = jnp.stack([magn_x, magn_y, magn_z])
    return (e_out, h_out, far_field)
```

```python
import math

import jax
import jax.numpy as jnp
from jax import lax
from jax.experimental import pallas as pl
from jax.experimental.pallas import tpu as pltpu
from jax.sharding import PartitionSpec as P

ITERS = 4


TIME_STEP = 0.5
PHASE_STEP = 0.9


def shifted(value, axis, steps):
    count = lax.axis_size(axis)
    pairs = [(source, (source + steps) % count) for source in range(count)]
    return lax.ppermute(value, axis, pairs)


def coefficients(material, eps_table, sigma_table):
    permit = jnp.zeros(material.shape, jnp.float32)
    conduct = jnp.zeros(material.shape, jnp.float32)
    for label in range(eps_table.shape[0]):
        hit = material == label
        permit = jnp.where(hit, eps_table[label], permit)
        conduct = jnp.where(hit, sigma_table[label], conduct)
    loss = conduct * TIME_STEP / (2.0 * permit)
    keep = (1.0 - loss) / (1.0 + loss)
    drive = TIME_STEP / (permit * (1.0 + loss))
    return (keep, drive)


def _z_up(f):
    depth = f.shape[-1]
    lane = lax.broadcasted_iota(jnp.int32, f.shape, 1)
    up = pltpu.roll(f, depth - 1, 1)
    return jnp.where(lane == depth - 1, 0.0, up) - f


def _z_down(f):
    lane = lax.broadcasted_iota(jnp.int32, f.shape, 1)
    down = pltpu.roll(f, 1, 1)
    return f - jnp.where(lane == 0, 0.0, down)


def _y_up(f, row):
    cells = f.shape[0]
    index = lax.broadcasted_iota(jnp.int32, f.shape, 0)
    up = pltpu.roll(f, cells - 1, 0)
    return jnp.where(index == cells - 1, row, up) - f


def _y_down(f, row):
    index = lax.broadcasted_iota(jnp.int32, f.shape, 0)
    down = pltpu.roll(f, 1, 0)
    return f - jnp.where(index == 0, row, down)


def _magn_kernel(e_ref, h_ref, ax_ref, ay_ref, h_out, bx_out, by_out):
    planes = e_ref.shape[1]
    for x in range(planes):
        ex = e_ref[0, x]
        ey = e_ref[1, x]
        ez = e_ref[2, x]
        if x + 1 < planes:
            ey_next = e_ref[1, x + 1]
            ez_next = e_ref[2, x + 1]
        else:
            ey_next = ax_ref[0]
            ez_next = ax_ref[1]
        hx = h_ref[0, x] - TIME_STEP * (_y_up(ez, ay_ref[1, x]) - _z_up(ey))
        hy = h_ref[1, x] - TIME_STEP * (_z_up(ex) - (ez_next - ez))
        hz = h_ref[2, x] - TIME_STEP * ((ey_next - ey) - _y_up(ex, ay_ref[0, x]))
        h_out[0, x] = hx
        h_out[1, x] = hy
        h_out[2, x] = hz
        cells = hx.shape[0]
        by_out[0, x] = hx[cells - 1:cells]
        by_out[1, x] = hz[cells - 1:cells]
        if x == planes - 1:
            bx_out[0] = hy
            bx_out[1] = hz


def _elec_kernel(e_ref, h_ref, keep_ref, drive_ref, bx_ref, by_ref, e_out, ax_out, ay_out):
    planes = e_ref.shape[1]
    for x in range(planes):
        hx = h_ref[0, x]
        hy = h_ref[1, x]
        hz = h_ref[2, x]
        if x > 0:
            hy_prev = h_ref[1, x - 1]
            hz_prev = h_ref[2, x - 1]
        else:
            hy_prev = bx_ref[0]
            hz_prev = bx_ref[1]
        keep = keep_ref[x]
        drive = drive_ref[x]
        ex = keep * e_ref[0, x] + drive * (_y_down(hz, by_ref[1, x]) - _z_down(hy))
        ey = keep * e_ref[1, x] + drive * (_z_down(hx) - (hz - hz_prev))
        ez = keep * e_ref[2, x] + drive * ((hy - hy_prev) - _y_down(hx, by_ref[0, x]))
        e_out[0, x] = ex
        e_out[1, x] = ey
        e_out[2, x] = ez
        ay_out[0, x] = ex[0:1]
        ay_out[1, x] = ez[0:1]
        if x == 0:
            ax_out[0] = ey
            ax_out[1] = ez


def _edges_of_elec(elec):
    return (elec[1:3, 0], jnp.stack([elec[0, :, 0:1], elec[2, :, 0:1]]))


def local(e_field, h_field, material, eps_table, sigma_table, angle_orders):
    keep, drive = coefficients(material, eps_table, sigma_table)
    comps, cells_x, cells_y, depth = e_field.shape
    elec = e_field
    magn = h_field
    plane_shape = jax.ShapeDtypeStruct((2, cells_y, depth), jnp.float32)
    row_shape = jax.ShapeDtypeStruct((2, cells_x, 1, depth), jnp.float32)
    field_shape = jax.ShapeDtypeStruct(e_field.shape, jnp.float32)
    magn_call = pl.pallas_call(_magn_kernel, out_shape=(field_shape, plane_shape, row_shape))
    elec_call = pl.pallas_call(_elec_kernel, out_shape=(field_shape, plane_shape, row_shape))
    edge_x, edge_y = _edges_of_elec(elec)
    mon_real = jnp.zeros((2, cells_x, cells_y), jnp.float32)
    mon_imag = jnp.zeros((2, cells_x, cells_y), jnp.float32)
    for number in range(ITERS):
        ahead_x = shifted(edge_x, "gx", -1)
        ahead_y = shifted(edge_y, "gy", -1)
        magn, back_x, back_y = magn_call(elec, magn, ahead_x, ahead_y)
        behind_x = shifted(back_x, "gx", 1)
        behind_y = shifted(back_y, "gy", 1)
        elec, edge_x, edge_y = elec_call(elec, magn, keep, drive, behind_x, behind_y)
        plane = elec[0:2, :, :, depth - 3]
        mon_real = mon_real + math.cos(PHASE_STEP * (number + 1)) * plane
        mon_imag = mon_imag - math.sin(PHASE_STEP * (number + 1)) * plane
    size_x = lax.axis_size("gx")
    size_y = lax.axis_size("gy")
    total_x = cells_x * size_x
    total_y = cells_y * size_y
    pos_x = lax.axis_index("gx") * cells_x + jnp.arange(cells_x, dtype=jnp.int32)
    pos_y = lax.axis_index("gy") * cells_y + jnp.arange(cells_y, dtype=jnp.int32)
    flat_real = mon_real.reshape(2, cells_x * cells_y).T
    flat_imag = mon_imag.reshape(2, cells_x * cells_y).T
    high = lax.Precision.HIGHEST
    angle_count = angle_orders.shape[0]
    owned = angle_count // size_x
    scale = 1.0 / math.sqrt(total_x * total_y)
    order_x = angle_orders[:, 0]
    order_y = angle_orders[:, 1]
    phase_int = (
        order_x[:, None, None] * pos_x[None, :, None] * total_y
        + order_y[:, None, None] * pos_y[None, None, :] * total_x
    ) % (total_x * total_y)
    theta = phase_int.astype(jnp.float32) * (2.0 * math.pi / (total_x * total_y))
    cosine = jnp.cos(theta).reshape(owned * lax.axis_size("gx"), cells_x * cells_y)
    sine = jnp.sin(theta).reshape(owned * lax.axis_size("gx"), cells_x * cells_y)
    real_part = jnp.dot(
        cosine, flat_real, precision=high, preferred_element_type=jnp.float32
    ) + jnp.dot(sine, flat_imag, precision=high, preferred_element_type=jnp.float32)
    imag_part = jnp.dot(
        cosine, flat_imag, precision=high, preferred_element_type=jnp.float32
    ) - jnp.dot(sine, flat_real, precision=high, preferred_element_type=jnp.float32)
    rows_sum = lax.psum_scatter(
        jnp.stack([real_part[:, 0], imag_part[:, 0], real_part[:, 1], imag_part[:, 1]], axis=1),
        "gx",
        scatter_dimension=0,
        tiled=True,
    )
    far_field = lax.psum(rows_sum, "gy") * scale
    return (elec, magn, far_field)


def solution(mesh):
    return jax.shard_map(
        local,
        mesh=mesh,
        in_specs=(
            P(None, ("clip", "gx"), "gy", None),
            P(None, ("clip", "gx"), "gy", None),
            P(("clip", "gx"), "gy", None),
            P(),
            P(),
            P(),
        ),
        out_specs=(
            P(None, ("clip", "gx"), "gy", None),
            P(None, ("clip", "gx"), "gy", None),
            P(("clip", "gx"), None),
        ),
        check_vma=False,
    )
```

```python
import math

import jax
import jax.numpy as jnp
from jax import lax
from jax.experimental import pallas as pl
from jax.experimental.pallas import tpu as pltpu
from jax.sharding import PartitionSpec as P

ITERS = 4


TIME_STEP = 0.5
PHASE_STEP = 0.9


def shifted(value, axis, steps):
    count = lax.axis_size(axis)
    pairs = [(source, (source + steps) % count) for source in range(count)]
    return lax.ppermute(value, axis, pairs)


def _coef_kernel(eps_ref, sigma_ref, mat_ref, keep_out, drive_out):
    planes = mat_ref.shape[0]
    for x in range(planes):
        material = mat_ref[x]
        permit = jnp.zeros(material.shape, jnp.float32)
        conduct = jnp.zeros(material.shape, jnp.float32)
        for label in range(eps_ref.shape[0]):
            hit = material == label
            permit = jnp.where(hit, eps_ref[label], permit)
            conduct = jnp.where(hit, sigma_ref[label], conduct)
        loss = conduct * TIME_STEP / (2.0 * permit)
        keep_out[x] = (1.0 - loss) / (1.0 + loss)
        drive_out[x] = TIME_STEP / (permit * (1.0 + loss))


def coefficients(material, eps_table, sigma_table):
    scalar = pl.BlockSpec(memory_space=pltpu.SMEM)
    whole = pl.BlockSpec(memory_space=pltpu.VMEM)
    out = jax.ShapeDtypeStruct(material.shape, jnp.float32)
    return pl.pallas_call(
        _coef_kernel,
        out_shape=(out, out),
        in_specs=[scalar, scalar, whole],
        out_specs=(whole, whole),
    )(eps_table, sigma_table, material)


def _z_up(f):
    depth = f.shape[-1]
    lane = lax.broadcasted_iota(jnp.int32, f.shape, 1)
    up = pltpu.roll(f, depth - 1, 1)
    return jnp.where(lane == depth - 1, 0.0, up) - f


def _z_down(f):
    lane = lax.broadcasted_iota(jnp.int32, f.shape, 1)
    down = pltpu.roll(f, 1, 1)
    return f - jnp.where(lane == 0, 0.0, down)


def _y_up(f, row):
    cells = f.shape[0]
    index = lax.broadcasted_iota(jnp.int32, f.shape, 0)
    up = pltpu.roll(f, cells - 1, 0)
    return jnp.where(index == cells - 1, row, up) - f


def _y_down(f, row):
    index = lax.broadcasted_iota(jnp.int32, f.shape, 0)
    down = pltpu.roll(f, 1, 0)
    return f - jnp.where(index == 0, row, down)


def _magn_kernel(e_ref, h_ref, ax_ref, ay_ref, h_out, bx_out, by_out):
    planes = e_ref.shape[1]
    for x in range(planes):
        ex = e_ref[0, x]
        ey = e_ref[1, x]
        ez = e_ref[2, x]
        if x + 1 < planes:
            ey_next = e_ref[1, x + 1]
            ez_next = e_ref[2, x + 1]
        else:
            ey_next = ax_ref[0]
            ez_next = ax_ref[1]
        hx = h_ref[0, x] - TIME_STEP * (_y_up(ez, ay_ref[1, x]) - _z_up(ey))
        hy = h_ref[1, x] - TIME_STEP * (_z_up(ex) - (ez_next - ez))
        hz = h_ref[2, x] - TIME_STEP * ((ey_next - ey) - _y_up(ex, ay_ref[0, x]))
        h_out[0, x] = hx
        h_out[1, x] = hy
        h_out[2, x] = hz
        cells = hx.shape[0]
        by_out[0, x] = hx[cells - 1:cells]
        by_out[1, x] = hz[cells - 1:cells]
        if x == planes - 1:
            bx_out[0] = hy
            bx_out[1] = hz


def _elec_kernel(e_ref, h_ref, keep_ref, drive_ref, bx_ref, by_ref, e_out, ax_out, ay_out):
    planes = e_ref.shape[1]
    for x in range(planes):
        hx = h_ref[0, x]
        hy = h_ref[1, x]
        hz = h_ref[2, x]
        if x > 0:
            hy_prev = h_ref[1, x - 1]
            hz_prev = h_ref[2, x - 1]
        else:
            hy_prev = bx_ref[0]
            hz_prev = bx_ref[1]
        keep = keep_ref[x]
        drive = drive_ref[x]
        ex = keep * e_ref[0, x] + drive * (_y_down(hz, by_ref[1, x]) - _z_down(hy))
        ey = keep * e_ref[1, x] + drive * (_z_down(hx) - (hz - hz_prev))
        ez = keep * e_ref[2, x] + drive * ((hy - hy_prev) - _y_down(hx, by_ref[0, x]))
        e_out[0, x] = ex
        e_out[1, x] = ey
        e_out[2, x] = ez
        ay_out[0, x] = ex[0:1]
        ay_out[1, x] = ez[0:1]
        if x == 0:
            ax_out[0] = ey
            ax_out[1] = ez


def _edges_of_elec(elec):
    return (elec[1:3, 0], jnp.stack([elec[0, :, 0:1], elec[2, :, 0:1]]))


def local(e_field, h_field, material, eps_table, sigma_table, angle_orders):
    keep, drive = coefficients(material, eps_table, sigma_table)
    comps, cells_x, cells_y, depth = e_field.shape
    elec = e_field
    magn = h_field
    plane_shape = jax.ShapeDtypeStruct((2, cells_y, depth), jnp.float32)
    row_shape = jax.ShapeDtypeStruct((2, cells_x, 1, depth), jnp.float32)
    field_shape = jax.ShapeDtypeStruct(e_field.shape, jnp.float32)
    magn_call = pl.pallas_call(_magn_kernel, out_shape=(field_shape, plane_shape, row_shape))
    elec_call = pl.pallas_call(_elec_kernel, out_shape=(field_shape, plane_shape, row_shape))
    edge_x, edge_y = _edges_of_elec(elec)
    mon_real = jnp.zeros((2, cells_x, cells_y), jnp.float32)
    mon_imag = jnp.zeros((2, cells_x, cells_y), jnp.float32)
    for number in range(ITERS):
        ahead_x = shifted(edge_x, "gx", -1)
        ahead_y = shifted(edge_y, "gy", -1)
        magn, back_x, back_y = magn_call(elec, magn, ahead_x, ahead_y)
        behind_x = shifted(back_x, "gx", 1)
        behind_y = shifted(back_y, "gy", 1)
        elec, edge_x, edge_y = elec_call(elec, magn, keep, drive, behind_x, behind_y)
        plane = elec[0:2, :, :, depth - 3]
        mon_real = mon_real + math.cos(PHASE_STEP * (number + 1)) * plane
        mon_imag = mon_imag - math.sin(PHASE_STEP * (number + 1)) * plane
    size_x = lax.axis_size("gx")
    size_y = lax.axis_size("gy")
    total_x = cells_x * size_x
    total_y = cells_y * size_y
    pos_x = lax.axis_index("gx") * cells_x + jnp.arange(cells_x, dtype=jnp.int32)
    pos_y = lax.axis_index("gy") * cells_y + jnp.arange(cells_y, dtype=jnp.int32)
    flat_real = mon_real.reshape(2, cells_x * cells_y).T
    flat_imag = mon_imag.reshape(2, cells_x * cells_y).T
    high = lax.Precision.HIGHEST
    angle_count = angle_orders.shape[0]
    owned = angle_count // size_x
    scale = 1.0 / math.sqrt(total_x * total_y)
    order_x = angle_orders[:, 0]
    order_y = angle_orders[:, 1]
    phase_int = (
        order_x[:, None, None] * pos_x[None, :, None] * total_y
        + order_y[:, None, None] * pos_y[None, None, :] * total_x
    ) % (total_x * total_y)
    theta = phase_int.astype(jnp.float32) * (2.0 * math.pi / (total_x * total_y))
    cosine = jnp.cos(theta).reshape(owned * lax.axis_size("gx"), cells_x * cells_y)
    sine = jnp.sin(theta).reshape(owned * lax.axis_size("gx"), cells_x * cells_y)
    real_part = jnp.dot(
        cosine, flat_real, precision=high, preferred_element_type=jnp.float32
    ) + jnp.dot(sine, flat_imag, precision=high, preferred_element_type=jnp.float32)
    imag_part = jnp.dot(
        cosine, flat_imag, precision=high, preferred_element_type=jnp.float32
    ) - jnp.dot(sine, flat_real, precision=high, preferred_element_type=jnp.float32)
    terms = jnp.stack([real_part[:, 0], imag_part[:, 0], real_part[:, 1], imag_part[:, 1]], axis=1)
    total = lax.psum(terms, ("gx", "gy"))
    far_field = lax.dynamic_slice_in_dim(total, lax.axis_index("gx") * owned, owned, 0) * scale
    return (elec, magn, far_field)


def solution(mesh):
    return jax.shard_map(
        local,
        mesh=mesh,
        in_specs=(
            P(None, ("clip", "gx"), "gy", None),
            P(None, ("clip", "gx"), "gy", None),
            P(("clip", "gx"), "gy", None),
            P(),
            P(),
            P(),
        ),
        out_specs=(
            P(None, ("clip", "gx"), "gy", None),
            P(None, ("clip", "gx"), "gy", None),
            P(("clip", "gx"), None),
        ),
        check_vma=False,
    )
```

```python
import math

import jax
import jax.numpy as jnp
from jax import lax
from jax.experimental import pallas as pl
from jax.experimental.pallas import tpu as pltpu
from jax.sharding import PartitionSpec as P

ITERS = 4


TIME_STEP = 0.5
PHASE_STEP = 0.9


def shifted(value, axis, steps):
    count = lax.axis_size(axis)
    pairs = [(source, (source + steps) % count) for source in range(count)]
    return lax.ppermute(value, axis, pairs)


def _coef_kernel(eps_ref, sigma_ref, mat_ref, keep_out, drive_out):
    planes = mat_ref.shape[0]
    for x in range(planes):
        material = mat_ref[x]
        permit = jnp.zeros(material.shape, jnp.float32)
        conduct = jnp.zeros(material.shape, jnp.float32)
        for label in range(eps_ref.shape[0]):
            hit = material == label
            permit = jnp.where(hit, eps_ref[label], permit)
            conduct = jnp.where(hit, sigma_ref[label], conduct)
        loss = conduct * TIME_STEP / (2.0 * permit)
        keep_out[x] = (1.0 - loss) / (1.0 + loss)
        drive_out[x] = TIME_STEP / (permit * (1.0 + loss))


def coefficients(material, eps_table, sigma_table):
    scalar = pl.BlockSpec(memory_space=pltpu.SMEM)
    whole = pl.BlockSpec(memory_space=pltpu.VMEM)
    out = jax.ShapeDtypeStruct(material.shape, jnp.float32)
    return pl.pallas_call(
        _coef_kernel,
        out_shape=(out, out),
        in_specs=[scalar, scalar, whole],
        out_specs=(whole, whole),
    )(eps_table, sigma_table, material)


def _z_up(f):
    depth = f.shape[-1]
    lane = lax.broadcasted_iota(jnp.int32, f.shape, 1)
    up = pltpu.roll(f, depth - 1, 1)
    return jnp.where(lane == depth - 1, 0.0, up) - f


def _z_down(f):
    lane = lax.broadcasted_iota(jnp.int32, f.shape, 1)
    down = pltpu.roll(f, 1, 1)
    return f - jnp.where(lane == 0, 0.0, down)


def _y_up(f, row):
    cells = f.shape[0]
    index = lax.broadcasted_iota(jnp.int32, f.shape, 0)
    up = pltpu.roll(f, cells - 1, 0)
    return jnp.where(index == cells - 1, row, up) - f


def _y_down(f, row):
    index = lax.broadcasted_iota(jnp.int32, f.shape, 0)
    down = pltpu.roll(f, 1, 0)
    return f - jnp.where(index == 0, row, down)


def _magn_kernel(e_ref, h_ref, ax_ref, ay_ref, h_out, bx_out, by_out):
    planes = e_ref.shape[1]
    for x in range(planes):
        ex = e_ref[0, x]
        ey = e_ref[1, x]
        ez = e_ref[2, x]
        if x + 1 < planes:
            ey_next = e_ref[1, x + 1]
            ez_next = e_ref[2, x + 1]
        else:
            ey_next = ax_ref[0]
            ez_next = ax_ref[1]
        hx = h_ref[0, x] - TIME_STEP * (_y_up(ez, ay_ref[1, x]) - _z_up(ey))
        hy = h_ref[1, x] - TIME_STEP * (_z_up(ex) - (ez_next - ez))
        hz = h_ref[2, x] - TIME_STEP * ((ey_next - ey) - _y_up(ex, ay_ref[0, x]))
        h_out[0, x] = hx
        h_out[1, x] = hy
        h_out[2, x] = hz
        cells = hx.shape[0]
        by_out[0, x] = hx[cells - 1:cells]
        by_out[1, x] = hz[cells - 1:cells]
        if x == planes - 1:
            bx_out[0] = hy
            bx_out[1] = hz


def _elec_kernel(e_ref, h_ref, keep_ref, drive_ref, bx_ref, by_ref, e_out, ax_out, ay_out):
    planes = e_ref.shape[1]
    for x in range(planes):
        hx = h_ref[0, x]
        hy = h_ref[1, x]
        hz = h_ref[2, x]
        if x > 0:
            hy_prev = h_ref[1, x - 1]
            hz_prev = h_ref[2, x - 1]
        else:
            hy_prev = bx_ref[0]
            hz_prev = bx_ref[1]
        keep = keep_ref[x]
        drive = drive_ref[x]
        ex = keep * e_ref[0, x] + drive * (_y_down(hz, by_ref[1, x]) - _z_down(hy))
        ey = keep * e_ref[1, x] + drive * (_z_down(hx) - (hz - hz_prev))
        ez = keep * e_ref[2, x] + drive * ((hy - hy_prev) - _y_down(hx, by_ref[0, x]))
        e_out[0, x] = ex
        e_out[1, x] = ey
        e_out[2, x] = ez
        ay_out[0, x] = ex[0:1]
        ay_out[1, x] = ez[0:1]
        if x == 0:
            ax_out[0] = ey
            ax_out[1] = ez


def _edges_of_elec(elec):
    return (elec[1:3, 0], jnp.stack([elec[0, :, 0:1], elec[2, :, 0:1]]))


def scatter_sum(rows, axis, owned):
    count = lax.axis_size(axis)
    index = lax.axis_index(axis)
    if count & (count - 1):
        return lax.psum_scatter(rows, axis, scatter_dimension=0, tiled=True)
    stride = count // 2
    while stride >= 1:
        half = rows.shape[0] // 2
        lower = rows[:half]
        upper = rows[half:]
        high = (index & stride) != 0
        keep = jnp.where(high, upper, lower)
        send = jnp.where(high, lower, upper)
        pairs = [(source, source ^ stride) for source in range(count)]
        rows = keep + lax.ppermute(send, axis, pairs)
        stride //= 2
    return rows


def pair_sum(value, axis):
    count = lax.axis_size(axis)
    if count == 1:
        return value
    if count == 2:
        return value + lax.ppermute(value, axis, [(0, 1), (1, 0)])
    return lax.psum(value, axis)


def local(e_field, h_field, material, eps_table, sigma_table, angle_orders):
    keep, drive = coefficients(material, eps_table, sigma_table)
    comps, cells_x, cells_y, depth = e_field.shape
    elec = e_field
    magn = h_field
    plane_shape = jax.ShapeDtypeStruct((2, cells_y, depth), jnp.float32)
    row_shape = jax.ShapeDtypeStruct((2, cells_x, 1, depth), jnp.float32)
    field_shape = jax.ShapeDtypeStruct(e_field.shape, jnp.float32)
    magn_call = pl.pallas_call(_magn_kernel, out_shape=(field_shape, plane_shape, row_shape))
    elec_call = pl.pallas_call(_elec_kernel, out_shape=(field_shape, plane_shape, row_shape))
    edge_x, edge_y = _edges_of_elec(elec)
    mon_real = jnp.zeros((2, cells_x, cells_y), jnp.float32)
    mon_imag = jnp.zeros((2, cells_x, cells_y), jnp.float32)
    for number in range(ITERS):
        ahead_x = shifted(edge_x, "gx", -1)
        ahead_y = shifted(edge_y, "gy", -1)
        magn, back_x, back_y = magn_call(elec, magn, ahead_x, ahead_y)
        behind_x = shifted(back_x, "gx", 1)
        behind_y = shifted(back_y, "gy", 1)
        elec, edge_x, edge_y = elec_call(elec, magn, keep, drive, behind_x, behind_y)
        plane = elec[0:2, :, :, depth - 3]
        mon_real = mon_real + math.cos(PHASE_STEP * (number + 1)) * plane
        mon_imag = mon_imag - math.sin(PHASE_STEP * (number + 1)) * plane
    size_x = lax.axis_size("gx")
    size_y = lax.axis_size("gy")
    total_x = cells_x * size_x
    total_y = cells_y * size_y
    pos_x = lax.axis_index("gx") * cells_x + jnp.arange(cells_x, dtype=jnp.int32)
    pos_y = lax.axis_index("gy") * cells_y + jnp.arange(cells_y, dtype=jnp.int32)
    flat_real = mon_real.reshape(2, cells_x * cells_y).T
    flat_imag = mon_imag.reshape(2, cells_x * cells_y).T
    high = lax.Precision.HIGHEST
    angle_count = angle_orders.shape[0]
    owned = angle_count // size_x
    scale = 1.0 / math.sqrt(total_x * total_y)
    order_x = angle_orders[:, 0]
    order_y = angle_orders[:, 1]
    phase_int = (
        order_x[:, None, None] * pos_x[None, :, None] * total_y
        + order_y[:, None, None] * pos_y[None, None, :] * total_x
    ) % (total_x * total_y)
    theta = phase_int.astype(jnp.float32) * (2.0 * math.pi / (total_x * total_y))
    cosine = jnp.cos(theta).reshape(owned * lax.axis_size("gx"), cells_x * cells_y)
    sine = jnp.sin(theta).reshape(owned * lax.axis_size("gx"), cells_x * cells_y)
    real_part = jnp.dot(
        cosine, flat_real, precision=high, preferred_element_type=jnp.float32
    ) + jnp.dot(sine, flat_imag, precision=high, preferred_element_type=jnp.float32)
    imag_part = jnp.dot(
        cosine, flat_imag, precision=high, preferred_element_type=jnp.float32
    ) - jnp.dot(sine, flat_real, precision=high, preferred_element_type=jnp.float32)
    terms = jnp.stack([real_part[:, 0], imag_part[:, 0], real_part[:, 1], imag_part[:, 1]], axis=1)
    far_field = scatter_sum(terms, "gx", owned)
    far_field = pair_sum(far_field, "gy") * scale
    return (elec, magn, far_field)


def solution(mesh):
    return jax.shard_map(
        local,
        mesh=mesh,
        in_specs=(
            P(None, ("clip", "gx"), "gy", None),
            P(None, ("clip", "gx"), "gy", None),
            P(("clip", "gx"), "gy", None),
            P(),
            P(),
            P(),
        ),
        out_specs=(
            P(None, ("clip", "gx"), "gy", None),
            P(None, ("clip", "gx"), "gy", None),
            P(("clip", "gx"), None),
        ),
        check_vma=False,
    )
```

```python
import math

import jax
import jax.numpy as jnp
from jax import lax
from jax.experimental import pallas as pl
from jax.experimental.pallas import tpu as pltpu
from jax.sharding import PartitionSpec as P

ITERS = 4


TIME_STEP = 0.5
PHASE_STEP = 0.9


def shifted(value, axis, steps):
    count = lax.axis_size(axis)
    pairs = [(source, (source + steps) % count) for source in range(count)]
    return lax.ppermute(value, axis, pairs)


def _coef_kernel(eps_ref, sigma_ref, mat_ref, keep_out, drive_out):
    planes = mat_ref.shape[0]
    for x in range(planes):
        material = mat_ref[x]
        permit = jnp.zeros(material.shape, jnp.float32)
        conduct = jnp.zeros(material.shape, jnp.float32)
        for label in range(eps_ref.shape[0]):
            hit = material == label
            permit = jnp.where(hit, eps_ref[label], permit)
            conduct = jnp.where(hit, sigma_ref[label], conduct)
        loss = conduct * TIME_STEP / (2.0 * permit)
        keep_out[x] = (1.0 - loss) / (1.0 + loss)
        drive_out[x] = TIME_STEP / (permit * (1.0 + loss))


def coefficients(material, eps_table, sigma_table):
    scalar = pl.BlockSpec(memory_space=pltpu.SMEM)
    whole = pl.BlockSpec(memory_space=pltpu.VMEM)
    out = jax.ShapeDtypeStruct(material.shape, jnp.float32)
    return pl.pallas_call(
        _coef_kernel,
        out_shape=(out, out),
        in_specs=[scalar, scalar, whole],
        out_specs=(whole, whole),
    )(eps_table, sigma_table, material)


def _z_up(f):
    depth = f.shape[-1]
    lane = lax.broadcasted_iota(jnp.int32, f.shape, 1)
    up = pltpu.roll(f, depth - 1, 1)
    return jnp.where(lane == depth - 1, 0.0, up) - f


def _z_down(f):
    lane = lax.broadcasted_iota(jnp.int32, f.shape, 1)
    down = pltpu.roll(f, 1, 1)
    return f - jnp.where(lane == 0, 0.0, down)


def _y_up(f, row):
    cells = f.shape[0]
    index = lax.broadcasted_iota(jnp.int32, f.shape, 0)
    up = pltpu.roll(f, cells - 1, 0)
    return jnp.where(index == cells - 1, row, up) - f


def _y_down(f, row):
    index = lax.broadcasted_iota(jnp.int32, f.shape, 0)
    down = pltpu.roll(f, 1, 0)
    return f - jnp.where(index == 0, row, down)


def _step_kernel(e_ref, h_ref, keep_ref, drive_ref, xlo_ref, xhi_ref, ylo_ref, yhi_ref,
                 c1_ref, c2_ref, e_out, h_out, xlo_out, xhi_out, ylo_out, yhi_out, c1_out, c2_out):
    planes = e_ref.shape[1]
    cells = e_ref.shape[2]
    ex_p = xlo_ref[0]
    ey_p = xlo_ref[1]
    ez_p = xlo_ref[2]
    hy_prev = xlo_ref[3] - TIME_STEP * (_z_up(ex_p) - (e_ref[2, 0] - ez_p))
    hz_prev = xlo_ref[4] - TIME_STEP * ((e_ref[1, 0] - ey_p) - _y_up(ex_p, c1_ref[...]))
    for x in range(planes):
        ex = e_ref[0, x]
        ey = e_ref[1, x]
        ez = e_ref[2, x]
        if x + 1 < planes:
            ey_next = e_ref[1, x + 1]
            ez_next = e_ref[2, x + 1]
            ey_m_next = ylo_ref[1, x + 1]
        else:
            ey_next = xhi_ref[0]
            ez_next = xhi_ref[1]
            ey_m_next = c2_ref[...]
        hx = h_ref[0, x] - TIME_STEP * (_y_up(ez, yhi_ref[1, x]) - _z_up(ey))
        hy = h_ref[1, x] - TIME_STEP * (_z_up(ex) - (ez_next - ez))
        hz = h_ref[2, x] - TIME_STEP * ((ey_next - ey) - _y_up(ex, yhi_ref[0, x]))
        ex_m = ylo_ref[0, x]
        ey_m = ylo_ref[1, x]
        ez_m = ylo_ref[2, x]
        hx_r = ylo_ref[3, x] - TIME_STEP * ((ez[0:1] - ez_m) - _z_up(ey_m))
        hz_r = ylo_ref[4, x] - TIME_STEP * ((ey_m_next - ey_m) - (ex[0:1] - ex_m))
        keep = keep_ref[x]
        drive = drive_ref[x]
        ex_new = keep * ex + drive * (_y_down(hz, hz_r) - _z_down(hy))
        ey_new = keep * ey + drive * (_z_down(hx) - (hz - hz_prev))
        ez_new = keep * ez + drive * ((hy - hy_prev) - _y_down(hx, hx_r))
        e_out[0, x] = ex_new
        e_out[1, x] = ey_new
        e_out[2, x] = ez_new
        h_out[0, x] = hx
        h_out[1, x] = hy
        h_out[2, x] = hz
        last = slice(cells - 1, cells)
        ylo_out[0, x] = ex_new[last]
        ylo_out[1, x] = ey_new[last]
        ylo_out[2, x] = ez_new[last]
        ylo_out[3, x] = hx[last]
        ylo_out[4, x] = hz[last]
        yhi_out[0, x] = ex_new[0:1]
        yhi_out[1, x] = ez_new[0:1]
        if x == 0:
            xhi_out[0] = ey_new
            xhi_out[1] = ez_new
            c2_out[...] = ey_new[last]
        if x == planes - 1:
            xlo_out[0] = ex_new
            xlo_out[1] = ey_new
            xlo_out[2] = ez_new
            xlo_out[3] = hy
            xlo_out[4] = hz
            c1_out[...] = ex_new[0:1]
        hy_prev = hy
        hz_prev = hz


def _halo_of(elec, magn):
    cells = elec.shape[2]
    last = slice(cells - 1, cells)
    xlo = jnp.stack([elec[0, -1], elec[1, -1], elec[2, -1], magn[1, -1], magn[2, -1]])
    xhi = elec[1:3, 0]
    ylo = jnp.stack([elec[0, :, last], elec[1, :, last], elec[2, :, last], magn[0, :, last], magn[2, :, last]])
    yhi = jnp.stack([elec[0, :, 0:1], elec[2, :, 0:1]])
    return (xlo, xhi, ylo, yhi, elec[0, -1, 0:1], elec[1, 0, last])


def diagonal(value, step_x, step_y):
    count_x = lax.axis_size("gx")
    count_y = lax.axis_size("gy")
    pairs = []
    for a in range(count_x):
        for b in range(count_y):
            target = ((a + step_x) % count_x) * count_y + (b + step_y) % count_y
            pairs.append((a * count_y + b, target))
    return lax.ppermute(value, ("gx", "gy"), pairs)


def exchange(halo):
    xlo, xhi, ylo, yhi, c1, c2 = halo
    return (
        shifted(xlo, "gx", 1),
        shifted(xhi, "gx", -1),
        shifted(ylo, "gy", 1),
        shifted(yhi, "gy", -1),
        diagonal(c1, 1, -1),
        diagonal(c2, -1, 1),
    )


def scatter_sum(rows, axis, owned):
    count = lax.axis_size(axis)
    index = lax.axis_index(axis)
    if count & (count - 1):
        return lax.psum_scatter(rows, axis, scatter_dimension=0, tiled=True)
    stride = count // 2
    while stride >= 1:
        half = rows.shape[0] // 2
        lower = rows[:half]
        upper = rows[half:]
        high = (index & stride) != 0
        keep = jnp.where(high, upper, lower)
        send = jnp.where(high, lower, upper)
        pairs = [(source, source ^ stride) for source in range(count)]
        rows = keep + lax.ppermute(send, axis, pairs)
        stride //= 2
    return rows


def pair_sum(value, axis):
    count = lax.axis_size(axis)
    if count == 1:
        return value
    if count == 2:
        return value + lax.ppermute(value, axis, [(0, 1), (1, 0)])
    return lax.psum(value, axis)


def local(e_field, h_field, material, eps_table, sigma_table, angle_orders):
    keep, drive = coefficients(material, eps_table, sigma_table)
    comps, cells_x, cells_y, depth = e_field.shape
    elec = e_field
    magn = h_field
    f32 = jnp.float32
    field_shape = jax.ShapeDtypeStruct(e_field.shape, f32)
    halo_shapes = (
        jax.ShapeDtypeStruct((5, cells_y, depth), f32),
        jax.ShapeDtypeStruct((2, cells_y, depth), f32),
        jax.ShapeDtypeStruct((5, cells_x, 1, depth), f32),
        jax.ShapeDtypeStruct((2, cells_x, 1, depth), f32),
        jax.ShapeDtypeStruct((1, depth), f32),
        jax.ShapeDtypeStruct((1, depth), f32),
    )
    step_call = pl.pallas_call(_step_kernel, out_shape=(field_shape, field_shape) + halo_shapes)
    halo = _halo_of(elec, magn)
    mon_real = jnp.zeros((2, cells_x, cells_y), f32)
    mon_imag = jnp.zeros((2, cells_x, cells_y), f32)
    for number in range(ITERS):
        received = exchange(halo)
        elec, magn, *halo = step_call(elec, magn, keep, drive, *received)
        plane = elec[0:2, :, :, depth - 3]
        mon_real = mon_real + math.cos(PHASE_STEP * (number + 1)) * plane
        mon_imag = mon_imag - math.sin(PHASE_STEP * (number + 1)) * plane
    size_x = lax.axis_size("gx")
    size_y = lax.axis_size("gy")
    total_x = cells_x * size_x
    total_y = cells_y * size_y
    pos_x = lax.axis_index("gx") * cells_x + jnp.arange(cells_x, dtype=jnp.int32)
    pos_y = lax.axis_index("gy") * cells_y + jnp.arange(cells_y, dtype=jnp.int32)
    flat_real = mon_real.reshape(2, cells_x * cells_y).T
    flat_imag = mon_imag.reshape(2, cells_x * cells_y).T
    high = lax.Precision.HIGHEST
    angle_count = angle_orders.shape[0]
    owned = angle_count // size_x
    scale = 1.0 / math.sqrt(total_x * total_y)
    order_x = angle_orders[:, 0]
    order_y = angle_orders[:, 1]
    phase_int = (
        order_x[:, None, None] * pos_x[None, :, None] * total_y
        + order_y[:, None, None] * pos_y[None, None, :] * total_x
    ) % (total_x * total_y)
    theta = phase_int.astype(jnp.float32) * (2.0 * math.pi / (total_x * total_y))
    cosine = jnp.cos(theta).reshape(owned * lax.axis_size("gx"), cells_x * cells_y)
    sine = jnp.sin(theta).reshape(owned * lax.axis_size("gx"), cells_x * cells_y)
    real_part = jnp.dot(
        cosine, flat_real, precision=high, preferred_element_type=jnp.float32
    ) + jnp.dot(sine, flat_imag, precision=high, preferred_element_type=jnp.float32)
    imag_part = jnp.dot(
        cosine, flat_imag, precision=high, preferred_element_type=jnp.float32
    ) - jnp.dot(sine, flat_real, precision=high, preferred_element_type=jnp.float32)
    terms = jnp.stack([real_part[:, 0], imag_part[:, 0], real_part[:, 1], imag_part[:, 1]], axis=1)
    far_field = scatter_sum(terms, "gx", owned)
    far_field = pair_sum(far_field, "gy") * scale
    return (elec, magn, far_field)


def solution(mesh):
    return jax.shard_map(
        local,
        mesh=mesh,
        in_specs=(
            P(None, ("clip", "gx"), "gy", None),
            P(None, ("clip", "gx"), "gy", None),
            P(("clip", "gx"), "gy", None),
            P(),
            P(),
            P(),
        ),
        out_specs=(
            P(None, ("clip", "gx"), "gy", None),
            P(None, ("clip", "gx"), "gy", None),
            P(("clip", "gx"), None),
        ),
        check_vma=False,
    )
```

```python
import math

import jax
import jax.numpy as jnp
from jax import lax
from jax.experimental import pallas as pl
from jax.experimental.pallas import tpu as pltpu
from jax.sharding import PartitionSpec as P

ITERS = 4


TIME_STEP = 0.5
PHASE_STEP = 0.9


def shifted(value, axis, steps):
    count = lax.axis_size(axis)
    pairs = [(source, (source + steps) % count) for source in range(count)]
    return lax.ppermute(value, axis, pairs)


def _coef_kernel(eps_ref, sigma_ref, mat_ref, keep_out, drive_out):
    planes = mat_ref.shape[0]
    for x in range(planes):
        material = mat_ref[x]
        permit = jnp.zeros(material.shape, jnp.float32)
        conduct = jnp.zeros(material.shape, jnp.float32)
        for label in range(eps_ref.shape[0]):
            hit = material == label
            permit = jnp.where(hit, eps_ref[label], permit)
            conduct = jnp.where(hit, sigma_ref[label], conduct)
        loss = conduct * TIME_STEP / (2.0 * permit)
        keep_out[x] = (1.0 - loss) / (1.0 + loss)
        drive_out[x] = TIME_STEP / (permit * (1.0 + loss))


def coefficients(material, eps_table, sigma_table):
    scalar = pl.BlockSpec(memory_space=pltpu.SMEM)
    whole = pl.BlockSpec(memory_space=pltpu.VMEM)
    out = jax.ShapeDtypeStruct(material.shape, jnp.float32)
    return pl.pallas_call(
        _coef_kernel,
        out_shape=(out, out),
        in_specs=[scalar, scalar, whole],
        out_specs=(whole, whole),
    )(eps_table, sigma_table, material)


def _z_up(f):
    depth = f.shape[-1]
    lane = lax.broadcasted_iota(jnp.int32, f.shape, 1)
    up = pltpu.roll(f, depth - 1, 1)
    return jnp.where(lane == depth - 1, 0.0, up) - f


def _z_down(f):
    lane = lax.broadcasted_iota(jnp.int32, f.shape, 1)
    down = pltpu.roll(f, 1, 1)
    return f - jnp.where(lane == 0, 0.0, down)


def _y_up(f, row):
    cells = f.shape[0]
    index = lax.broadcasted_iota(jnp.int32, f.shape, 0)
    up = pltpu.roll(f, cells - 1, 0)
    return jnp.where(index == cells - 1, row, up) - f


def _y_down(f, row):
    index = lax.broadcasted_iota(jnp.int32, f.shape, 0)
    down = pltpu.roll(f, 1, 0)
    return f - jnp.where(index == 0, row, down)


def _step_kernel(e_ref, h_ref, keep_ref, drive_ref, xlo_ref, xhi_ref, y_ref, c1_ref, c2_ref,
                 e_out, h_out, xlo_out, xhi_out, y_out, c1_out, c2_out):
    ylo_ref = y_ref
    yhi_ref = y_ref.at[5:7]
    ylo_out = y_out
    yhi_out = y_out.at[5:7]
    planes = e_ref.shape[1]
    cells = e_ref.shape[2]
    ex_p = xlo_ref[0]
    ey_p = xlo_ref[1]
    ez_p = xlo_ref[2]
    hy_prev = xlo_ref[3] - TIME_STEP * (_z_up(ex_p) - (e_ref[2, 0] - ez_p))
    hz_prev = xlo_ref[4] - TIME_STEP * ((e_ref[1, 0] - ey_p) - _y_up(ex_p, c1_ref[...]))
    for x in range(planes):
        ex = e_ref[0, x]
        ey = e_ref[1, x]
        ez = e_ref[2, x]
        if x + 1 < planes:
            ey_next = e_ref[1, x + 1]
            ez_next = e_ref[2, x + 1]
            ey_m_next = ylo_ref[1, x + 1]
        else:
            ey_next = xhi_ref[0]
            ez_next = xhi_ref[1]
            ey_m_next = c2_ref[...]
        hx = h_ref[0, x] - TIME_STEP * (_y_up(ez, yhi_ref[1, x]) - _z_up(ey))
        hy = h_ref[1, x] - TIME_STEP * (_z_up(ex) - (ez_next - ez))
        hz = h_ref[2, x] - TIME_STEP * ((ey_next - ey) - _y_up(ex, yhi_ref[0, x]))
        ex_m = ylo_ref[0, x]
        ey_m = ylo_ref[1, x]
        ez_m = ylo_ref[2, x]
        hx_r = ylo_ref[3, x] - TIME_STEP * ((ez[0:1] - ez_m) - _z_up(ey_m))
        hz_r = ylo_ref[4, x] - TIME_STEP * ((ey_m_next - ey_m) - (ex[0:1] - ex_m))
        keep = keep_ref[x]
        drive = drive_ref[x]
        ex_new = keep * ex + drive * (_y_down(hz, hz_r) - _z_down(hy))
        ey_new = keep * ey + drive * (_z_down(hx) - (hz - hz_prev))
        ez_new = keep * ez + drive * ((hy - hy_prev) - _y_down(hx, hx_r))
        e_out[0, x] = ex_new
        e_out[1, x] = ey_new
        e_out[2, x] = ez_new
        h_out[0, x] = hx
        h_out[1, x] = hy
        h_out[2, x] = hz
        last = slice(cells - 1, cells)
        ylo_out[0, x] = ex_new[last]
        ylo_out[1, x] = ey_new[last]
        ylo_out[2, x] = ez_new[last]
        ylo_out[3, x] = hx[last]
        ylo_out[4, x] = hz[last]
        yhi_out[0, x] = ex_new[0:1]
        yhi_out[1, x] = ez_new[0:1]
        if x == 0:
            xhi_out[0] = ey_new
            xhi_out[1] = ez_new
            c2_out[...] = ey_new[last]
        if x == planes - 1:
            xlo_out[0] = ex_new
            xlo_out[1] = ey_new
            xlo_out[2] = ez_new
            xlo_out[3] = hy
            xlo_out[4] = hz
            c1_out[...] = ex_new[0:1]
        hy_prev = hy
        hz_prev = hz


def _halo_kernel(e_ref, h_ref, xlo_out, xhi_out, y_out, c1_out, c2_out):
    planes = e_ref.shape[1]
    cells = e_ref.shape[2]
    last = slice(cells - 1, cells)
    for x in range(planes):
        ex = e_ref[0, x]
        ez = e_ref[2, x]
        y_out[0, x] = ex[last]
        y_out[1, x] = e_ref[1, x][last]
        y_out[2, x] = ez[last]
        y_out[3, x] = h_ref[0, x][last]
        y_out[4, x] = h_ref[2, x][last]
        y_out[5, x] = ex[0:1]
        y_out[6, x] = ez[0:1]
    xhi_out[0] = e_ref[1, 0]
    xhi_out[1] = e_ref[2, 0]
    c2_out[...] = e_ref[1, 0][last]
    xlo_out[0] = e_ref[0, planes - 1]
    xlo_out[1] = e_ref[1, planes - 1]
    xlo_out[2] = e_ref[2, planes - 1]
    xlo_out[3] = h_ref[1, planes - 1]
    xlo_out[4] = h_ref[2, planes - 1]
    c1_out[...] = e_ref[0, planes - 1][0:1]


def diagonal(value, step_x, step_y):
    count_x = lax.axis_size("gx")
    count_y = lax.axis_size("gy")
    pairs = []
    for a in range(count_x):
        for b in range(count_y):
            target = ((a + step_x) % count_x) * count_y + (b + step_y) % count_y
            pairs.append((a * count_y + b, target))
    return lax.ppermute(value, ("gx", "gy"), pairs)


def exchange(halo):
    xlo, xhi, rows, c1, c2 = halo
    if lax.axis_size("gy") == 2:
        rows = shifted(rows, "gy", 1)
    else:
        rows = jnp.concatenate([shifted(rows[0:5], "gy", 1), shifted(rows[5:7], "gy", -1)])
    return (
        shifted(xlo, "gx", 1),
        shifted(xhi, "gx", -1),
        rows,
        diagonal(c1, 1, -1),
        diagonal(c2, -1, 1),
    )


def trig_basis(angle_orders, cells_x, cells_y):
    size_x = lax.axis_size("gx")
    size_y = lax.axis_size("gy")
    total_x = cells_x * size_x
    total_y = cells_y * size_y
    pos_x = lax.axis_index("gx") * cells_x + jnp.arange(cells_x, dtype=jnp.int32)
    pos_y = lax.axis_index("gy") * cells_y + jnp.arange(cells_y, dtype=jnp.int32)
    order_x = angle_orders[:, 0]
    order_y = angle_orders[:, 1]
    phase_int = (
        order_x[:, None, None] * pos_x[None, :, None] * total_y
        + order_y[:, None, None] * pos_y[None, None, :] * total_x
    ) % (total_x * total_y)
    theta = phase_int.astype(jnp.float32) * (2.0 * math.pi / (total_x * total_y))
    theta = theta.reshape(angle_orders.shape[0], cells_x * cells_y)
    return jnp.concatenate([jnp.cos(theta), jnp.sin(theta)])


def transform(basis, columns):
    return jnp.dot(basis, columns, precision=lax.Precision.HIGHEST, preferred_element_type=jnp.float32)


def flat(plane):
    return plane.reshape(plane.shape[0], -1).T


def scatter_sum(rows, axis, owned):
    count = lax.axis_size(axis)
    index = lax.axis_index(axis)
    if count & (count - 1):
        return lax.psum_scatter(rows, axis, scatter_dimension=0, tiled=True)
    stride = count // 2
    while stride >= 1:
        half = rows.shape[0] // 2
        lower = rows[:half]
        upper = rows[half:]
        high = (index & stride) != 0
        keep = jnp.where(high, upper, lower)
        send = jnp.where(high, lower, upper)
        pairs = [(source, source ^ stride) for source in range(count)]
        rows = keep + lax.ppermute(send, axis, pairs)
        stride //= 2
    return rows


def pair_sum(value, axis):
    count = lax.axis_size(axis)
    if count == 1:
        return value
    if count == 2:
        return value + lax.ppermute(value, axis, [(0, 1), (1, 0)])
    return lax.psum(value, axis)


def local(e_field, h_field, material, eps_table, sigma_table, angle_orders):
    comps, cells_x, cells_y, depth = e_field.shape
    f32 = jnp.float32
    field_shape = jax.ShapeDtypeStruct(e_field.shape, f32)
    halo_shapes = (
        jax.ShapeDtypeStruct((5, cells_y, depth), f32),
        jax.ShapeDtypeStruct((2, cells_y, depth), f32),
        jax.ShapeDtypeStruct((7, cells_x, 1, depth), f32),
        jax.ShapeDtypeStruct((1, depth), f32),
        jax.ShapeDtypeStruct((1, depth), f32),
    )
    step_call = pl.pallas_call(_step_kernel, out_shape=(field_shape, field_shape) + halo_shapes)
    halo = pl.pallas_call(_halo_kernel, out_shape=halo_shapes)(e_field, h_field)
    received = exchange(halo)
    keep, drive = coefficients(material, eps_table, sigma_table)
    basis = trig_basis(angle_orders, cells_x, cells_y)
    keep, drive, basis, received = lax.optimization_barrier((keep, drive, basis, received))
    angle_count = angle_orders.shape[0]
    elec = e_field
    magn = h_field
    mon_real = jnp.zeros((2, cells_x, cells_y), f32)
    mon_imag = jnp.zeros((2, cells_x, cells_y), f32)
    early = jnp.zeros((2 * angle_count, 4), f32)
    for number in range(ITERS):
        if number > 0:
            received = exchange(halo)
        if number == ITERS - 1 and number > 0:
            early = transform(basis, jnp.concatenate([flat(mon_real), flat(mon_imag)], axis=1))
            early, received = lax.optimization_barrier((early, received))
        elec, magn, *halo = step_call(elec, magn, keep, drive, *received)
        if number < ITERS - 1:
            plane = elec[0:2, :, :, depth - 3]
            mon_real = mon_real + math.cos(PHASE_STEP * (number + 1)) * plane
            mon_imag = mon_imag - math.sin(PHASE_STEP * (number + 1)) * plane
    late = transform(basis, flat(elec[0:2, :, :, depth - 3]))
    cos_last = math.cos(PHASE_STEP * ITERS)
    sin_last = math.sin(PHASE_STEP * ITERS)
    cos_rows = slice(0, angle_count)
    sin_rows = slice(angle_count, 2 * angle_count)
    columns = []
    for comp in range(2):
        cos_p = late[cos_rows, comp]
        sin_p = late[sin_rows, comp]
        real = early[cos_rows, comp] + early[sin_rows, 2 + comp] + (cos_last * cos_p - sin_last * sin_p)
        imag = early[cos_rows, 2 + comp] - early[sin_rows, comp] - (sin_last * cos_p + cos_last * sin_p)
        columns += [real, imag]
    terms = jnp.stack(columns, axis=1)
    owned = angle_count // lax.axis_size("gx")
    scale = 1.0 / math.sqrt(cells_x * lax.axis_size("gx") * cells_y * lax.axis_size("gy"))
    far_field = scatter_sum(terms, "gx", owned)
    far_field = pair_sum(far_field, "gy") * scale
    return (elec, magn, far_field)


def solution(mesh):
    return jax.shard_map(
        local,
        mesh=mesh,
        in_specs=(
            P(None, ("clip", "gx"), "gy", None),
            P(None, ("clip", "gx"), "gy", None),
            P(("clip", "gx"), "gy", None),
            P(),
            P(),
            P(),
        ),
        out_specs=(
            P(None, ("clip", "gx"), "gy", None),
            P(None, ("clip", "gx"), "gy", None),
            P(("clip", "gx"), None),
        ),
        check_vma=False,
    )
```

```python
import math

import jax
import jax.numpy as jnp
from jax import lax
from jax.experimental import pallas as pl
from jax.experimental.pallas import tpu as pltpu
from jax.sharding import PartitionSpec as P

ITERS = 4


TIME_STEP = 0.5
PHASE_STEP = 0.9


def shifted(value, axis, steps):
    count = lax.axis_size(axis)
    pairs = [(source, (source + steps) % count) for source in range(count)]
    return lax.ppermute(value, axis, pairs)


def _coef_kernel(eps_ref, sigma_ref, mat_ref, keep_out, drive_out):
    planes = mat_ref.shape[0]
    for x in range(planes):
        material = mat_ref[x]
        permit = jnp.zeros(material.shape, jnp.float32)
        conduct = jnp.zeros(material.shape, jnp.float32)
        for label in range(eps_ref.shape[0]):
            hit = material == label
            permit = jnp.where(hit, eps_ref[label], permit)
            conduct = jnp.where(hit, sigma_ref[label], conduct)
        loss = conduct * TIME_STEP / (2.0 * permit)
        keep_out[x] = (1.0 - loss) / (1.0 + loss)
        drive_out[x] = TIME_STEP / (permit * (1.0 + loss))


def coefficients(material, eps_table, sigma_table):
    scalar = pl.BlockSpec(memory_space=pltpu.SMEM)
    whole = pl.BlockSpec(memory_space=pltpu.VMEM)
    out = jax.ShapeDtypeStruct(material.shape, jnp.float32)
    return pl.pallas_call(
        _coef_kernel,
        out_shape=(out, out),
        in_specs=[scalar, scalar, whole],
        out_specs=(whole, whole),
    )(eps_table, sigma_table, material)


def _z_up(f):
    depth = f.shape[-1]
    lane = lax.broadcasted_iota(jnp.int32, f.shape, 1)
    up = pltpu.roll(f, depth - 1, 1)
    return jnp.where(lane == depth - 1, 0.0, up) - f


def _z_down(f):
    lane = lax.broadcasted_iota(jnp.int32, f.shape, 1)
    down = pltpu.roll(f, 1, 1)
    return f - jnp.where(lane == 0, 0.0, down)


def _y_up(f, row):
    cells = f.shape[0]
    index = lax.broadcasted_iota(jnp.int32, f.shape, 0)
    up = pltpu.roll(f, cells - 1, 0)
    return jnp.where(index == cells - 1, row, up) - f


def _y_down(f, row):
    index = lax.broadcasted_iota(jnp.int32, f.shape, 0)
    down = pltpu.roll(f, 1, 0)
    return f - jnp.where(index == 0, row, down)


def _step_kernel(e_ref, h_ref, keep_ref, drive_ref, xlo_ref, xhi_ref, y_ref,
                 e_out, h_out, xlo_out, xhi_out, y_out):
    c1_ref = y_ref.at[7, 0]
    c2_ref = y_ref.at[8, 0]
    ylo_ref = y_ref
    yhi_ref = y_ref.at[5:7]
    ylo_out = y_out
    yhi_out = y_out.at[5:7]
    planes = e_ref.shape[1]
    cells = e_ref.shape[2]
    ex_p = xlo_ref[0]
    ey_p = xlo_ref[1]
    ez_p = xlo_ref[2]
    hy_prev = xlo_ref[3] - TIME_STEP * (_z_up(ex_p) - (e_ref[2, 0] - ez_p))
    hz_prev = xlo_ref[4] - TIME_STEP * ((e_ref[1, 0] - ey_p) - _y_up(ex_p, c1_ref[...]))
    for x in range(planes):
        ex = e_ref[0, x]
        ey = e_ref[1, x]
        ez = e_ref[2, x]
        if x + 1 < planes:
            ey_next = e_ref[1, x + 1]
            ez_next = e_ref[2, x + 1]
            ey_m_next = ylo_ref[1, x + 1]
        else:
            ey_next = xhi_ref[0]
            ez_next = xhi_ref[1]
            ey_m_next = c2_ref[...]
        hx = h_ref[0, x] - TIME_STEP * (_y_up(ez, yhi_ref[1, x]) - _z_up(ey))
        hy = h_ref[1, x] - TIME_STEP * (_z_up(ex) - (ez_next - ez))
        hz = h_ref[2, x] - TIME_STEP * ((ey_next - ey) - _y_up(ex, yhi_ref[0, x]))
        ex_m = ylo_ref[0, x]
        ey_m = ylo_ref[1, x]
        ez_m = ylo_ref[2, x]
        hx_r = ylo_ref[3, x] - TIME_STEP * ((ez[0:1] - ez_m) - _z_up(ey_m))
        hz_r = ylo_ref[4, x] - TIME_STEP * ((ey_m_next - ey_m) - (ex[0:1] - ex_m))
        keep = keep_ref[x]
        drive = drive_ref[x]
        ex_new = keep * ex + drive * (_y_down(hz, hz_r) - _z_down(hy))
        ey_new = keep * ey + drive * (_z_down(hx) - (hz - hz_prev))
        ez_new = keep * ez + drive * ((hy - hy_prev) - _y_down(hx, hx_r))
        e_out[0, x] = ex_new
        e_out[1, x] = ey_new
        e_out[2, x] = ez_new
        h_out[0, x] = hx
        h_out[1, x] = hy
        h_out[2, x] = hz
        last = slice(cells - 1, cells)
        ylo_out[0, x] = ex_new[last]
        ylo_out[1, x] = ey_new[last]
        ylo_out[2, x] = ez_new[last]
        ylo_out[3, x] = hx[last]
        ylo_out[4, x] = hz[last]
        yhi_out[0, x] = ex_new[0:1]
        yhi_out[1, x] = ez_new[0:1]
        if x == 0:
            xhi_out[0] = ey_new
            xhi_out[1] = ez_new
        if x == planes - 1:
            xlo_out[0] = ex_new
            xlo_out[1] = ey_new
            xlo_out[2] = ez_new
            xlo_out[3] = hy
            xlo_out[4] = hz
        hy_prev = hy
        hz_prev = hz


def _halo_kernel(e_ref, h_ref, xlo_out, xhi_out, y_out):
    planes = e_ref.shape[1]
    cells = e_ref.shape[2]
    last = slice(cells - 1, cells)
    for x in range(planes):
        ex = e_ref[0, x]
        ez = e_ref[2, x]
        y_out[0, x] = ex[last]
        y_out[1, x] = e_ref[1, x][last]
        y_out[2, x] = ez[last]
        y_out[3, x] = h_ref[0, x][last]
        y_out[4, x] = h_ref[2, x][last]
        y_out[5, x] = ex[0:1]
        y_out[6, x] = ez[0:1]
    xhi_out[0] = e_ref[1, 0]
    xhi_out[1] = e_ref[2, 0]
    xlo_out[0] = e_ref[0, planes - 1]
    xlo_out[1] = e_ref[1, planes - 1]
    xlo_out[2] = e_ref[2, planes - 1]
    xlo_out[3] = h_ref[1, planes - 1]
    xlo_out[4] = h_ref[2, planes - 1]


def exchange(halo):
    xlo, xhi, rows = halo
    xlo = shifted(xlo, "gx", 1)
    xhi = shifted(xhi, "gx", -1)
    cells = xhi.shape[1]
    corners = jnp.zeros((2,) + rows.shape[1:], rows.dtype)
    corners = corners.at[0, 0].set(xlo[0, 0:1]).at[1, 0].set(xhi[0, cells - 1:cells])
    message = jnp.concatenate([rows, corners])
    if lax.axis_size("gy") == 2:
        rows = shifted(message, "gy", 1)
    else:
        before = shifted(message, "gy", 1)
        after = shifted(message, "gy", -1)
        rows = jnp.concatenate([before[0:5], after[5:8], before[8:9]])
    return (xlo, xhi, rows)


def trig_basis(angle_orders, cells_x, cells_y):
    size_x = lax.axis_size("gx")
    size_y = lax.axis_size("gy")
    total_x = cells_x * size_x
    total_y = cells_y * size_y
    pos_x = lax.axis_index("gx") * cells_x + jnp.arange(cells_x, dtype=jnp.int32)
    pos_y = lax.axis_index("gy") * cells_y + jnp.arange(cells_y, dtype=jnp.int32)
    order_x = angle_orders[:, 0]
    order_y = angle_orders[:, 1]
    phase_int = (
        order_x[:, None, None] * pos_x[None, :, None] * total_y
        + order_y[:, None, None] * pos_y[None, None, :] * total_x
    ) % (total_x * total_y)
    theta = phase_int.astype(jnp.float32) * (2.0 * math.pi / (total_x * total_y))
    theta = theta.reshape(angle_orders.shape[0], cells_x * cells_y)
    return jnp.concatenate([jnp.cos(theta), jnp.sin(theta)])


def transform(basis, columns):
    return jnp.dot(basis, columns, precision=lax.Precision.HIGHEST, preferred_element_type=jnp.float32)


def flat(plane):
    return plane.reshape(plane.shape[0], -1).T


def scatter_sum(rows, axis, owned):
    count = lax.axis_size(axis)
    index = lax.axis_index(axis)
    if count & (count - 1):
        return lax.psum_scatter(rows, axis, scatter_dimension=0, tiled=True)
    stride = count // 2
    while stride >= 1:
        half = rows.shape[0] // 2
        lower = rows[:half]
        upper = rows[half:]
        high = (index & stride) != 0
        keep = jnp.where(high, upper, lower)
        send = jnp.where(high, lower, upper)
        pairs = [(source, source ^ stride) for source in range(count)]
        rows = keep + lax.ppermute(send, axis, pairs)
        stride //= 2
    return rows


def pair_sum(value, axis):
    count = lax.axis_size(axis)
    if count == 1:
        return value
    if count == 2:
        return value + lax.ppermute(value, axis, [(0, 1), (1, 0)])
    return lax.psum(value, axis)


def local(e_field, h_field, material, eps_table, sigma_table, angle_orders):
    comps, cells_x, cells_y, depth = e_field.shape
    f32 = jnp.float32
    field_shape = jax.ShapeDtypeStruct(e_field.shape, f32)
    halo_shapes = (
        jax.ShapeDtypeStruct((5, cells_y, depth), f32),
        jax.ShapeDtypeStruct((2, cells_y, depth), f32),
        jax.ShapeDtypeStruct((7, cells_x, 1, depth), f32),
    )
    step_call = pl.pallas_call(_step_kernel, out_shape=(field_shape, field_shape) + halo_shapes)
    halo = pl.pallas_call(_halo_kernel, out_shape=halo_shapes)(e_field, h_field)
    received = exchange(halo)
    keep, drive = coefficients(material, eps_table, sigma_table)
    basis = trig_basis(angle_orders, cells_x, cells_y)
    keep, drive, basis, received = lax.optimization_barrier((keep, drive, basis, received))
    angle_count = angle_orders.shape[0]
    elec = e_field
    magn = h_field
    mon_real = jnp.zeros((2, cells_x, cells_y), f32)
    mon_imag = jnp.zeros((2, cells_x, cells_y), f32)
    early = jnp.zeros((2 * angle_count, 4), f32)
    for number in range(ITERS):
        if number > 0:
            received = exchange(halo)
        if number == ITERS - 1 and number > 0:
            early = transform(basis, jnp.concatenate([flat(mon_real), flat(mon_imag)], axis=1))
            early, received = lax.optimization_barrier((early, received))
        elec, magn, *halo = step_call(elec, magn, keep, drive, *received)
        if number < ITERS - 1:
            plane = elec[0:2, :, :, depth - 3]
            mon_real = mon_real + math.cos(PHASE_STEP * (number + 1)) * plane
            mon_imag = mon_imag - math.sin(PHASE_STEP * (number + 1)) * plane
    late = transform(basis, flat(elec[0:2, :, :, depth - 3]))
    cos_last = math.cos(PHASE_STEP * ITERS)
    sin_last = math.sin(PHASE_STEP * ITERS)
    cos_rows = slice(0, angle_count)
    sin_rows = slice(angle_count, 2 * angle_count)
    columns = []
    for comp in range(2):
        cos_p = late[cos_rows, comp]
        sin_p = late[sin_rows, comp]
        real = early[cos_rows, comp] + early[sin_rows, 2 + comp] + (cos_last * cos_p - sin_last * sin_p)
        imag = early[cos_rows, 2 + comp] - early[sin_rows, comp] - (sin_last * cos_p + cos_last * sin_p)
        columns += [real, imag]
    terms = jnp.stack(columns, axis=1)
    owned = angle_count // lax.axis_size("gx")
    scale = 1.0 / math.sqrt(cells_x * lax.axis_size("gx") * cells_y * lax.axis_size("gy"))
    far_field = scatter_sum(terms, "gx", owned)
    far_field = pair_sum(far_field, "gy") * scale
    return (elec, magn, far_field)


def solution(mesh):
    return jax.shard_map(
        local,
        mesh=mesh,
        in_specs=(
            P(None, ("clip", "gx"), "gy", None),
            P(None, ("clip", "gx"), "gy", None),
            P(("clip", "gx"), "gy", None),
            P(),
            P(),
            P(),
        ),
        out_specs=(
            P(None, ("clip", "gx"), "gy", None),
            P(None, ("clip", "gx"), "gy", None),
            P(("clip", "gx"), None),
        ),
        check_vma=False,
    )
```

```python
import math

import jax
import jax.numpy as jnp
from jax import lax
from jax.experimental import pallas as pl
from jax.experimental.pallas import tpu as pltpu
from jax.sharding import PartitionSpec as P

ITERS = 4


TIME_STEP = 0.5
PHASE_STEP = 0.9


def shifted(value, axis, steps):
    count = lax.axis_size(axis)
    pairs = [(source, (source + steps) % count) for source in range(count)]
    return lax.ppermute(value, axis, pairs)


def _coef_kernel(eps_ref, sigma_ref, mat_ref, keep_out, drive_out):
    planes = mat_ref.shape[0]
    for x in range(planes):
        material = mat_ref[x]
        permit = jnp.zeros(material.shape, jnp.float32)
        conduct = jnp.zeros(material.shape, jnp.float32)
        for label in range(eps_ref.shape[0]):
            hit = material == label
            permit = jnp.where(hit, eps_ref[label], permit)
            conduct = jnp.where(hit, sigma_ref[label], conduct)
        loss = conduct * TIME_STEP / (2.0 * permit)
        keep_out[x] = (1.0 - loss) / (1.0 + loss)
        drive_out[x] = TIME_STEP / (permit * (1.0 + loss))


def coefficients(material, eps_table, sigma_table):
    scalar = pl.BlockSpec(memory_space=pltpu.SMEM)
    whole = pl.BlockSpec(memory_space=pltpu.VMEM)
    out = jax.ShapeDtypeStruct(material.shape, jnp.float32)
    return pl.pallas_call(
        _coef_kernel,
        out_shape=(out, out),
        in_specs=[scalar, scalar, whole],
        out_specs=(whole, whole),
    )(eps_table, sigma_table, material)


def _z_up(f):
    depth = f.shape[-1]
    lane = lax.broadcasted_iota(jnp.int32, f.shape, 1)
    up = pltpu.roll(f, depth - 1, 1)
    return jnp.where(lane == depth - 1, 0.0, up) - f


def _z_down(f):
    lane = lax.broadcasted_iota(jnp.int32, f.shape, 1)
    down = pltpu.roll(f, 1, 1)
    return f - jnp.where(lane == 0, 0.0, down)


def _y_up(f, row):
    cells = f.shape[0]
    index = lax.broadcasted_iota(jnp.int32, f.shape, 0)
    up = pltpu.roll(f, cells - 1, 0)
    return jnp.where(index == cells - 1, row, up) - f


def _y_down(f, row):
    index = lax.broadcasted_iota(jnp.int32, f.shape, 0)
    down = pltpu.roll(f, 1, 0)
    return f - jnp.where(index == 0, row, down)


def _step_body(e_ref, h_ref, keep_ref, drive_ref, xlo_ref, xhi_ref, y_ref,
               e_out, h_out, xlo_out, xhi_out, y_out, ready, done):
    c1_ref = y_ref.at[7, 0]
    c2_ref = y_ref.at[8, 0]
    ylo_ref = y_ref
    yhi_ref = y_ref.at[5:7]
    ylo_out = y_out
    yhi_out = y_out.at[5:7]
    planes = e_ref.shape[1]
    cells = e_ref.shape[2]
    ready(0)
    ex_p = xlo_ref[0]
    ey_p = xlo_ref[1]
    ez_p = xlo_ref[2]
    hy_prev = xlo_ref[3] - TIME_STEP * (_z_up(ex_p) - (e_ref[2, 0] - ez_p))
    hz_prev = xlo_ref[4] - TIME_STEP * ((e_ref[1, 0] - ey_p) - _y_up(ex_p, c1_ref[...]))
    for x in range(planes):
        if x + 1 < planes:
            ready(x + 1)
        ex = e_ref[0, x]
        ey = e_ref[1, x]
        ez = e_ref[2, x]
        if x + 1 < planes:
            ey_next = e_ref[1, x + 1]
            ez_next = e_ref[2, x + 1]
            ey_m_next = ylo_ref[1, x + 1]
        else:
            ey_next = xhi_ref[0]
            ez_next = xhi_ref[1]
            ey_m_next = c2_ref[...]
        hx = h_ref[0, x] - TIME_STEP * (_y_up(ez, yhi_ref[1, x]) - _z_up(ey))
        hy = h_ref[1, x] - TIME_STEP * (_z_up(ex) - (ez_next - ez))
        hz = h_ref[2, x] - TIME_STEP * ((ey_next - ey) - _y_up(ex, yhi_ref[0, x]))
        ex_m = ylo_ref[0, x]
        ey_m = ylo_ref[1, x]
        ez_m = ylo_ref[2, x]
        hx_r = ylo_ref[3, x] - TIME_STEP * ((ez[0:1] - ez_m) - _z_up(ey_m))
        hz_r = ylo_ref[4, x] - TIME_STEP * ((ey_m_next - ey_m) - (ex[0:1] - ex_m))
        keep = keep_ref[x]
        drive = drive_ref[x]
        ex_new = keep * ex + drive * (_y_down(hz, hz_r) - _z_down(hy))
        ey_new = keep * ey + drive * (_z_down(hx) - (hz - hz_prev))
        ez_new = keep * ez + drive * ((hy - hy_prev) - _y_down(hx, hx_r))
        e_out[0, x] = ex_new
        e_out[1, x] = ey_new
        e_out[2, x] = ez_new
        h_out[0, x] = hx
        h_out[1, x] = hy
        h_out[2, x] = hz
        done(x)
        last = slice(cells - 1, cells)
        ylo_out[0, x] = ex_new[last]
        ylo_out[1, x] = ey_new[last]
        ylo_out[2, x] = ez_new[last]
        ylo_out[3, x] = hx[last]
        ylo_out[4, x] = hz[last]
        yhi_out[0, x] = ex_new[0:1]
        yhi_out[1, x] = ez_new[0:1]
        if x == 0:
            xhi_out[0] = ey_new
            xhi_out[1] = ez_new
        if x == planes - 1:
            xlo_out[0] = ex_new
            xlo_out[1] = ey_new
            xlo_out[2] = ez_new
            xlo_out[3] = hy
            xlo_out[4] = hz
        hy_prev = hy
        hz_prev = hz


def _step_kernel(e_hbm, h_hbm, keep_hbm, drive_hbm, xlo_ref, xhi_ref, y_ref,
                 e_hbm_out, h_hbm_out, xlo_out, xhi_out, y_out,
                 e_v, h_v, keep_v, drive_v, e_new, h_new, in_sem, out_sem):
    planes = e_hbm.shape[1]

    def fetch(x):
        return [
            pltpu.make_async_copy(e_hbm.at[:, x], e_v.at[:, x], in_sem.at[0, x]),
            pltpu.make_async_copy(h_hbm.at[:, x], h_v.at[:, x], in_sem.at[1, x]),
            pltpu.make_async_copy(keep_hbm.at[x], keep_v.at[x], in_sem.at[2, x]),
            pltpu.make_async_copy(drive_hbm.at[x], drive_v.at[x], in_sem.at[3, x]),
        ]

    fetches = [fetch(x) for x in range(planes)]
    for group in fetches:
        for copy in group:
            copy.start()
    stores = []

    def ready(x):
        for copy in fetches[x]:
            copy.wait()

    def done(x):
        for source, target, index in ((e_new, e_hbm_out, 0), (h_new, h_hbm_out, 1)):
            copy = pltpu.make_async_copy(source.at[:, x], target.at[:, x], out_sem.at[index, x])
            copy.start()
            stores.append(copy)

    _step_body(e_v, h_v, keep_v, drive_v, xlo_ref, xhi_ref, y_ref,
               e_new, h_new, xlo_out, xhi_out, y_out, ready, done)
    for copy in stores:
        copy.wait()


def _halo_kernel(e_ref, h_ref, xlo_out, xhi_out, y_out):
    planes = e_ref.shape[1]
    cells = e_ref.shape[2]
    last = slice(cells - 1, cells)
    for x in range(planes):
        ex = e_ref[0, x]
        ez = e_ref[2, x]
        y_out[0, x] = ex[last]
        y_out[1, x] = e_ref[1, x][last]
        y_out[2, x] = ez[last]
        y_out[3, x] = h_ref[0, x][last]
        y_out[4, x] = h_ref[2, x][last]
        y_out[5, x] = ex[0:1]
        y_out[6, x] = ez[0:1]
    xhi_out[0] = e_ref[1, 0]
    xhi_out[1] = e_ref[2, 0]
    xlo_out[0] = e_ref[0, planes - 1]
    xlo_out[1] = e_ref[1, planes - 1]
    xlo_out[2] = e_ref[2, planes - 1]
    xlo_out[3] = h_ref[1, planes - 1]
    xlo_out[4] = h_ref[2, planes - 1]


def exchange(halo):
    xlo, xhi, rows = halo
    xlo = shifted(xlo, "gx", 1)
    xhi = shifted(xhi, "gx", -1)
    cells = xhi.shape[1]
    corners = jnp.zeros((2,) + rows.shape[1:], rows.dtype)
    corners = corners.at[0, 0].set(xlo[0, 0:1]).at[1, 0].set(xhi[0, cells - 1:cells])
    message = jnp.concatenate([rows, corners])
    if lax.axis_size("gy") == 2:
        rows = shifted(message, "gy", 1)
    else:
        before = shifted(message, "gy", 1)
        after = shifted(message, "gy", -1)
        rows = jnp.concatenate([before[0:5], after[5:8], before[8:9]])
    return (xlo, xhi, rows)


def trig_basis(angle_orders, cells_x, cells_y):
    size_x = lax.axis_size("gx")
    size_y = lax.axis_size("gy")
    total_x = cells_x * size_x
    total_y = cells_y * size_y
    pos_x = lax.axis_index("gx") * cells_x + jnp.arange(cells_x, dtype=jnp.int32)
    pos_y = lax.axis_index("gy") * cells_y + jnp.arange(cells_y, dtype=jnp.int32)
    order_x = angle_orders[:, 0]
    order_y = angle_orders[:, 1]
    phase_int = (
        order_x[:, None, None] * pos_x[None, :, None] * total_y
        + order_y[:, None, None] * pos_y[None, None, :] * total_x
    ) % (total_x * total_y)
    theta = phase_int.astype(jnp.float32) * (2.0 * math.pi / (total_x * total_y))
    theta = theta.reshape(angle_orders.shape[0], cells_x * cells_y)
    return jnp.concatenate([jnp.cos(theta), jnp.sin(theta)])


def transform(basis, columns):
    return jnp.dot(basis, columns, precision=lax.Precision.HIGHEST, preferred_element_type=jnp.float32)


def flat(plane):
    return plane.reshape(plane.shape[0], -1).T


def scatter_sum(rows, axis, owned):
    count = lax.axis_size(axis)
    index = lax.axis_index(axis)
    if count & (count - 1):
        return lax.psum_scatter(rows, axis, scatter_dimension=0, tiled=True)
    stride = count // 2
    while stride >= 1:
        half = rows.shape[0] // 2
        lower = rows[:half]
        upper = rows[half:]
        high = (index & stride) != 0
        keep = jnp.where(high, upper, lower)
        send = jnp.where(high, lower, upper)
        pairs = [(source, source ^ stride) for source in range(count)]
        rows = keep + lax.ppermute(send, axis, pairs)
        stride //= 2
    return rows


def pair_sum(value, axis):
    count = lax.axis_size(axis)
    if count == 1:
        return value
    if count == 2:
        return value + lax.ppermute(value, axis, [(0, 1), (1, 0)])
    return lax.psum(value, axis)


def local(e_field, h_field, material, eps_table, sigma_table, angle_orders):
    comps, cells_x, cells_y, depth = e_field.shape
    f32 = jnp.float32
    field_shape = jax.ShapeDtypeStruct(e_field.shape, f32)
    halo_shapes = (
        jax.ShapeDtypeStruct((5, cells_y, depth), f32),
        jax.ShapeDtypeStruct((2, cells_y, depth), f32),
        jax.ShapeDtypeStruct((7, cells_x, 1, depth), f32),
    )
    vmem = pl.BlockSpec(memory_space=pltpu.VMEM)
    anywhere = pl.BlockSpec(memory_space=pl.ANY)
    step_call = pl.pallas_call(
        _step_kernel,
        out_shape=(field_shape, field_shape) + halo_shapes,
        in_specs=[anywhere] * 4 + [vmem] * 3,
        out_specs=(anywhere, anywhere) + (vmem,) * 3,
        scratch_shapes=[
            pltpu.VMEM(e_field.shape, f32),
            pltpu.VMEM(e_field.shape, f32),
            pltpu.VMEM(material.shape, f32),
            pltpu.VMEM(material.shape, f32),
            pltpu.VMEM(e_field.shape, f32),
            pltpu.VMEM(e_field.shape, f32),
            pltpu.SemaphoreType.DMA((4, cells_x)),
            pltpu.SemaphoreType.DMA((2, cells_x)),
        ],
    )
    halo = pl.pallas_call(_halo_kernel, out_shape=halo_shapes)(e_field, h_field)
    received = exchange(halo)
    keep, drive = coefficients(material, eps_table, sigma_table)
    basis = trig_basis(angle_orders, cells_x, cells_y)
    keep, drive, basis, received = lax.optimization_barrier((keep, drive, basis, received))
    angle_count = angle_orders.shape[0]
    elec = e_field
    magn = h_field
    mon_real = jnp.zeros((2, cells_x, cells_y), f32)
    mon_imag = jnp.zeros((2, cells_x, cells_y), f32)
    early = jnp.zeros((2 * angle_count, 4), f32)
    for number in range(ITERS):
        if number > 0:
            received = exchange(halo)
        if number == ITERS - 1 and number > 0:
            early = transform(basis, jnp.concatenate([flat(mon_real), flat(mon_imag)], axis=1))
            early, received = lax.optimization_barrier((early, received))
        elec, magn, *halo = step_call(elec, magn, keep, drive, *received)
        if number < ITERS - 1:
            plane = elec[0:2, :, :, depth - 3]
            mon_real = mon_real + math.cos(PHASE_STEP * (number + 1)) * plane
            mon_imag = mon_imag - math.sin(PHASE_STEP * (number + 1)) * plane
    late = transform(basis, flat(elec[0:2, :, :, depth - 3]))
    cos_last = math.cos(PHASE_STEP * ITERS)
    sin_last = math.sin(PHASE_STEP * ITERS)
    cos_rows = slice(0, angle_count)
    sin_rows = slice(angle_count, 2 * angle_count)
    columns = []
    for comp in range(2):
        cos_p = late[cos_rows, comp]
        sin_p = late[sin_rows, comp]
        real = early[cos_rows, comp] + early[sin_rows, 2 + comp] + (cos_last * cos_p - sin_last * sin_p)
        imag = early[cos_rows, 2 + comp] - early[sin_rows, comp] - (sin_last * cos_p + cos_last * sin_p)
        columns += [real, imag]
    terms = jnp.stack(columns, axis=1)
    owned = angle_count // lax.axis_size("gx")
    scale = 1.0 / math.sqrt(cells_x * lax.axis_size("gx") * cells_y * lax.axis_size("gy"))
    far_field = scatter_sum(terms, "gx", owned)
    far_field = pair_sum(far_field, "gy") * scale
    return (elec, magn, far_field)


def solution(mesh):
    return jax.shard_map(
        local,
        mesh=mesh,
        in_specs=(
            P(None, ("clip", "gx"), "gy", None),
            P(None, ("clip", "gx"), "gy", None),
            P(("clip", "gx"), "gy", None),
            P(),
            P(),
            P(),
        ),
        out_specs=(
            P(None, ("clip", "gx"), "gy", None),
            P(None, ("clip", "gx"), "gy", None),
            P(("clip", "gx"), None),
        ),
        check_vma=False,
    )
```

```python
import functools
import math

import jax
import jax.numpy as jnp
from jax import lax
from jax.experimental import pallas as pl
from jax.experimental.pallas import tpu as pltpu
from jax.sharding import PartitionSpec as P

ITERS = 4


TIME_STEP = 0.5
PHASE_STEP = 0.9


def shifted(value, axis, steps):
    count = lax.axis_size(axis)
    pairs = [(source, (source + steps) % count) for source in range(count)]
    return lax.ppermute(value, axis, pairs)


def _coef_kernel(eps_ref, sigma_ref, mat_ref, keep_out, drive_out):
    planes = mat_ref.shape[0]
    for x in range(planes):
        material = mat_ref[x]
        permit = jnp.zeros(material.shape, jnp.float32)
        conduct = jnp.zeros(material.shape, jnp.float32)
        for label in range(eps_ref.shape[0]):
            hit = material == label
            permit = jnp.where(hit, eps_ref[label], permit)
            conduct = jnp.where(hit, sigma_ref[label], conduct)
        loss = conduct * TIME_STEP / (2.0 * permit)
        keep_out[x] = (1.0 - loss) / (1.0 + loss)
        drive_out[x] = TIME_STEP / (permit * (1.0 + loss))


def coefficients(material, eps_table, sigma_table):
    scalar = pl.BlockSpec(memory_space=pltpu.SMEM)
    whole = pl.BlockSpec(memory_space=pltpu.VMEM)
    out = jax.ShapeDtypeStruct(material.shape, jnp.float32)
    return pl.pallas_call(
        _coef_kernel,
        out_shape=(out, out),
        in_specs=[scalar, scalar, whole],
        out_specs=(whole, whole),
    )(eps_table, sigma_table, material)


def _z_up(f):
    depth = f.shape[-1]
    lane = lax.broadcasted_iota(jnp.int32, f.shape, 1)
    up = pltpu.roll(f, depth - 1, 1)
    return jnp.where(lane == depth - 1, 0.0, up) - f


def _z_down(f):
    lane = lax.broadcasted_iota(jnp.int32, f.shape, 1)
    down = pltpu.roll(f, 1, 1)
    return f - jnp.where(lane == 0, 0.0, down)


def _y_up(f, row):
    cells = f.shape[0]
    index = lax.broadcasted_iota(jnp.int32, f.shape, 0)
    up = pltpu.roll(f, cells - 1, 0)
    return jnp.where(index == cells - 1, row, up) - f


def _y_down(f, row):
    index = lax.broadcasted_iota(jnp.int32, f.shape, 0)
    down = pltpu.roll(f, 1, 0)
    return f - jnp.where(index == 0, row, down)


def _magn_plane(elec, magn, x, planes, xhi_ref, yhi_ref):
    ex = elec(0, x)
    ey = elec(1, x)
    ez = elec(2, x)
    if x + 1 < planes:
        ey_next = elec(1, x + 1)
        ez_next = elec(2, x + 1)
    else:
        ey_next = xhi_ref[0]
        ez_next = xhi_ref[1]
    hx = magn(0, x) - TIME_STEP * (_y_up(ez, yhi_ref[1, x]) - _z_up(ey))
    hy = magn(1, x) - TIME_STEP * (_z_up(ex) - (ez_next - ez))
    hz = magn(2, x) - TIME_STEP * ((ey_next - ey) - _y_up(ex, yhi_ref[0, x]))
    return (ex, ey, ez, hx, hy, hz)


def _magn_before(elec, xlo_ref, c1_ref):
    ex_p = xlo_ref[0]
    ey_p = xlo_ref[1]
    ez_p = xlo_ref[2]
    hy = xlo_ref[3] - TIME_STEP * (_z_up(ex_p) - (elec(2, 0) - ez_p))
    hz = xlo_ref[4] - TIME_STEP * ((elec(1, 0) - ey_p) - _y_up(ex_p, c1_ref[...]))
    return (hy, hz)


def _elec_plane(x, planes, old, hy_prev, hz_prev, ylo_ref, c2_ref, keep, drive):
    ex, ey, ez, hx, hy, hz = old
    if x + 1 < planes:
        ey_m_next = ylo_ref[1, x + 1]
    else:
        ey_m_next = c2_ref[...]
    ex_m = ylo_ref[0, x]
    ey_m = ylo_ref[1, x]
    ez_m = ylo_ref[2, x]
    hx_r = ylo_ref[3, x] - TIME_STEP * ((ez[0:1] - ez_m) - _z_up(ey_m))
    hz_r = ylo_ref[4, x] - TIME_STEP * ((ey_m_next - ey_m) - (ex[0:1] - ex_m))
    ex_new = keep * ex + drive * (_y_down(hz, hz_r) - _z_down(hy))
    ey_new = keep * ey + drive * (_z_down(hx) - (hz - hz_prev))
    ez_new = keep * ez + drive * ((hy - hy_prev) - _y_down(hx, hx_r))
    return (ex_new, ey_new, ez_new)


def _step_kernel(e_ref, h_ref, keep_ref, drive_ref, xlo_ref, xhi_ref, y_ref, e_out, h_out, y_out):
    c1_ref = y_ref.at[7, 0]
    c2_ref = y_ref.at[8, 0]
    yhi_ref = y_ref.at[5:7]
    planes = e_ref.shape[1]
    cells = e_ref.shape[2]
    elec = lambda comp, x: e_ref[comp, x]
    magn = lambda comp, x: h_ref[comp, x]
    hy_prev, hz_prev = _magn_before(elec, xlo_ref, c1_ref)
    for x in range(planes):
        old = _magn_plane(elec, magn, x, planes, xhi_ref, yhi_ref)
        ex_new, ey_new, ez_new = _elec_plane(
            x, planes, old, hy_prev, hz_prev, y_ref, c2_ref, keep_ref[x], drive_ref[x]
        )
        hx, hy, hz = old[3:]
        e_out[0, x] = ex_new
        e_out[1, x] = ey_new
        e_out[2, x] = ez_new
        h_out[0, x] = hx
        h_out[1, x] = hy
        h_out[2, x] = hz
        last = slice(cells - 1, cells)
        y_out[0, x] = ex_new[last]
        y_out[1, x] = ey_new[last]
        y_out[2, x] = ez_new[last]
        y_out[3, x] = hx[last]
        y_out[4, x] = hz[last]
        y_out[5, x] = ex_new[0:1]
        y_out[6, x] = ez_new[0:1]
        hy_prev = hy
        hz_prev = hz


def _edge_kernel(e_first, e_second, e_penult, e_last, h_first, h_penult, h_last,
                 keep_first, keep_last, drive_first, drive_last, xlo_ref, xhi_ref, y_ref,
                 xlo_out, xhi_out, *, planes):
    c1_ref = y_ref.at[7, 0]
    c2_ref = y_ref.at[8, 0]
    yhi_ref = y_ref.at[5:7]
    e_blocks = {0: e_first, 1: e_second, planes - 2: e_penult, planes - 1: e_last}
    h_blocks = {0: h_first, planes - 2: h_penult, planes - 1: h_last}
    elec = lambda comp, x: e_blocks[x][comp, 0]
    magn = lambda comp, x: h_blocks[x][comp, 0]
    hy_prev, hz_prev = _magn_before(elec, xlo_ref, c1_ref)
    old = _magn_plane(elec, magn, 0, planes, xhi_ref, yhi_ref)
    ex_new, ey_new, ez_new = _elec_plane(
        0, planes, old, hy_prev, hz_prev, y_ref, c2_ref, keep_first[0], drive_first[0]
    )
    xhi_out[0] = ey_new
    xhi_out[1] = ez_new
    penult = _magn_plane(elec, magn, planes - 2, planes, xhi_ref, yhi_ref)
    old = _magn_plane(elec, magn, planes - 1, planes, xhi_ref, yhi_ref)
    ex_new, ey_new, ez_new = _elec_plane(
        planes - 1, planes, old, penult[4], penult[5], y_ref, c2_ref, keep_last[0], drive_last[0]
    )
    xlo_out[0] = ex_new
    xlo_out[1] = ey_new
    xlo_out[2] = ez_new
    xlo_out[3] = old[4]
    xlo_out[4] = old[5]


def _halo_kernel(e_ref, h_ref, xlo_out, xhi_out, y_out):
    planes = e_ref.shape[1]
    cells = e_ref.shape[2]
    last = slice(cells - 1, cells)
    for x in range(planes):
        ex = e_ref[0, x]
        ez = e_ref[2, x]
        y_out[0, x] = ex[last]
        y_out[1, x] = e_ref[1, x][last]
        y_out[2, x] = ez[last]
        y_out[3, x] = h_ref[0, x][last]
        y_out[4, x] = h_ref[2, x][last]
        y_out[5, x] = ex[0:1]
        y_out[6, x] = ez[0:1]
    xhi_out[0] = e_ref[1, 0]
    xhi_out[1] = e_ref[2, 0]
    xlo_out[0] = e_ref[0, planes - 1]
    xlo_out[1] = e_ref[1, planes - 1]
    xlo_out[2] = e_ref[2, planes - 1]
    xlo_out[3] = h_ref[1, planes - 1]
    xlo_out[4] = h_ref[2, planes - 1]


def exchange_x(xlo, xhi):
    return (shifted(xlo, "gx", 1), shifted(xhi, "gx", -1))


def exchange_y(rows, xlo, xhi):
    cells = xhi.shape[1]
    corners = jnp.zeros((2,) + rows.shape[1:], rows.dtype)
    corners = corners.at[0, 0].set(xlo[0, 0:1]).at[1, 0].set(xhi[0, cells - 1:cells])
    message = jnp.concatenate([rows, corners])
    if lax.axis_size("gy") == 2:
        return shifted(message, "gy", 1)
    before = shifted(message, "gy", 1)
    after = shifted(message, "gy", -1)
    return jnp.concatenate([before[0:5], after[5:8], before[8:9]])


def trig_basis(angle_orders, cells_x, cells_y):
    size_x = lax.axis_size("gx")
    size_y = lax.axis_size("gy")
    total_x = cells_x * size_x
    total_y = cells_y * size_y
    pos_x = lax.axis_index("gx") * cells_x + jnp.arange(cells_x, dtype=jnp.int32)
    pos_y = lax.axis_index("gy") * cells_y + jnp.arange(cells_y, dtype=jnp.int32)
    order_x = angle_orders[:, 0]
    order_y = angle_orders[:, 1]
    phase_int = (
        order_x[:, None, None] * pos_x[None, :, None] * total_y
        + order_y[:, None, None] * pos_y[None, None, :] * total_x
    ) % (total_x * total_y)
    theta = phase_int.astype(jnp.float32) * (2.0 * math.pi / (total_x * total_y))
    theta = theta.reshape(angle_orders.shape[0], cells_x * cells_y)
    return jnp.concatenate([jnp.cos(theta), jnp.sin(theta)])


def transform(basis, columns):
    return jnp.dot(basis, columns, precision=lax.Precision.HIGHEST, preferred_element_type=jnp.float32)


def flat(plane):
    return plane.reshape(plane.shape[0], -1).T


def scatter_sum(rows, axis, owned):
    count = lax.axis_size(axis)
    index = lax.axis_index(axis)
    if count & (count - 1):
        return lax.psum_scatter(rows, axis, scatter_dimension=0, tiled=True)
    stride = count // 2
    while stride >= 1:
        half = rows.shape[0] // 2
        lower = rows[:half]
        upper = rows[half:]
        high = (index & stride) != 0
        keep = jnp.where(high, upper, lower)
        send = jnp.where(high, lower, upper)
        pairs = [(source, source ^ stride) for source in range(count)]
        rows = keep + lax.ppermute(send, axis, pairs)
        stride //= 2
    return rows


def pair_sum(value, axis):
    count = lax.axis_size(axis)
    if count == 1:
        return value
    if count == 2:
        return value + lax.ppermute(value, axis, [(0, 1), (1, 0)])
    return lax.psum(value, axis)


def local(e_field, h_field, material, eps_table, sigma_table, angle_orders):
    comps, cells_x, cells_y, depth = e_field.shape
    f32 = jnp.float32
    field_shape = jax.ShapeDtypeStruct(e_field.shape, f32)
    xlo_shape = jax.ShapeDtypeStruct((5, cells_y, depth), f32)
    xhi_shape = jax.ShapeDtypeStruct((2, cells_y, depth), f32)
    rows_shape = jax.ShapeDtypeStruct((7, cells_x, 1, depth), f32)
    step_call = pl.pallas_call(_step_kernel, out_shape=(field_shape, field_shape, rows_shape))
    whole = pl.BlockSpec(memory_space=pltpu.VMEM)

    def field_plane(index):
        return pl.BlockSpec((comps, 1, cells_y, depth), lambda i: (0, index, 0, 0))

    def coef_plane(index):
        return pl.BlockSpec((1, cells_y, depth), lambda i: (index, 0, 0))

    first = 0
    last = cells_x - 1
    edge_call = pl.pallas_call(
        functools.partial(_edge_kernel, planes=cells_x),
        out_shape=(xlo_shape, xhi_shape),
        grid=(1,),
        in_specs=[field_plane(i) for i in (first, 1, last - 1, last)]
        + [field_plane(i) for i in (first, last - 1, last)]
        + [coef_plane(first), coef_plane(last), coef_plane(first), coef_plane(last)]
        + [whole] * 3,
        out_specs=(whole, whole),
    )
    xlo, xhi, rows = pl.pallas_call(_halo_kernel, out_shape=(xlo_shape, xhi_shape, rows_shape))(
        e_field, h_field
    )
    xlo, xhi = exchange_x(xlo, xhi)
    rows = exchange_y(rows, xlo, xhi)
    keep, drive = coefficients(material, eps_table, sigma_table)
    basis = trig_basis(angle_orders, cells_x, cells_y)
    keep, drive, basis, xlo, xhi, rows = lax.optimization_barrier((keep, drive, basis, xlo, xhi, rows))
    angle_count = angle_orders.shape[0]
    elec = e_field
    magn = h_field
    mon_real = jnp.zeros((2, cells_x, cells_y), f32)
    mon_imag = jnp.zeros((2, cells_x, cells_y), f32)
    early = jnp.zeros((2 * angle_count, 4), f32)
    for number in range(ITERS):
        if number == ITERS - 1 and number > 0:
            early = transform(basis, jnp.concatenate([flat(mon_real), flat(mon_imag)], axis=1))
            early, xlo, xhi, rows = lax.optimization_barrier((early, xlo, xhi, rows))
        if number + 1 < ITERS:
            edges = edge_call(
                elec, elec, elec, elec, magn, magn, magn, keep, keep, drive, drive, xlo, xhi, rows
            )
            next_xlo, next_xhi = exchange_x(*edges)
        elec, magn, new_rows = step_call(elec, magn, keep, drive, xlo, xhi, rows)
        if number + 1 < ITERS:
            xlo, xhi = next_xlo, next_xhi
            rows = exchange_y(new_rows, xlo, xhi)
        if number < ITERS - 1:
            plane = elec[0:2, :, :, depth - 3]
            mon_real = mon_real + math.cos(PHASE_STEP * (number + 1)) * plane
            mon_imag = mon_imag - math.sin(PHASE_STEP * (number + 1)) * plane
    late = transform(basis, flat(elec[0:2, :, :, depth - 3]))
    cos_last = math.cos(PHASE_STEP * ITERS)
    sin_last = math.sin(PHASE_STEP * ITERS)
    cos_rows = slice(0, angle_count)
    sin_rows = slice(angle_count, 2 * angle_count)
    columns = []
    for comp in range(2):
        cos_p = late[cos_rows, comp]
        sin_p = late[sin_rows, comp]
        real = early[cos_rows, comp] + early[sin_rows, 2 + comp] + (cos_last * cos_p - sin_last * sin_p)
        imag = early[cos_rows, 2 + comp] - early[sin_rows, comp] - (sin_last * cos_p + cos_last * sin_p)
        columns += [real, imag]
    terms = jnp.stack(columns, axis=1)
    owned = angle_count // lax.axis_size("gx")
    scale = 1.0 / math.sqrt(cells_x * lax.axis_size("gx") * cells_y * lax.axis_size("gy"))
    far_field = scatter_sum(terms, "gx", owned)
    far_field = pair_sum(far_field, "gy") * scale
    return (elec, magn, far_field)


def solution(mesh):
    return jax.shard_map(
        local,
        mesh=mesh,
        in_specs=(
            P(None, ("clip", "gx"), "gy", None),
            P(None, ("clip", "gx"), "gy", None),
            P(("clip", "gx"), "gy", None),
            P(),
            P(),
            P(),
        ),
        out_specs=(
            P(None, ("clip", "gx"), "gy", None),
            P(None, ("clip", "gx"), "gy", None),
            P(("clip", "gx"), None),
        ),
        check_vma=False,
    )
```

```python
import functools
import math

import jax
import jax.numpy as jnp
from jax import lax
from jax.experimental import pallas as pl
from jax.experimental.pallas import tpu as pltpu
from jax.sharding import PartitionSpec as P

ITERS = 4


TIME_STEP = 0.5
PHASE_STEP = 0.9


def shifted(value, axis, steps):
    count = lax.axis_size(axis)
    pairs = [(source, (source + steps) % count) for source in range(count)]
    return lax.ppermute(value, axis, pairs)


def _coef_kernel(eps_ref, sigma_ref, mat_ref, keep_out, drive_out):
    planes = mat_ref.shape[0]
    for x in range(planes):
        material = mat_ref[x]
        permit = jnp.zeros(material.shape, jnp.float32)
        conduct = jnp.zeros(material.shape, jnp.float32)
        for label in range(eps_ref.shape[0]):
            hit = material == label
            permit = jnp.where(hit, eps_ref[label], permit)
            conduct = jnp.where(hit, sigma_ref[label], conduct)
        loss = conduct * TIME_STEP / (2.0 * permit)
        keep_out[x] = (1.0 - loss) / (1.0 + loss)
        drive_out[x] = TIME_STEP / (permit * (1.0 + loss))


def coefficients(material, eps_table, sigma_table):
    scalar = pl.BlockSpec(memory_space=pltpu.SMEM)
    whole = pl.BlockSpec(memory_space=pltpu.VMEM)
    out = jax.ShapeDtypeStruct(material.shape, jnp.float32)
    return pl.pallas_call(
        _coef_kernel,
        out_shape=(out, out),
        in_specs=[scalar, scalar, whole],
        out_specs=(whole, whole),
    )(eps_table, sigma_table, material)


def _z_up(f):
    depth = f.shape[-1]
    lane = lax.broadcasted_iota(jnp.int32, f.shape, 1)
    up = pltpu.roll(f, depth - 1, 1)
    return jnp.where(lane == depth - 1, 0.0, up) - f


def _z_down(f):
    lane = lax.broadcasted_iota(jnp.int32, f.shape, 1)
    down = pltpu.roll(f, 1, 1)
    return f - jnp.where(lane == 0, 0.0, down)


def _y_up(f, row):
    cells = f.shape[0]
    index = lax.broadcasted_iota(jnp.int32, f.shape, 0)
    up = pltpu.roll(f, cells - 1, 0)
    return jnp.where(index == cells - 1, row, up) - f


def _y_down(f, row):
    index = lax.broadcasted_iota(jnp.int32, f.shape, 0)
    down = pltpu.roll(f, 1, 0)
    return f - jnp.where(index == 0, row, down)


def _magn_plane(elec, magn, x, planes, xhi_ref, yhi_ref):
    ex = elec(0, x)
    ey = elec(1, x)
    ez = elec(2, x)
    if x + 1 < planes:
        ey_next = elec(1, x + 1)
        ez_next = elec(2, x + 1)
    else:
        ey_next = xhi_ref[0]
        ez_next = xhi_ref[1]
    hx = magn(0, x) - TIME_STEP * (_y_up(ez, yhi_ref[1, x]) - _z_up(ey))
    hy = magn(1, x) - TIME_STEP * (_z_up(ex) - (ez_next - ez))
    hz = magn(2, x) - TIME_STEP * ((ey_next - ey) - _y_up(ex, yhi_ref[0, x]))
    return (ex, ey, ez, hx, hy, hz)


def _magn_before(elec, xlo_ref, c1_ref):
    ex_p = xlo_ref[0]
    ey_p = xlo_ref[1]
    ez_p = xlo_ref[2]
    hy = xlo_ref[3] - TIME_STEP * (_z_up(ex_p) - (elec(2, 0) - ez_p))
    hz = xlo_ref[4] - TIME_STEP * ((elec(1, 0) - ey_p) - _y_up(ex_p, c1_ref[...]))
    return (hy, hz)


def _elec_plane(x, planes, old, hy_prev, hz_prev, ylo_ref, c2_ref, keep, drive):
    ex, ey, ez, hx, hy, hz = old
    if x + 1 < planes:
        ey_m_next = ylo_ref[1, x + 1]
    else:
        ey_m_next = c2_ref[...]
    ex_m = ylo_ref[0, x]
    ey_m = ylo_ref[1, x]
    ez_m = ylo_ref[2, x]
    hx_r = ylo_ref[3, x] - TIME_STEP * ((ez[0:1] - ez_m) - _z_up(ey_m))
    hz_r = ylo_ref[4, x] - TIME_STEP * ((ey_m_next - ey_m) - (ex[0:1] - ex_m))
    ex_new = keep * ex + drive * (_y_down(hz, hz_r) - _z_down(hy))
    ey_new = keep * ey + drive * (_z_down(hx) - (hz - hz_prev))
    ez_new = keep * ez + drive * ((hy - hy_prev) - _y_down(hx, hx_r))
    return (ex_new, ey_new, ez_new)


def _step_kernel(e_ref, h_ref, keep_ref, drive_ref, xlo_ref, xhi_ref, y_ref, basis_ref,
                 e_out, h_out, y_out, g_out):
    c1_ref = y_ref.at[7, 0]
    c2_ref = y_ref.at[8, 0]
    yhi_ref = y_ref.at[5:7]
    planes = e_ref.shape[1]
    cells = e_ref.shape[2]
    elec = lambda comp, x: e_ref[comp, x]
    magn = lambda comp, x: h_ref[comp, x]
    hy_prev, hz_prev = _magn_before(elec, xlo_ref, c1_ref)
    sums = [None, None]
    for x in range(planes):
        old = _magn_plane(elec, magn, x, planes, xhi_ref, yhi_ref)
        ex_new, ey_new, ez_new = _elec_plane(
            x, planes, old, hy_prev, hz_prev, y_ref, c2_ref, keep_ref[x], drive_ref[x]
        )
        hx, hy, hz = old[3:]
        e_out[0, x] = ex_new
        e_out[1, x] = ey_new
        e_out[2, x] = ez_new
        h_out[0, x] = hx
        h_out[1, x] = hy
        h_out[2, x] = hz
        last = slice(cells - 1, cells)
        y_out[0, x] = ex_new[last]
        y_out[1, x] = ey_new[last]
        y_out[2, x] = ez_new[last]
        y_out[3, x] = hx[last]
        y_out[4, x] = hz[last]
        y_out[5, x] = ex_new[0:1]
        y_out[6, x] = ez_new[0:1]
        hy_prev = hy
        hz_prev = hz
        for comp, field in ((0, ex_new), (1, ey_new)):
            part = jnp.dot(basis_ref[x], field, precision=lax.Precision.HIGHEST,
                           preferred_element_type=jnp.float32)
            sums[comp] = part if sums[comp] is None else sums[comp] + part
    g_out[0] = sums[0]
    g_out[1] = sums[1]


def _edge_kernel(e_first, e_second, e_penult, e_last, h_first, h_penult, h_last,
                 keep_first, keep_last, drive_first, drive_last, xlo_ref, xhi_ref, y_ref,
                 xlo_out, xhi_out, *, planes):
    c1_ref = y_ref.at[7, 0]
    c2_ref = y_ref.at[8, 0]
    yhi_ref = y_ref.at[5:7]
    e_blocks = {0: e_first, 1: e_second, planes - 2: e_penult, planes - 1: e_last}
    h_blocks = {0: h_first, planes - 2: h_penult, planes - 1: h_last}
    elec = lambda comp, x: e_blocks[x][comp, 0]
    magn = lambda comp, x: h_blocks[x][comp, 0]
    hy_prev, hz_prev = _magn_before(elec, xlo_ref, c1_ref)
    old = _magn_plane(elec, magn, 0, planes, xhi_ref, yhi_ref)
    ex_new, ey_new, ez_new = _elec_plane(
        0, planes, old, hy_prev, hz_prev, y_ref, c2_ref, keep_first[0], drive_first[0]
    )
    xhi_out[0] = ey_new
    xhi_out[1] = ez_new
    penult = _magn_plane(elec, magn, planes - 2, planes, xhi_ref, yhi_ref)
    old = _magn_plane(elec, magn, planes - 1, planes, xhi_ref, yhi_ref)
    ex_new, ey_new, ez_new = _elec_plane(
        planes - 1, planes, old, penult[4], penult[5], y_ref, c2_ref, keep_last[0], drive_last[0]
    )
    xlo_out[0] = ex_new
    xlo_out[1] = ey_new
    xlo_out[2] = ez_new
    xlo_out[3] = old[4]
    xlo_out[4] = old[5]


def _halo_kernel(e_ref, h_ref, xlo_out, xhi_out, y_out):
    planes = e_ref.shape[1]
    cells = e_ref.shape[2]
    last = slice(cells - 1, cells)
    for x in range(planes):
        ex = e_ref[0, x]
        ez = e_ref[2, x]
        y_out[0, x] = ex[last]
        y_out[1, x] = e_ref[1, x][last]
        y_out[2, x] = ez[last]
        y_out[3, x] = h_ref[0, x][last]
        y_out[4, x] = h_ref[2, x][last]
        y_out[5, x] = ex[0:1]
        y_out[6, x] = ez[0:1]
    xhi_out[0] = e_ref[1, 0]
    xhi_out[1] = e_ref[2, 0]
    xlo_out[0] = e_ref[0, planes - 1]
    xlo_out[1] = e_ref[1, planes - 1]
    xlo_out[2] = e_ref[2, planes - 1]
    xlo_out[3] = h_ref[1, planes - 1]
    xlo_out[4] = h_ref[2, planes - 1]


def exchange_x(xlo, xhi):
    return (shifted(xlo, "gx", 1), shifted(xhi, "gx", -1))


def exchange_y(rows, xlo, xhi):
    cells = xhi.shape[1]
    corners = jnp.zeros((2,) + rows.shape[1:], rows.dtype)
    corners = corners.at[0, 0].set(xlo[0, 0:1]).at[1, 0].set(xhi[0, cells - 1:cells])
    message = jnp.concatenate([rows, corners])
    if lax.axis_size("gy") == 2:
        return shifted(message, "gy", 1)
    before = shifted(message, "gy", 1)
    after = shifted(message, "gy", -1)
    return jnp.concatenate([before[0:5], after[5:8], before[8:9]])


def trig_basis(angle_orders, cells_x, cells_y):
    size_x = lax.axis_size("gx")
    size_y = lax.axis_size("gy")
    total_x = cells_x * size_x
    total_y = cells_y * size_y
    pos_x = lax.axis_index("gx") * cells_x + jnp.arange(cells_x, dtype=jnp.int32)
    pos_y = lax.axis_index("gy") * cells_y + jnp.arange(cells_y, dtype=jnp.int32)
    order_x = angle_orders[:, 0]
    order_y = angle_orders[:, 1]
    phase_int = (
        order_x[:, None, None] * pos_x[None, :, None] * total_y
        + order_y[:, None, None] * pos_y[None, None, :] * total_x
    ) % (total_x * total_y)
    theta = phase_int.astype(jnp.float32) * (2.0 * math.pi / (total_x * total_y))
    theta = theta.reshape(angle_orders.shape[0], cells_x * cells_y)
    return jnp.concatenate([jnp.cos(theta), jnp.sin(theta)])


def transform(basis, columns):
    return jnp.dot(basis, columns, precision=lax.Precision.HIGHEST, preferred_element_type=jnp.float32)


def flat(plane):
    return plane.reshape(plane.shape[0], -1).T


def scatter_sum(rows, axis, owned):
    count = lax.axis_size(axis)
    index = lax.axis_index(axis)
    if count & (count - 1):
        return lax.psum_scatter(rows, axis, scatter_dimension=0, tiled=True)
    stride = count // 2
    while stride >= 1:
        half = rows.shape[0] // 2
        lower = rows[:half]
        upper = rows[half:]
        high = (index & stride) != 0
        keep = jnp.where(high, upper, lower)
        send = jnp.where(high, lower, upper)
        pairs = [(source, source ^ stride) for source in range(count)]
        rows = keep + lax.ppermute(send, axis, pairs)
        stride //= 2
    return rows


def pair_sum(value, axis):
    count = lax.axis_size(axis)
    if count == 1:
        return value
    if count == 2:
        return value + lax.ppermute(value, axis, [(0, 1), (1, 0)])
    return lax.psum(value, axis)


def local(e_field, h_field, material, eps_table, sigma_table, angle_orders):
    comps, cells_x, cells_y, depth = e_field.shape
    f32 = jnp.float32
    field_shape = jax.ShapeDtypeStruct(e_field.shape, f32)
    xlo_shape = jax.ShapeDtypeStruct((5, cells_y, depth), f32)
    xhi_shape = jax.ShapeDtypeStruct((2, cells_y, depth), f32)
    rows_shape = jax.ShapeDtypeStruct((7, cells_x, 1, depth), f32)
    angle_count = angle_orders.shape[0]
    sums_shape = jax.ShapeDtypeStruct((2, 2 * angle_count, depth), f32)
    step_call = pl.pallas_call(
        _step_kernel, out_shape=(field_shape, field_shape, rows_shape, sums_shape)
    )
    whole = pl.BlockSpec(memory_space=pltpu.VMEM)

    def field_plane(index):
        return pl.BlockSpec((comps, 1, cells_y, depth), lambda i: (0, index, 0, 0))

    def coef_plane(index):
        return pl.BlockSpec((1, cells_y, depth), lambda i: (index, 0, 0))

    first = 0
    last = cells_x - 1
    edge_call = pl.pallas_call(
        functools.partial(_edge_kernel, planes=cells_x),
        out_shape=(xlo_shape, xhi_shape),
        grid=(1,),
        in_specs=[field_plane(i) for i in (first, 1, last - 1, last)]
        + [field_plane(i) for i in (first, last - 1, last)]
        + [coef_plane(first), coef_plane(last), coef_plane(first), coef_plane(last)]
        + [whole] * 3,
        out_specs=(whole, whole),
    )
    xlo, xhi, rows = pl.pallas_call(_halo_kernel, out_shape=(xlo_shape, xhi_shape, rows_shape))(
        e_field, h_field
    )
    xlo, xhi = exchange_x(xlo, xhi)
    keep, drive = coefficients(material, eps_table, sigma_table)
    keep, drive, xlo, xhi = lax.optimization_barrier((keep, drive, xlo, xhi))
    rows = exchange_y(rows, xlo, xhi)
    basis = trig_basis(angle_orders, cells_x, cells_y)
    basis = basis.reshape(2 * angle_count, cells_x, cells_y).transpose(1, 0, 2)
    basis, rows = lax.optimization_barrier((basis, rows))
    elec = e_field
    magn = h_field
    columns = [[], []]
    for number in range(ITERS):
        if number + 1 < ITERS:
            edges = edge_call(
                elec, elec, elec, elec, magn, magn, magn, keep, keep, drive, drive, xlo, xhi, rows
            )
            next_xlo, next_xhi = exchange_x(*edges)
        elec, magn, new_rows, sums = step_call(elec, magn, keep, drive, xlo, xhi, rows, basis)
        if number + 1 < ITERS:
            xlo, xhi = next_xlo, next_xhi
            rows = exchange_y(new_rows, xlo, xhi)
        weight_cos = math.cos(PHASE_STEP * (number + 1))
        weight_sin = math.sin(PHASE_STEP * (number + 1))
        picked = sums[:, :, depth - 3]
        for comp in range(2):
            cos_p = picked[comp, :angle_count]
            sin_p = picked[comp, angle_count:]
            columns[comp].append((weight_cos * cos_p - weight_sin * sin_p, -weight_sin * cos_p - weight_cos * sin_p))
    stacked = []
    for comp in range(2):
        real = columns[comp][0][0]
        imag = columns[comp][0][1]
        for more_real, more_imag in columns[comp][1:]:
            real = real + more_real
            imag = imag + more_imag
        stacked += [real, imag]
    columns = stacked
    terms = jnp.stack(columns, axis=1)
    owned = angle_count // lax.axis_size("gx")
    scale = 1.0 / math.sqrt(cells_x * lax.axis_size("gx") * cells_y * lax.axis_size("gy"))
    far_field = scatter_sum(terms, "gx", owned)
    far_field = pair_sum(far_field, "gy") * scale
    return (elec, magn, far_field)


def solution(mesh):
    return jax.shard_map(
        local,
        mesh=mesh,
        in_specs=(
            P(None, ("clip", "gx"), "gy", None),
            P(None, ("clip", "gx"), "gy", None),
            P(("clip", "gx"), "gy", None),
            P(),
            P(),
            P(),
        ),
        out_specs=(
            P(None, ("clip", "gx"), "gy", None),
            P(None, ("clip", "gx"), "gy", None),
            P(("clip", "gx"), None),
        ),
        check_vma=False,
    )
```

```python
import functools
import math

import jax
import jax.numpy as jnp
from jax import lax
from jax.experimental import pallas as pl
from jax.experimental.pallas import tpu as pltpu
from jax.sharding import PartitionSpec as P

ITERS = 4


TIME_STEP = 0.5
PHASE_STEP = 0.9


def shifted(value, axis, steps):
    count = lax.axis_size(axis)
    pairs = [(source, (source + steps) % count) for source in range(count)]
    return lax.ppermute(value, axis, pairs)


def _coef_kernel(eps_ref, sigma_ref, mat_ref, keep_out, drive_out):
    planes = mat_ref.shape[0]
    for x in range(planes):
        material = mat_ref[x]
        permit = jnp.zeros(material.shape, jnp.float32)
        conduct = jnp.zeros(material.shape, jnp.float32)
        for label in range(eps_ref.shape[0]):
            hit = material == label
            permit = jnp.where(hit, eps_ref[label], permit)
            conduct = jnp.where(hit, sigma_ref[label], conduct)
        loss = conduct * TIME_STEP / (2.0 * permit)
        keep_out[x] = (1.0 - loss) / (1.0 + loss)
        drive_out[x] = TIME_STEP / (permit * (1.0 + loss))


def coefficients(material, eps_table, sigma_table):
    scalar = pl.BlockSpec(memory_space=pltpu.SMEM)
    whole = pl.BlockSpec(memory_space=pltpu.VMEM)
    out = jax.ShapeDtypeStruct(material.shape, jnp.float32)
    return pl.pallas_call(
        _coef_kernel,
        out_shape=(out, out),
        in_specs=[scalar, scalar, whole],
        out_specs=(whole, whole),
    )(eps_table, sigma_table, material)


def _z_up(f):
    depth = f.shape[-1]
    lane = lax.broadcasted_iota(jnp.int32, f.shape, 1)
    up = pltpu.roll(f, depth - 1, 1)
    return jnp.where(lane == depth - 1, 0.0, up) - f


def _z_down(f):
    lane = lax.broadcasted_iota(jnp.int32, f.shape, 1)
    down = pltpu.roll(f, 1, 1)
    return f - jnp.where(lane == 0, 0.0, down)


def _y_up(f, row):
    cells = f.shape[0]
    index = lax.broadcasted_iota(jnp.int32, f.shape, 0)
    up = pltpu.roll(f, cells - 1, 0)
    return jnp.where(index == cells - 1, row, up) - f


def _y_down(f, row):
    index = lax.broadcasted_iota(jnp.int32, f.shape, 0)
    down = pltpu.roll(f, 1, 0)
    return f - jnp.where(index == 0, row, down)


def _magn_plane(elec, magn, x, planes, xhi_ref, yhi_ref):
    ex = elec(0, x)
    ey = elec(1, x)
    ez = elec(2, x)
    if x + 1 < planes:
        ey_next = elec(1, x + 1)
        ez_next = elec(2, x + 1)
    else:
        ey_next = xhi_ref[0]
        ez_next = xhi_ref[1]
    hx = magn(0, x) - TIME_STEP * (_y_up(ez, yhi_ref[1, x]) - _z_up(ey))
    hy = magn(1, x) - TIME_STEP * (_z_up(ex) - (ez_next - ez))
    hz = magn(2, x) - TIME_STEP * ((ey_next - ey) - _y_up(ex, yhi_ref[0, x]))
    return (ex, ey, ez, hx, hy, hz)


def _magn_before(elec, xlo_ref, c1_ref):
    ex_p = xlo_ref[0]
    ey_p = xlo_ref[1]
    ez_p = xlo_ref[2]
    hy = xlo_ref[3] - TIME_STEP * (_z_up(ex_p) - (elec(2, 0) - ez_p))
    hz = xlo_ref[4] - TIME_STEP * ((elec(1, 0) - ey_p) - _y_up(ex_p, c1_ref[...]))
    return (hy, hz)


def _elec_plane(x, planes, old, hy_prev, hz_prev, ylo_ref, c2_ref, keep, drive):
    ex, ey, ez, hx, hy, hz = old
    if x + 1 < planes:
        ey_m_next = ylo_ref[1, x + 1]
    else:
        ey_m_next = c2_ref[...]
    ex_m = ylo_ref[0, x]
    ey_m = ylo_ref[1, x]
    ez_m = ylo_ref[2, x]
    hx_r = ylo_ref[3, x] - TIME_STEP * ((ez[0:1] - ez_m) - _z_up(ey_m))
    hz_r = ylo_ref[4, x] - TIME_STEP * ((ey_m_next - ey_m) - (ex[0:1] - ex_m))
    ex_new = keep * ex + drive * (_y_down(hz, hz_r) - _z_down(hy))
    ey_new = keep * ey + drive * (_z_down(hx) - (hz - hz_prev))
    ez_new = keep * ez + drive * ((hy - hy_prev) - _y_down(hx, hx_r))
    return (ex_new, ey_new, ez_new)


def _step_kernel(e_ref, h_ref, keep_ref, drive_ref, xlo_ref, xhi_ref, y_ref, basis_ref,
                 e_out, h_out, y_out, g_out):
    c1_ref = y_ref.at[7, 0]
    c2_ref = y_ref.at[8, 0]
    yhi_ref = y_ref.at[5:7]
    planes = e_ref.shape[1]
    cells = e_ref.shape[2]
    elec = lambda comp, x: e_ref[comp, x]
    magn = lambda comp, x: h_ref[comp, x]
    hy_prev, hz_prev = _magn_before(elec, xlo_ref, c1_ref)
    sums = [None, None]
    for x in range(planes):
        old = _magn_plane(elec, magn, x, planes, xhi_ref, yhi_ref)
        ex_new, ey_new, ez_new = _elec_plane(
            x, planes, old, hy_prev, hz_prev, y_ref, c2_ref, keep_ref[x], drive_ref[x]
        )
        hx, hy, hz = old[3:]
        e_out[0, x] = ex_new
        e_out[1, x] = ey_new
        e_out[2, x] = ez_new
        h_out[0, x] = hx
        h_out[1, x] = hy
        h_out[2, x] = hz
        last = slice(cells - 1, cells)
        y_out[0, x] = ex_new[last]
        y_out[1, x] = ey_new[last]
        y_out[2, x] = ez_new[last]
        y_out[3, x] = hx[last]
        y_out[4, x] = hz[last]
        y_out[5, x] = ex_new[0:1]
        y_out[6, x] = ez_new[0:1]
        hy_prev = hy
        hz_prev = hz
        for comp, field in ((0, ex_new), (1, ey_new)):
            part = jnp.dot(basis_ref[x], field, precision=lax.Precision.HIGHEST,
                           preferred_element_type=jnp.float32)
            sums[comp] = part if sums[comp] is None else sums[comp] + part
    depth = e_ref.shape[3]
    for comp in range(2):
        g_out[comp] = sums[comp].T[depth - 3:depth - 2]


def _edge_kernel(e_first, e_second, e_penult, e_last, h_first, h_penult, h_last,
                 keep_first, keep_last, drive_first, drive_last, xlo_ref, xhi_ref, y_ref,
                 xlo_out, xhi_out, *, planes):
    c1_ref = y_ref.at[7, 0]
    c2_ref = y_ref.at[8, 0]
    yhi_ref = y_ref.at[5:7]
    e_blocks = {0: e_first, 1: e_second, planes - 2: e_penult, planes - 1: e_last}
    h_blocks = {0: h_first, planes - 2: h_penult, planes - 1: h_last}
    elec = lambda comp, x: e_blocks[x][comp, 0]
    magn = lambda comp, x: h_blocks[x][comp, 0]
    hy_prev, hz_prev = _magn_before(elec, xlo_ref, c1_ref)
    old = _magn_plane(elec, magn, 0, planes, xhi_ref, yhi_ref)
    ex_new, ey_new, ez_new = _elec_plane(
        0, planes, old, hy_prev, hz_prev, y_ref, c2_ref, keep_first[0], drive_first[0]
    )
    xhi_out[0] = ey_new
    xhi_out[1] = ez_new
    penult = _magn_plane(elec, magn, planes - 2, planes, xhi_ref, yhi_ref)
    old = _magn_plane(elec, magn, planes - 1, planes, xhi_ref, yhi_ref)
    ex_new, ey_new, ez_new = _elec_plane(
        planes - 1, planes, old, penult[4], penult[5], y_ref, c2_ref, keep_last[0], drive_last[0]
    )
    xlo_out[0] = ex_new
    xlo_out[1] = ey_new
    xlo_out[2] = ez_new
    xlo_out[3] = old[4]
    xlo_out[4] = old[5]


def _halo_kernel(e_first, e_last, h_last, e_top, e_bottom, h_bottom, xlo_out, xhi_out, y_out):
    planes = e_top.shape[1]
    slab = e_top.shape[2]
    last = slice(slab - 1, slab)
    for x in range(planes):
        y_out[0, x] = e_bottom[0, x][last]
        y_out[1, x] = e_bottom[1, x][last]
        y_out[2, x] = e_bottom[2, x][last]
        y_out[3, x] = h_bottom[0, x][last]
        y_out[4, x] = h_bottom[2, x][last]
        y_out[5, x] = e_top[0, x][0:1]
        y_out[6, x] = e_top[2, x][0:1]
    xhi_out[0] = e_first[1, 0]
    xhi_out[1] = e_first[2, 0]
    xlo_out[0] = e_last[0, 0]
    xlo_out[1] = e_last[1, 0]
    xlo_out[2] = e_last[2, 0]
    xlo_out[3] = h_last[1, 0]
    xlo_out[4] = h_last[2, 0]


def exchange_x(xlo, xhi):
    return (shifted(xlo, "gx", 1), shifted(xhi, "gx", -1))


def exchange_y(rows, xlo, xhi):
    cells = xhi.shape[1]
    corners = jnp.zeros((2,) + rows.shape[1:], rows.dtype)
    corners = corners.at[0, 0].set(xlo[0, 0:1]).at[1, 0].set(xhi[0, cells - 1:cells])
    message = jnp.concatenate([rows, corners])
    if lax.axis_size("gy") == 2:
        return shifted(message, "gy", 1)
    before = shifted(message, "gy", 1)
    after = shifted(message, "gy", -1)
    return jnp.concatenate([before[0:5], after[5:8], before[8:9]])


def trig_basis(angle_orders, cells_x, cells_y):
    size_x = lax.axis_size("gx")
    size_y = lax.axis_size("gy")
    total_x = cells_x * size_x
    total_y = cells_y * size_y
    pos_x = lax.axis_index("gx") * cells_x + jnp.arange(cells_x, dtype=jnp.int32)
    pos_y = lax.axis_index("gy") * cells_y + jnp.arange(cells_y, dtype=jnp.int32)
    order_x = angle_orders[:, 0]
    order_y = angle_orders[:, 1]
    phase_int = (
        order_x[:, None, None] * pos_x[None, :, None] * total_y
        + order_y[:, None, None] * pos_y[None, None, :] * total_x
    ) % (total_x * total_y)
    theta = phase_int.astype(jnp.float32) * (2.0 * math.pi / (total_x * total_y))
    theta = theta.reshape(angle_orders.shape[0], cells_x * cells_y)
    return jnp.concatenate([jnp.cos(theta), jnp.sin(theta)])


def transform(basis, columns):
    return jnp.dot(basis, columns, precision=lax.Precision.HIGHEST, preferred_element_type=jnp.float32)


def flat(plane):
    return plane.reshape(plane.shape[0], -1).T


def scatter_sum(rows, axis, owned):
    count = lax.axis_size(axis)
    index = lax.axis_index(axis)
    if count & (count - 1):
        return lax.psum_scatter(rows, axis, scatter_dimension=0, tiled=True)
    stride = count // 2
    while stride >= 1:
        half = rows.shape[0] // 2
        lower = rows[:half]
        upper = rows[half:]
        high = (index & stride) != 0
        keep = jnp.where(high, upper, lower)
        send = jnp.where(high, lower, upper)
        pairs = [(source, source ^ stride) for source in range(count)]
        rows = keep + lax.ppermute(send, axis, pairs)
        stride //= 2
    return rows


def pair_sum(value, axis):
    count = lax.axis_size(axis)
    if count == 1:
        return value
    if count == 2:
        return value + lax.ppermute(value, axis, [(0, 1), (1, 0)])
    return lax.psum(value, axis)


def local(e_field, h_field, material, eps_table, sigma_table, angle_orders):
    comps, cells_x, cells_y, depth = e_field.shape
    f32 = jnp.float32
    field_shape = jax.ShapeDtypeStruct(e_field.shape, f32)
    xlo_shape = jax.ShapeDtypeStruct((5, cells_y, depth), f32)
    xhi_shape = jax.ShapeDtypeStruct((2, cells_y, depth), f32)
    rows_shape = jax.ShapeDtypeStruct((7, cells_x, 1, depth), f32)
    angle_count = angle_orders.shape[0]
    sums_shape = jax.ShapeDtypeStruct((2, 1, 2 * angle_count), f32)
    step_call = pl.pallas_call(
        _step_kernel, out_shape=(field_shape, field_shape, rows_shape, sums_shape)
    )
    whole = pl.BlockSpec(memory_space=pltpu.VMEM)

    def field_plane(index):
        return pl.BlockSpec((comps, 1, cells_y, depth), lambda i: (0, index, 0, 0))

    def coef_plane(index):
        return pl.BlockSpec((1, cells_y, depth), lambda i: (index, 0, 0))

    first = 0
    last = cells_x - 1
    edge_call = pl.pallas_call(
        functools.partial(_edge_kernel, planes=cells_x),
        out_shape=(xlo_shape, xhi_shape),
        grid=(1,),
        in_specs=[field_plane(i) for i in (first, 1, last - 1, last)]
        + [field_plane(i) for i in (first, last - 1, last)]
        + [coef_plane(first), coef_plane(last), coef_plane(first), coef_plane(last)]
        + [whole] * 3,
        out_specs=(whole, whole),
    )
    slab = 8
    slabs = cells_y // slab

    def row_slab(index):
        return pl.BlockSpec((comps, cells_x, slab, depth), lambda i: (0, 0, index, 0))

    xlo, xhi, rows = pl.pallas_call(
        _halo_kernel,
        out_shape=(xlo_shape, xhi_shape, rows_shape),
        grid=(1,),
        in_specs=[field_plane(first), field_plane(last), field_plane(last),
                  row_slab(0), row_slab(slabs - 1), row_slab(slabs - 1)],
        out_specs=(whole, whole, whole),
    )(e_field, e_field, h_field, e_field, e_field, h_field)
    xlo, xhi = exchange_x(xlo, xhi)
    keep, drive = coefficients(material, eps_table, sigma_table)
    keep, drive, xlo, xhi = lax.optimization_barrier((keep, drive, xlo, xhi))
    rows = exchange_y(rows, xlo, xhi)
    basis = trig_basis(angle_orders, cells_x, cells_y)
    basis = basis.reshape(2 * angle_count, cells_x, cells_y).transpose(1, 0, 2)
    basis, rows = lax.optimization_barrier((basis, rows))
    elec = e_field
    magn = h_field
    columns = [[], []]
    for number in range(ITERS):
        if number + 1 < ITERS:
            edges = edge_call(
                elec, elec, elec, elec, magn, magn, magn, keep, keep, drive, drive, xlo, xhi, rows
            )
            next_xlo, next_xhi = exchange_x(*edges)
        elec, magn, new_rows, sums = step_call(elec, magn, keep, drive, xlo, xhi, rows, basis)
        if number + 1 < ITERS:
            xlo, xhi = next_xlo, next_xhi
            rows = exchange_y(new_rows, xlo, xhi)
        weight_cos = math.cos(PHASE_STEP * (number + 1))
        weight_sin = math.sin(PHASE_STEP * (number + 1))
        picked = sums[:, 0]
        for comp in range(2):
            cos_p = picked[comp, :angle_count]
            sin_p = picked[comp, angle_count:]
            columns[comp].append((weight_cos * cos_p - weight_sin * sin_p, -weight_sin * cos_p - weight_cos * sin_p))
    stacked = []
    for comp in range(2):
        real = columns[comp][0][0]
        imag = columns[comp][0][1]
        for more_real, more_imag in columns[comp][1:]:
            real = real + more_real
            imag = imag + more_imag
        stacked += [real, imag]
    columns = stacked
    terms = jnp.stack(columns, axis=1)
    owned = angle_count // lax.axis_size("gx")
    scale = 1.0 / math.sqrt(cells_x * lax.axis_size("gx") * cells_y * lax.axis_size("gy"))
    far_field = scatter_sum(terms, "gx", owned)
    far_field = pair_sum(far_field, "gy") * scale
    return (elec, magn, far_field)


def solution(mesh):
    return jax.shard_map(
        local,
        mesh=mesh,
        in_specs=(
            P(None, ("clip", "gx"), "gy", None),
            P(None, ("clip", "gx"), "gy", None),
            P(("clip", "gx"), "gy", None),
            P(),
            P(),
            P(),
        ),
        out_specs=(
            P(None, ("clip", "gx"), "gy", None),
            P(None, ("clip", "gx"), "gy", None),
            P(("clip", "gx"), None),
        ),
        check_vma=False,
    )
```

```python
import functools
import math

import jax
import jax.numpy as jnp
from jax import lax
from jax.experimental import pallas as pl
from jax.experimental.pallas import tpu as pltpu
from jax.sharding import PartitionSpec as P

ITERS = 4


TIME_STEP = 0.5
PHASE_STEP = 0.9


def shifted(value, axis, steps):
    count = lax.axis_size(axis)
    pairs = [(source, (source + steps) % count) for source in range(count)]
    return lax.ppermute(value, axis, pairs)


def _coef_kernel(eps_ref, sigma_ref, mat_ref, keep_out, drive_out):
    planes = mat_ref.shape[0]
    for x in range(planes):
        material = mat_ref[x]
        permit = jnp.zeros(material.shape, jnp.float32)
        conduct = jnp.zeros(material.shape, jnp.float32)
        for label in range(eps_ref.shape[0]):
            hit = material == label
            permit = jnp.where(hit, eps_ref[label], permit)
            conduct = jnp.where(hit, sigma_ref[label], conduct)
        loss = conduct * TIME_STEP / (2.0 * permit)
        keep_out[x] = (1.0 - loss) / (1.0 + loss)
        drive_out[x] = TIME_STEP / (permit * (1.0 + loss))


def coefficients(material, eps_table, sigma_table):
    scalar = pl.BlockSpec(memory_space=pltpu.SMEM)
    whole = pl.BlockSpec(memory_space=pltpu.VMEM)
    out = jax.ShapeDtypeStruct(material.shape, jnp.float32)
    return pl.pallas_call(
        _coef_kernel,
        out_shape=(out, out),
        in_specs=[scalar, scalar, whole],
        out_specs=(whole, whole),
    )(eps_table, sigma_table, material)


def _z_up(f):
    depth = f.shape[-1]
    lane = lax.broadcasted_iota(jnp.int32, f.shape, 1)
    up = pltpu.roll(f, depth - 1, 1)
    return jnp.where(lane == depth - 1, 0.0, up) - f


def _z_down(f):
    lane = lax.broadcasted_iota(jnp.int32, f.shape, 1)
    down = pltpu.roll(f, 1, 1)
    return f - jnp.where(lane == 0, 0.0, down)


def _y_up(f, row):
    cells = f.shape[0]
    index = lax.broadcasted_iota(jnp.int32, f.shape, 0)
    up = pltpu.roll(f, cells - 1, 0)
    return jnp.where(index == cells - 1, row, up) - f


def _y_down(f, row):
    index = lax.broadcasted_iota(jnp.int32, f.shape, 0)
    down = pltpu.roll(f, 1, 0)
    return f - jnp.where(index == 0, row, down)


def _magn_plane(elec, magn, x, planes, xhi_ref, yhi_ref):
    ex = elec(0, x)
    ey = elec(1, x)
    ez = elec(2, x)
    if x + 1 < planes:
        ey_next = elec(1, x + 1)
        ez_next = elec(2, x + 1)
    else:
        ey_next = xhi_ref[0]
        ez_next = xhi_ref[1]
    hx = magn(0, x) - TIME_STEP * (_y_up(ez, yhi_ref[1, x]) - _z_up(ey))
    hy = magn(1, x) - TIME_STEP * (_z_up(ex) - (ez_next - ez))
    hz = magn(2, x) - TIME_STEP * ((ey_next - ey) - _y_up(ex, yhi_ref[0, x]))
    return (ex, ey, ez, hx, hy, hz)


def _magn_before(elec, xlo_ref, c1_ref):
    ex_p = xlo_ref[0]
    ey_p = xlo_ref[1]
    ez_p = xlo_ref[2]
    hy = xlo_ref[3] - TIME_STEP * (_z_up(ex_p) - (elec(2, 0) - ez_p))
    hz = xlo_ref[4] - TIME_STEP * ((elec(1, 0) - ey_p) - _y_up(ex_p, c1_ref[...]))
    return (hy, hz)


def _elec_plane(x, planes, old, hy_prev, hz_prev, ylo_ref, c2_ref, keep, drive):
    ex, ey, ez, hx, hy, hz = old
    if x + 1 < planes:
        ey_m_next = ylo_ref[1, x + 1]
    else:
        ey_m_next = c2_ref[...]
    ex_m = ylo_ref[0, x]
    ey_m = ylo_ref[1, x]
    ez_m = ylo_ref[2, x]
    hx_r = ylo_ref[3, x] - TIME_STEP * ((ez[0:1] - ez_m) - _z_up(ey_m))
    hz_r = ylo_ref[4, x] - TIME_STEP * ((ey_m_next - ey_m) - (ex[0:1] - ex_m))
    ex_new = keep * ex + drive * (_y_down(hz, hz_r) - _z_down(hy))
    ey_new = keep * ey + drive * (_z_down(hx) - (hz - hz_prev))
    ez_new = keep * ez + drive * ((hy - hy_prev) - _y_down(hx, hx_r))
    return (ex_new, ey_new, ez_new)


def _step_kernel(e_ref, h_ref, keep_ref, drive_ref, xlo_ref, xhi_ref, y_ref, basis_ref,
                 e_out, h_out, y_out, g_out):
    c1_ref = y_ref.at[7, 0]
    c2_ref = y_ref.at[8, 0]
    yhi_ref = y_ref.at[5:7]
    planes = e_ref.shape[1]
    cells = e_ref.shape[2]
    elec = lambda comp, x: e_ref[comp, x]
    magn = lambda comp, x: h_ref[comp, x]
    hy_prev, hz_prev = _magn_before(elec, xlo_ref, c1_ref)
    sums = [None, None]
    for x in range(planes):
        old = _magn_plane(elec, magn, x, planes, xhi_ref, yhi_ref)
        ex_new, ey_new, ez_new = _elec_plane(
            x, planes, old, hy_prev, hz_prev, y_ref, c2_ref, keep_ref[x], drive_ref[x]
        )
        hx, hy, hz = old[3:]
        e_out[0, x] = ex_new
        e_out[1, x] = ey_new
        e_out[2, x] = ez_new
        h_out[0, x] = hx
        h_out[1, x] = hy
        h_out[2, x] = hz
        last = slice(cells - 1, cells)
        y_out[0, x] = ex_new[last]
        y_out[1, x] = ey_new[last]
        y_out[2, x] = ez_new[last]
        y_out[3, x] = hx[last]
        y_out[4, x] = hz[last]
        y_out[5, x] = ex_new[0:1]
        y_out[6, x] = ez_new[0:1]
        hy_prev = hy
        hz_prev = hz
        for comp, field in ((0, ex_new), (1, ey_new)):
            part = jnp.dot(basis_ref[x], field, precision=lax.Precision.HIGHEST,
                           preferred_element_type=jnp.float32)
            sums[comp] = part if sums[comp] is None else sums[comp] + part
    depth = e_ref.shape[3]
    for comp in range(2):
        g_out[comp] = sums[comp].T[depth - 3:depth - 2]


def _edge_kernel(e_first, e_second, e_penult, e_last, h_first, h_penult, h_last,
                 keep_first, keep_last, drive_first, drive_last, xlo_ref, xhi_ref, y_ref,
                 xlo_out, xhi_out, *, planes):
    c1_ref = y_ref.at[7, 0]
    c2_ref = y_ref.at[8, 0]
    yhi_ref = y_ref.at[5:7]
    e_blocks = {0: e_first, 1: e_second, planes - 2: e_penult, planes - 1: e_last}
    h_blocks = {0: h_first, planes - 2: h_penult, planes - 1: h_last}
    elec = lambda comp, x: e_blocks[x][comp, 0]
    magn = lambda comp, x: h_blocks[x][comp, 0]
    hy_prev, hz_prev = _magn_before(elec, xlo_ref, c1_ref)
    old = _magn_plane(elec, magn, 0, planes, xhi_ref, yhi_ref)
    ex_new, ey_new, ez_new = _elec_plane(
        0, planes, old, hy_prev, hz_prev, y_ref, c2_ref, keep_first[0], drive_first[0]
    )
    xhi_out[0] = ey_new
    xhi_out[1] = ez_new
    penult = _magn_plane(elec, magn, planes - 2, planes, xhi_ref, yhi_ref)
    old = _magn_plane(elec, magn, planes - 1, planes, xhi_ref, yhi_ref)
    ex_new, ey_new, ez_new = _elec_plane(
        planes - 1, planes, old, penult[4], penult[5], y_ref, c2_ref, keep_last[0], drive_last[0]
    )
    xlo_out[0] = ex_new
    xlo_out[1] = ey_new
    xlo_out[2] = ez_new
    xlo_out[3] = old[4]
    xlo_out[4] = old[5]


def _halo_kernel(e_first, e_last, h_last, e_top, e_bottom, h_bottom, xlo_out, xhi_out, y_out):
    planes = e_top.shape[1]
    slab = e_top.shape[2]
    last = slice(slab - 1, slab)
    for x in range(planes):
        y_out[0, x] = e_bottom[0, x][last]
        y_out[1, x] = e_bottom[1, x][last]
        y_out[2, x] = e_bottom[2, x][last]
        y_out[3, x] = h_bottom[0, x][last]
        y_out[4, x] = h_bottom[2, x][last]
        y_out[5, x] = e_top[0, x][0:1]
        y_out[6, x] = e_top[2, x][0:1]
    xhi_out[0] = e_first[1, 0]
    xhi_out[1] = e_first[2, 0]
    xlo_out[0] = e_last[0, 0]
    xlo_out[1] = e_last[1, 0]
    xlo_out[2] = e_last[2, 0]
    xlo_out[3] = h_last[1, 0]
    xlo_out[4] = h_last[2, 0]


def exchange_x(xlo, xhi):
    return (shifted(xlo, "gx", 1), shifted(xhi, "gx", -1))


def exchange_y(rows, xlo, xhi):
    cells = xhi.shape[1]
    corners = jnp.stack([xlo[0, 0:1], xhi[0, cells - 1:cells]])[:, None]
    message = lax.dynamic_update_slice(rows, corners, (7, 0, 0, 0))
    if lax.axis_size("gy") == 2:
        return shifted(message, "gy", 1)
    before = shifted(message, "gy", 1)
    after = shifted(message, "gy", -1)
    return jnp.concatenate([before[0:5], after[5:8], before[8:9]])


def trig_basis(angle_orders, cells_x, cells_y):
    size_x = lax.axis_size("gx")
    size_y = lax.axis_size("gy")
    total_x = cells_x * size_x
    total_y = cells_y * size_y
    pos_x = lax.axis_index("gx") * cells_x + jnp.arange(cells_x, dtype=jnp.int32)
    pos_y = lax.axis_index("gy") * cells_y + jnp.arange(cells_y, dtype=jnp.int32)
    order_x = angle_orders[:, 0]
    order_y = angle_orders[:, 1]
    phase_int = (
        order_x[:, None, None] * pos_x[None, :, None] * total_y
        + order_y[:, None, None] * pos_y[None, None, :] * total_x
    ) % (total_x * total_y)
    theta = phase_int.astype(jnp.float32) * (2.0 * math.pi / (total_x * total_y))
    theta = theta.reshape(angle_orders.shape[0], cells_x * cells_y)
    return jnp.concatenate([jnp.cos(theta), jnp.sin(theta)])


def transform(basis, columns):
    return jnp.dot(basis, columns, precision=lax.Precision.HIGHEST, preferred_element_type=jnp.float32)


def flat(plane):
    return plane.reshape(plane.shape[0], -1).T


def scatter_sum(rows, axis, owned):
    count = lax.axis_size(axis)
    index = lax.axis_index(axis)
    if count & (count - 1):
        return lax.psum_scatter(rows, axis, scatter_dimension=0, tiled=True)
    stride = count // 2
    while stride >= 1:
        half = rows.shape[0] // 2
        lower = rows[:half]
        upper = rows[half:]
        high = (index & stride) != 0
        keep = jnp.where(high, upper, lower)
        send = jnp.where(high, lower, upper)
        pairs = [(source, source ^ stride) for source in range(count)]
        rows = keep + lax.ppermute(send, axis, pairs)
        stride //= 2
    return rows


def pair_sum(value, axis):
    count = lax.axis_size(axis)
    if count == 1:
        return value
    if count == 2:
        return value + lax.ppermute(value, axis, [(0, 1), (1, 0)])
    return lax.psum(value, axis)


def local(e_field, h_field, material, eps_table, sigma_table, angle_orders):
    comps, cells_x, cells_y, depth = e_field.shape
    f32 = jnp.float32
    field_shape = jax.ShapeDtypeStruct(e_field.shape, f32)
    xlo_shape = jax.ShapeDtypeStruct((5, cells_y, depth), f32)
    xhi_shape = jax.ShapeDtypeStruct((2, cells_y, depth), f32)
    rows_shape = jax.ShapeDtypeStruct((9, cells_x, 1, depth), f32)
    angle_count = angle_orders.shape[0]
    sums_shape = jax.ShapeDtypeStruct((2, 1, 2 * angle_count), f32)
    step_call = pl.pallas_call(
        _step_kernel, out_shape=(field_shape, field_shape, rows_shape, sums_shape)
    )
    whole = pl.BlockSpec(memory_space=pltpu.VMEM)

    def field_plane(index):
        return pl.BlockSpec((comps, 1, cells_y, depth), lambda i: (0, index, 0, 0))

    def coef_plane(index):
        return pl.BlockSpec((1, cells_y, depth), lambda i: (index, 0, 0))

    first = 0
    last = cells_x - 1
    edge_call = pl.pallas_call(
        functools.partial(_edge_kernel, planes=cells_x),
        out_shape=(xlo_shape, xhi_shape),
        grid=(1,),
        in_specs=[field_plane(i) for i in (first, 1, last - 1, last)]
        + [field_plane(i) for i in (first, last - 1, last)]
        + [coef_plane(first), coef_plane(last), coef_plane(first), coef_plane(last)]
        + [whole] * 3,
        out_specs=(whole, whole),
    )
    slab = 8
    slabs = cells_y // slab

    def row_slab(index):
        return pl.BlockSpec((comps, cells_x, slab, depth), lambda i: (0, 0, index, 0))

    xlo, xhi, rows = pl.pallas_call(
        _halo_kernel,
        out_shape=(xlo_shape, xhi_shape, rows_shape),
        grid=(1,),
        in_specs=[field_plane(first), field_plane(last), field_plane(last),
                  row_slab(0), row_slab(slabs - 1), row_slab(slabs - 1)],
        out_specs=(whole, whole, whole),
    )(e_field, e_field, h_field, e_field, e_field, h_field)
    xlo, xhi = exchange_x(xlo, xhi)
    keep, drive = coefficients(material, eps_table, sigma_table)
    keep, drive, xlo, xhi = lax.optimization_barrier((keep, drive, xlo, xhi))
    rows = exchange_y(rows, xlo, xhi)
    basis = trig_basis(angle_orders, cells_x, cells_y)
    basis = basis.reshape(2 * angle_count, cells_x, cells_y).transpose(1, 0, 2)
    basis, rows = lax.optimization_barrier((basis, rows))
    elec = e_field
    magn = h_field
    columns = [[], []]
    for number in range(ITERS):
        if number + 1 < ITERS:
            edges = edge_call(
                elec, elec, elec, elec, magn, magn, magn, keep, keep, drive, drive, xlo, xhi, rows
            )
            next_xlo, next_xhi = exchange_x(*edges)
        elec, magn, new_rows, sums = step_call(elec, magn, keep, drive, xlo, xhi, rows, basis)
        if number + 1 < ITERS:
            xlo, xhi = next_xlo, next_xhi
            rows = exchange_y(new_rows, xlo, xhi)
        weight_cos = math.cos(PHASE_STEP * (number + 1))
        weight_sin = math.sin(PHASE_STEP * (number + 1))
        picked = sums[:, 0]
        for comp in range(2):
            cos_p = picked[comp, :angle_count]
            sin_p = picked[comp, angle_count:]
            columns[comp].append((weight_cos * cos_p - weight_sin * sin_p, -weight_sin * cos_p - weight_cos * sin_p))
    stacked = []
    for comp in range(2):
        real = columns[comp][0][0]
        imag = columns[comp][0][1]
        for more_real, more_imag in columns[comp][1:]:
            real = real + more_real
            imag = imag + more_imag
        stacked += [real, imag]
    columns = stacked
    terms = jnp.stack(columns, axis=1)
    owned = angle_count // lax.axis_size("gx")
    scale = 1.0 / math.sqrt(cells_x * lax.axis_size("gx") * cells_y * lax.axis_size("gy"))
    far_field = scatter_sum(terms, "gx", owned)
    far_field = pair_sum(far_field, "gy") * scale
    return (elec, magn, far_field)


def solution(mesh):
    return jax.shard_map(
        local,
        mesh=mesh,
        in_specs=(
            P(None, ("clip", "gx"), "gy", None),
            P(None, ("clip", "gx"), "gy", None),
            P(("clip", "gx"), "gy", None),
            P(),
            P(),
            P(),
        ),
        out_specs=(
            P(None, ("clip", "gx"), "gy", None),
            P(None, ("clip", "gx"), "gy", None),
            P(("clip", "gx"), None),
        ),
        check_vma=False,
    )
```

```python
import functools
import math

import jax
import jax.numpy as jnp
from jax import lax
from jax.experimental import pallas as pl
from jax.experimental.pallas import tpu as pltpu
from jax.sharding import PartitionSpec as P

ITERS = 4


TIME_STEP = 0.5
PHASE_STEP = 0.9


def shifted(value, axis, steps):
    count = lax.axis_size(axis)
    pairs = [(source, (source + steps) % count) for source in range(count)]
    return lax.ppermute(value, axis, pairs)


def _coef_kernel(eps_ref, sigma_ref, mat_ref, keep_out, drive_out):
    planes = mat_ref.shape[0]
    for x in range(planes):
        material = mat_ref[x]
        permit = jnp.zeros(material.shape, jnp.float32)
        conduct = jnp.zeros(material.shape, jnp.float32)
        for label in range(eps_ref.shape[0]):
            hit = material == label
            permit = jnp.where(hit, eps_ref[label], permit)
            conduct = jnp.where(hit, sigma_ref[label], conduct)
        loss = conduct * TIME_STEP / (2.0 * permit)
        keep_out[x] = (1.0 - loss) / (1.0 + loss)
        drive_out[x] = TIME_STEP / (permit * (1.0 + loss))


def coefficients(material, eps_table, sigma_table):
    scalar = pl.BlockSpec(memory_space=pltpu.SMEM)
    whole = pl.BlockSpec(memory_space=pltpu.VMEM)
    out = jax.ShapeDtypeStruct(material.shape, jnp.float32)
    return pl.pallas_call(
        _coef_kernel,
        out_shape=(out, out),
        in_specs=[scalar, scalar, whole],
        out_specs=(whole, whole),
    )(eps_table, sigma_table, material)


def _z_up(f):
    depth = f.shape[-1]
    lane = lax.broadcasted_iota(jnp.int32, f.shape, 1)
    up = pltpu.roll(f, depth - 1, 1)
    return jnp.where(lane == depth - 1, 0.0, up) - f


def _z_down(f):
    lane = lax.broadcasted_iota(jnp.int32, f.shape, 1)
    down = pltpu.roll(f, 1, 1)
    return f - jnp.where(lane == 0, 0.0, down)


def _y_up(f, row):
    cells = f.shape[0]
    index = lax.broadcasted_iota(jnp.int32, f.shape, 0)
    up = pltpu.roll(f, cells - 1, 0)
    return jnp.where(index == cells - 1, row, up) - f


def _y_down(f, row):
    index = lax.broadcasted_iota(jnp.int32, f.shape, 0)
    down = pltpu.roll(f, 1, 0)
    return f - jnp.where(index == 0, row, down)


def _magn_plane(elec, magn, x, planes, xhi_ref, yhi_ref):
    ex = elec(0, x)
    ey = elec(1, x)
    ez = elec(2, x)
    if x + 1 < planes:
        ey_next = elec(1, x + 1)
        ez_next = elec(2, x + 1)
    else:
        ey_next = xhi_ref[0]
        ez_next = xhi_ref[1]
    hx = magn(0, x) - TIME_STEP * (_y_up(ez, yhi_ref[1, x]) - _z_up(ey))
    hy = magn(1, x) - TIME_STEP * (_z_up(ex) - (ez_next - ez))
    hz = magn(2, x) - TIME_STEP * ((ey_next - ey) - _y_up(ex, yhi_ref[0, x]))
    return (ex, ey, ez, hx, hy, hz)


def _magn_before(elec, xlo_ref, c1_ref):
    ex_p = xlo_ref[0]
    ey_p = xlo_ref[1]
    ez_p = xlo_ref[2]
    hy = xlo_ref[3] - TIME_STEP * (_z_up(ex_p) - (elec(2, 0) - ez_p))
    hz = xlo_ref[4] - TIME_STEP * ((elec(1, 0) - ey_p) - _y_up(ex_p, c1_ref[...]))
    return (hy, hz)


def _elec_plane(x, planes, old, hy_prev, hz_prev, ylo_ref, c2_ref, keep, drive):
    ex, ey, ez, hx, hy, hz = old
    if x + 1 < planes:
        ey_m_next = ylo_ref[1, x + 1]
    else:
        ey_m_next = c2_ref[...]
    ex_m = ylo_ref[0, x]
    ey_m = ylo_ref[1, x]
    ez_m = ylo_ref[2, x]
    hx_r = ylo_ref[3, x] - TIME_STEP * ((ez[0:1] - ez_m) - _z_up(ey_m))
    hz_r = ylo_ref[4, x] - TIME_STEP * ((ey_m_next - ey_m) - (ex[0:1] - ex_m))
    ex_new = keep * ex + drive * (_y_down(hz, hz_r) - _z_down(hy))
    ey_new = keep * ey + drive * (_z_down(hx) - (hz - hz_prev))
    ez_new = keep * ez + drive * ((hy - hy_prev) - _y_down(hx, hx_r))
    return (ex_new, ey_new, ez_new)


def _step_kernel(e_ref, h_ref, keep_ref, drive_ref, xlo_ref, xhi_ref, y_ref, basis_ref,
                 e_out, h_out, y_out, g_out):
    c1_ref = y_ref.at[7, 0]
    c2_ref = y_ref.at[8, 0]
    yhi_ref = y_ref.at[5:7]
    planes = e_ref.shape[1]
    cells = e_ref.shape[2]
    elec = lambda comp, x: e_ref[comp, x]
    magn = lambda comp, x: h_ref[comp, x]
    hy_prev, hz_prev = _magn_before(elec, xlo_ref, c1_ref)
    sums = [None, None]
    for x in range(planes):
        old = _magn_plane(elec, magn, x, planes, xhi_ref, yhi_ref)
        ex_new, ey_new, ez_new = _elec_plane(
            x, planes, old, hy_prev, hz_prev, y_ref, c2_ref, keep_ref[x], drive_ref[x]
        )
        hx, hy, hz = old[3:]
        e_out[0, x] = ex_new
        e_out[1, x] = ey_new
        e_out[2, x] = ez_new
        h_out[0, x] = hx
        h_out[1, x] = hy
        h_out[2, x] = hz
        last = slice(cells - 1, cells)
        y_out[0, x] = ex_new[last]
        y_out[1, x] = ey_new[last]
        y_out[2, x] = ez_new[last]
        y_out[3, x] = hx[last]
        y_out[4, x] = hz[last]
        y_out[5, x] = ex_new[0:1]
        y_out[6, x] = ez_new[0:1]
        hy_prev = hy
        hz_prev = hz
        for comp, field in ((0, ex_new), (1, ey_new)):
            part = jnp.dot(basis_ref[x], field, precision=lax.Precision.HIGHEST,
                           preferred_element_type=jnp.float32)
            sums[comp] = part if sums[comp] is None else sums[comp] + part
    depth = e_ref.shape[3]
    for comp in range(2):
        g_out[comp] = sums[comp].T[depth - 3:depth - 2]


def _edge_kernel(e_first, e_second, e_penult, e_last, h_first, h_penult, h_last,
                 keep_first, keep_last, drive_first, drive_last, xlo_ref, xhi_ref, y_ref,
                 xlo_out, xhi_out, *, planes):
    c1_ref = y_ref.at[7, 0]
    c2_ref = y_ref.at[8, 0]
    yhi_ref = y_ref.at[5:7]
    e_blocks = {0: e_first, 1: e_second, planes - 2: e_penult, planes - 1: e_last}
    h_blocks = {0: h_first, planes - 2: h_penult, planes - 1: h_last}
    elec = lambda comp, x: e_blocks[x][comp, 0]
    magn = lambda comp, x: h_blocks[x][comp, 0]
    hy_prev, hz_prev = _magn_before(elec, xlo_ref, c1_ref)
    old = _magn_plane(elec, magn, 0, planes, xhi_ref, yhi_ref)
    ex_new, ey_new, ez_new = _elec_plane(
        0, planes, old, hy_prev, hz_prev, y_ref, c2_ref, keep_first[0], drive_first[0]
    )
    xhi_out[0] = ey_new
    xhi_out[1] = ez_new
    penult = _magn_plane(elec, magn, planes - 2, planes, xhi_ref, yhi_ref)
    old = _magn_plane(elec, magn, planes - 1, planes, xhi_ref, yhi_ref)
    ex_new, ey_new, ez_new = _elec_plane(
        planes - 1, planes, old, penult[4], penult[5], y_ref, c2_ref, keep_last[0], drive_last[0]
    )
    xlo_out[0] = ex_new
    xlo_out[1] = ey_new
    xlo_out[2] = ez_new
    xlo_out[3] = old[4]
    xlo_out[4] = old[5]


def _halo_kernel(e_first, e_last, h_last, e_top, e_bottom, h_bottom, xlo_out, xhi_out, y_out,
                 c1_out, c2_out):
    planes = e_top.shape[1]
    slab = e_top.shape[2]
    last = slice(slab - 1, slab)
    cells = e_first.shape[2]
    c1_out[...] = e_last[0, 0][0:1]
    c2_out[...] = e_first[1, 0][cells - 1:cells]
    for x in range(planes):
        y_out[0, x] = e_bottom[0, x][last]
        y_out[1, x] = e_bottom[1, x][last]
        y_out[2, x] = e_bottom[2, x][last]
        y_out[3, x] = h_bottom[0, x][last]
        y_out[4, x] = h_bottom[2, x][last]
        y_out[5, x] = e_top[0, x][0:1]
        y_out[6, x] = e_top[2, x][0:1]
    xhi_out[0] = e_first[1, 0]
    xhi_out[1] = e_first[2, 0]
    xlo_out[0] = e_last[0, 0]
    xlo_out[1] = e_last[1, 0]
    xlo_out[2] = e_last[2, 0]
    xlo_out[3] = h_last[1, 0]
    xlo_out[4] = h_last[2, 0]


def diagonal(value, step_x, step_y):
    count_x = lax.axis_size("gx")
    count_y = lax.axis_size("gy")
    pairs = []
    for a in range(count_x):
        for b in range(count_y):
            target = ((a + step_x) % count_x) * count_y + (b + step_y) % count_y
            pairs.append((a * count_y + b, target))
    return lax.ppermute(value, ("gx", "gy"), pairs)


def exchange_x(xlo, xhi):
    return (shifted(xlo, "gx", 1), shifted(xhi, "gx", -1))


def exchange_y(rows, xlo, xhi):
    cells = xhi.shape[1]
    corners = jnp.zeros((2,) + rows.shape[1:], rows.dtype)
    corners = corners.at[0, 0].set(xlo[0, 0:1]).at[1, 0].set(xhi[0, cells - 1:cells])
    message = jnp.concatenate([rows, corners])
    if lax.axis_size("gy") == 2:
        return shifted(message, "gy", 1)
    before = shifted(message, "gy", 1)
    after = shifted(message, "gy", -1)
    return jnp.concatenate([before[0:5], after[5:8], before[8:9]])


def trig_basis(angle_orders, cells_x, cells_y):
    size_x = lax.axis_size("gx")
    size_y = lax.axis_size("gy")
    total_x = cells_x * size_x
    total_y = cells_y * size_y
    pos_x = lax.axis_index("gx") * cells_x + jnp.arange(cells_x, dtype=jnp.int32)
    pos_y = lax.axis_index("gy") * cells_y + jnp.arange(cells_y, dtype=jnp.int32)
    order_x = angle_orders[:, 0]
    order_y = angle_orders[:, 1]
    phase_int = (
        order_x[:, None, None] * pos_x[None, :, None] * total_y
        + order_y[:, None, None] * pos_y[None, None, :] * total_x
    ) % (total_x * total_y)
    theta = phase_int.astype(jnp.float32) * (2.0 * math.pi / (total_x * total_y))
    theta = theta.reshape(angle_orders.shape[0], cells_x * cells_y)
    return jnp.concatenate([jnp.cos(theta), jnp.sin(theta)])


def transform(basis, columns):
    return jnp.dot(basis, columns, precision=lax.Precision.HIGHEST, preferred_element_type=jnp.float32)


def flat(plane):
    return plane.reshape(plane.shape[0], -1).T


def scatter_sum(rows, axis, owned):
    count = lax.axis_size(axis)
    index = lax.axis_index(axis)
    if count & (count - 1):
        return lax.psum_scatter(rows, axis, scatter_dimension=0, tiled=True)
    stride = count // 2
    while stride >= 1:
        half = rows.shape[0] // 2
        lower = rows[:half]
        upper = rows[half:]
        high = (index & stride) != 0
        keep = jnp.where(high, upper, lower)
        send = jnp.where(high, lower, upper)
        pairs = [(source, source ^ stride) for source in range(count)]
        rows = keep + lax.ppermute(send, axis, pairs)
        stride //= 2
    return rows


def pair_sum(value, axis):
    count = lax.axis_size(axis)
    if count == 1:
        return value
    if count == 2:
        return value + lax.ppermute(value, axis, [(0, 1), (1, 0)])
    return lax.psum(value, axis)


def local(e_field, h_field, material, eps_table, sigma_table, angle_orders):
    comps, cells_x, cells_y, depth = e_field.shape
    f32 = jnp.float32
    field_shape = jax.ShapeDtypeStruct(e_field.shape, f32)
    xlo_shape = jax.ShapeDtypeStruct((5, cells_y, depth), f32)
    xhi_shape = jax.ShapeDtypeStruct((2, cells_y, depth), f32)
    rows_shape = jax.ShapeDtypeStruct((7, cells_x, 1, depth), f32)
    angle_count = angle_orders.shape[0]
    sums_shape = jax.ShapeDtypeStruct((2, 1, 2 * angle_count), f32)
    step_call = pl.pallas_call(
        _step_kernel, out_shape=(field_shape, field_shape, rows_shape, sums_shape)
    )
    whole = pl.BlockSpec(memory_space=pltpu.VMEM)

    def field_plane(index):
        return pl.BlockSpec((comps, 1, cells_y, depth), lambda i: (0, index, 0, 0))

    def coef_plane(index):
        return pl.BlockSpec((1, cells_y, depth), lambda i: (index, 0, 0))

    first = 0
    last = cells_x - 1
    edge_call = pl.pallas_call(
        functools.partial(_edge_kernel, planes=cells_x),
        out_shape=(xlo_shape, xhi_shape),
        grid=(1,),
        in_specs=[field_plane(i) for i in (first, 1, last - 1, last)]
        + [field_plane(i) for i in (first, last - 1, last)]
        + [coef_plane(first), coef_plane(last), coef_plane(first), coef_plane(last)]
        + [whole] * 3,
        out_specs=(whole, whole),
    )
    slab = 8
    slabs = cells_y // slab

    def row_slab(index):
        return pl.BlockSpec((comps, cells_x, slab, depth), lambda i: (0, 0, index, 0))

    corner_shape = jax.ShapeDtypeStruct((1, depth), f32)
    xlo, xhi, rows, corner_1, corner_2 = pl.pallas_call(
        _halo_kernel,
        out_shape=(xlo_shape, xhi_shape, rows_shape, corner_shape, corner_shape),
        grid=(1,),
        in_specs=[field_plane(first), field_plane(last), field_plane(last),
                  row_slab(0), row_slab(slabs - 1), row_slab(slabs - 1)],
        out_specs=(whole,) * 5,
    )(e_field, e_field, h_field, e_field, e_field, h_field)
    xlo, xhi = exchange_x(xlo, xhi)
    if lax.axis_size("gy") == 2:
        rows = shifted(rows, "gy", 1)
    else:
        rows = jnp.concatenate([shifted(rows[0:5], "gy", 1), shifted(rows[5:7], "gy", -1)])
    corner_1 = diagonal(corner_1, 1, -1)
    corner_2 = diagonal(corner_2, -1, 1)
    keep, drive = coefficients(material, eps_table, sigma_table)
    keep, drive, xlo, xhi = lax.optimization_barrier((keep, drive, xlo, xhi))
    corners = jnp.zeros((2,) + rows.shape[1:], f32)
    corners = corners.at[0, 0].set(corner_1).at[1, 0].set(corner_2)
    rows = jnp.concatenate([rows, corners])
    basis = trig_basis(angle_orders, cells_x, cells_y)
    basis = basis.reshape(2 * angle_count, cells_x, cells_y).transpose(1, 0, 2)
    basis, rows = lax.optimization_barrier((basis, rows))
    elec = e_field
    magn = h_field
    columns = [[], []]
    for number in range(ITERS):
        if number + 1 < ITERS:
            edges = edge_call(
                elec, elec, elec, elec, magn, magn, magn, keep, keep, drive, drive, xlo, xhi, rows
            )
            next_xlo, next_xhi = exchange_x(*edges)
        elec, magn, new_rows, sums = step_call(elec, magn, keep, drive, xlo, xhi, rows, basis)
        if number + 1 < ITERS:
            xlo, xhi = next_xlo, next_xhi
            rows = exchange_y(new_rows, xlo, xhi)
        weight_cos = math.cos(PHASE_STEP * (number + 1))
        weight_sin = math.sin(PHASE_STEP * (number + 1))
        picked = sums[:, 0]
        for comp in range(2):
            cos_p = picked[comp, :angle_count]
            sin_p = picked[comp, angle_count:]
            columns[comp].append((weight_cos * cos_p - weight_sin * sin_p, -weight_sin * cos_p - weight_cos * sin_p))
    stacked = []
    for comp in range(2):
        real = columns[comp][0][0]
        imag = columns[comp][0][1]
        for more_real, more_imag in columns[comp][1:]:
            real = real + more_real
            imag = imag + more_imag
        stacked += [real, imag]
    columns = stacked
    terms = jnp.stack(columns, axis=1)
    owned = angle_count // lax.axis_size("gx")
    scale = 1.0 / math.sqrt(cells_x * lax.axis_size("gx") * cells_y * lax.axis_size("gy"))
    far_field = scatter_sum(terms, "gx", owned)
    far_field = pair_sum(far_field, "gy") * scale
    return (elec, magn, far_field)


def solution(mesh):
    return jax.shard_map(
        local,
        mesh=mesh,
        in_specs=(
            P(None, ("clip", "gx"), "gy", None),
            P(None, ("clip", "gx"), "gy", None),
            P(("clip", "gx"), "gy", None),
            P(),
            P(),
            P(),
        ),
        out_specs=(
            P(None, ("clip", "gx"), "gy", None),
            P(None, ("clip", "gx"), "gy", None),
            P(("clip", "gx"), None),
        ),
        check_vma=False,
    )
```

```python
import functools
import math

import jax
import jax.numpy as jnp
from jax import lax
from jax.experimental import pallas as pl
from jax.experimental.pallas import tpu as pltpu
from jax.sharding import PartitionSpec as P

ITERS = 4


TIME_STEP = 0.5
PHASE_STEP = 0.9


def shifted(value, axis, steps):
    count = lax.axis_size(axis)
    pairs = [(source, (source + steps) % count) for source in range(count)]
    return lax.ppermute(value, axis, pairs)


def _coef_kernel(eps_ref, sigma_ref, mat_ref, keep_out, drive_out):
    planes = mat_ref.shape[0]
    for x in range(planes):
        material = mat_ref[x]
        permit = jnp.zeros(material.shape, jnp.float32)
        conduct = jnp.zeros(material.shape, jnp.float32)
        for label in range(eps_ref.shape[0]):
            hit = material == label
            permit = jnp.where(hit, eps_ref[label], permit)
            conduct = jnp.where(hit, sigma_ref[label], conduct)
        loss = conduct * TIME_STEP / (2.0 * permit)
        keep_out[x] = (1.0 - loss) / (1.0 + loss)
        drive_out[x] = TIME_STEP / (permit * (1.0 + loss))


def coefficients(material, eps_table, sigma_table):
    scalar = pl.BlockSpec(memory_space=pltpu.SMEM)
    whole = pl.BlockSpec(memory_space=pltpu.VMEM)
    out = jax.ShapeDtypeStruct(material.shape, jnp.float32)
    return pl.pallas_call(
        _coef_kernel,
        out_shape=(out, out),
        in_specs=[scalar, scalar, whole],
        out_specs=(whole, whole),
    )(eps_table, sigma_table, material)


def _z_up(f):
    depth = f.shape[-1]
    lane = lax.broadcasted_iota(jnp.int32, f.shape, 1)
    up = pltpu.roll(f, depth - 1, 1)
    return jnp.where(lane == depth - 1, 0.0, up) - f


def _z_down(f):
    lane = lax.broadcasted_iota(jnp.int32, f.shape, 1)
    down = pltpu.roll(f, 1, 1)
    return f - jnp.where(lane == 0, 0.0, down)


def _y_up(f, row):
    cells = f.shape[0]
    index = lax.broadcasted_iota(jnp.int32, f.shape, 0)
    up = pltpu.roll(f, cells - 1, 0)
    return jnp.where(index == cells - 1, row, up) - f


def _y_down(f, row):
    index = lax.broadcasted_iota(jnp.int32, f.shape, 0)
    down = pltpu.roll(f, 1, 0)
    return f - jnp.where(index == 0, row, down)


def _magn_plane(elec, magn, x, planes, xhi_ref, yhi_ref):
    ex = elec(0, x)
    ey = elec(1, x)
    ez = elec(2, x)
    if x + 1 < planes:
        ey_next = elec(1, x + 1)
        ez_next = elec(2, x + 1)
    else:
        ey_next = xhi_ref[0]
        ez_next = xhi_ref[1]
    hx = magn(0, x) - TIME_STEP * (_y_up(ez, yhi_ref[1, x:x + 1]) - _z_up(ey))
    hy = magn(1, x) - TIME_STEP * (_z_up(ex) - (ez_next - ez))
    hz = magn(2, x) - TIME_STEP * ((ey_next - ey) - _y_up(ex, yhi_ref[0, x:x + 1]))
    return (ex, ey, ez, hx, hy, hz)


def _magn_before(elec, xlo_ref, c1_ref):
    ex_p = xlo_ref[0]
    ey_p = xlo_ref[1]
    ez_p = xlo_ref[2]
    hy = xlo_ref[3] - TIME_STEP * (_z_up(ex_p) - (elec(2, 0) - ez_p))
    hz = xlo_ref[4] - TIME_STEP * ((elec(1, 0) - ey_p) - _y_up(ex_p, c1_ref[...]))
    return (hy, hz)


def _elec_plane(x, planes, old, hy_prev, hz_prev, ylo_ref, c2_ref, keep, drive):
    ex, ey, ez, hx, hy, hz = old
    if x + 1 < planes:
        ey_m_next = ylo_ref[1, x + 1:x + 2]
    else:
        ey_m_next = c2_ref[...]
    ex_m = ylo_ref[0, x:x + 1]
    ey_m = ylo_ref[1, x:x + 1]
    ez_m = ylo_ref[2, x:x + 1]
    hx_r = ylo_ref[3, x:x + 1] - TIME_STEP * ((ez[0:1] - ez_m) - _z_up(ey_m))
    hz_r = ylo_ref[4, x:x + 1] - TIME_STEP * ((ey_m_next - ey_m) - (ex[0:1] - ex_m))
    ex_new = keep * ex + drive * (_y_down(hz, hz_r) - _z_down(hy))
    ey_new = keep * ey + drive * (_z_down(hx) - (hz - hz_prev))
    ez_new = keep * ez + drive * ((hy - hy_prev) - _y_down(hx, hx_r))
    return (ex_new, ey_new, ez_new)


def _step_kernel(e_ref, h_ref, keep_ref, drive_ref, xlo_ref, xhi_ref, y_ref, basis_ref,
                 e_out, h_out, y_out, g_out):
    c1_ref = y_ref.at[7, 0:1]
    c2_ref = y_ref.at[8, 0:1]
    yhi_ref = y_ref.at[5:7]
    planes = e_ref.shape[1]
    cells = e_ref.shape[2]
    elec = lambda comp, x: e_ref[comp, x]
    magn = lambda comp, x: h_ref[comp, x]
    hy_prev, hz_prev = _magn_before(elec, xlo_ref, c1_ref)
    sums = [None, None]
    for x in range(planes):
        old = _magn_plane(elec, magn, x, planes, xhi_ref, yhi_ref)
        ex_new, ey_new, ez_new = _elec_plane(
            x, planes, old, hy_prev, hz_prev, y_ref, c2_ref, keep_ref[x], drive_ref[x]
        )
        hx, hy, hz = old[3:]
        e_out[0, x] = ex_new
        e_out[1, x] = ey_new
        e_out[2, x] = ez_new
        h_out[0, x] = hx
        h_out[1, x] = hy
        h_out[2, x] = hz
        last = slice(cells - 1, cells)
        y_out[0, x:x + 1] = ex_new[last]
        y_out[1, x:x + 1] = ey_new[last]
        y_out[2, x:x + 1] = ez_new[last]
        y_out[3, x:x + 1] = hx[last]
        y_out[4, x:x + 1] = hz[last]
        y_out[5, x:x + 1] = ex_new[0:1]
        y_out[6, x:x + 1] = ez_new[0:1]
        hy_prev = hy
        hz_prev = hz
        for comp, field in ((0, ex_new), (1, ey_new)):
            part = jnp.dot(basis_ref[x], field, precision=lax.Precision.HIGHEST,
                           preferred_element_type=jnp.float32)
            sums[comp] = part if sums[comp] is None else sums[comp] + part
    depth = e_ref.shape[3]
    for comp in range(2):
        g_out[comp] = sums[comp].T[depth - 3:depth - 2]


def _edge_kernel(e_first, e_second, e_penult, e_last, h_first, h_penult, h_last,
                 keep_first, keep_last, drive_first, drive_last, xlo_ref, xhi_ref, y_ref,
                 xlo_out, xhi_out, *, planes):
    c1_ref = y_ref.at[7, 0:1]
    c2_ref = y_ref.at[8, 0:1]
    yhi_ref = y_ref.at[5:7]
    e_blocks = {0: e_first, 1: e_second, planes - 2: e_penult, planes - 1: e_last}
    h_blocks = {0: h_first, planes - 2: h_penult, planes - 1: h_last}
    elec = lambda comp, x: e_blocks[x][comp, 0]
    magn = lambda comp, x: h_blocks[x][comp, 0]
    hy_prev, hz_prev = _magn_before(elec, xlo_ref, c1_ref)
    old = _magn_plane(elec, magn, 0, planes, xhi_ref, yhi_ref)
    ex_new, ey_new, ez_new = _elec_plane(
        0, planes, old, hy_prev, hz_prev, y_ref, c2_ref, keep_first[0], drive_first[0]
    )
    xhi_out[0] = ey_new
    xhi_out[1] = ez_new
    penult = _magn_plane(elec, magn, planes - 2, planes, xhi_ref, yhi_ref)
    old = _magn_plane(elec, magn, planes - 1, planes, xhi_ref, yhi_ref)
    ex_new, ey_new, ez_new = _elec_plane(
        planes - 1, planes, old, penult[4], penult[5], y_ref, c2_ref, keep_last[0], drive_last[0]
    )
    xlo_out[0] = ex_new
    xlo_out[1] = ey_new
    xlo_out[2] = ez_new
    xlo_out[3] = old[4]
    xlo_out[4] = old[5]


def _halo_kernel(e_first, e_last, h_last, e_top, e_bottom, h_bottom, xlo_out, xhi_out, y_out):
    planes = e_top.shape[1]
    slab = e_top.shape[2]
    last = slice(slab - 1, slab)
    for x in range(planes):
        y_out[0, x:x + 1] = e_bottom[0, x][last]
        y_out[1, x:x + 1] = e_bottom[1, x][last]
        y_out[2, x:x + 1] = e_bottom[2, x][last]
        y_out[3, x:x + 1] = h_bottom[0, x][last]
        y_out[4, x:x + 1] = h_bottom[2, x][last]
        y_out[5, x:x + 1] = e_top[0, x][0:1]
        y_out[6, x:x + 1] = e_top[2, x][0:1]
    xhi_out[0] = e_first[1, 0]
    xhi_out[1] = e_first[2, 0]
    xlo_out[0] = e_last[0, 0]
    xlo_out[1] = e_last[1, 0]
    xlo_out[2] = e_last[2, 0]
    xlo_out[3] = h_last[1, 0]
    xlo_out[4] = h_last[2, 0]


def exchange_x(xlo, xhi):
    return (shifted(xlo, "gx", 1), shifted(xhi, "gx", -1))


def exchange_y(rows, xlo, xhi):
    cells = xhi.shape[1]
    corners = jnp.zeros((2,) + rows.shape[1:], rows.dtype)
    corners = corners.at[0, 0:1].set(xlo[0, 0:1]).at[1, 0:1].set(xhi[0, cells - 1:cells])
    message = jnp.concatenate([rows, corners])
    if lax.axis_size("gy") == 2:
        return shifted(message, "gy", 1)
    before = shifted(message, "gy", 1)
    after = shifted(message, "gy", -1)
    return jnp.concatenate([before[0:5], after[5:8], before[8:9]])


def trig_basis(angle_orders, cells_x, cells_y):
    size_x = lax.axis_size("gx")
    size_y = lax.axis_size("gy")
    total_x = cells_x * size_x
    total_y = cells_y * size_y
    pos_x = lax.axis_index("gx") * cells_x + jnp.arange(cells_x, dtype=jnp.int32)
    pos_y = lax.axis_index("gy") * cells_y + jnp.arange(cells_y, dtype=jnp.int32)
    order_x = angle_orders[:, 0]
    order_y = angle_orders[:, 1]
    phase_int = (
        order_x[:, None, None] * pos_x[None, :, None] * total_y
        + order_y[:, None, None] * pos_y[None, None, :] * total_x
    ) % (total_x * total_y)
    theta = phase_int.astype(jnp.float32) * (2.0 * math.pi / (total_x * total_y))
    theta = theta.reshape(angle_orders.shape[0], cells_x * cells_y)
    return jnp.concatenate([jnp.cos(theta), jnp.sin(theta)])


def transform(basis, columns):
    return jnp.dot(basis, columns, precision=lax.Precision.HIGHEST, preferred_element_type=jnp.float32)


def flat(plane):
    return plane.reshape(plane.shape[0], -1).T


def scatter_sum(rows, axis, owned):
    count = lax.axis_size(axis)
    index = lax.axis_index(axis)
    if count & (count - 1):
        return lax.psum_scatter(rows, axis, scatter_dimension=0, tiled=True)
    stride = count // 2
    while stride >= 1:
        half = rows.shape[0] // 2
        lower = rows[:half]
        upper = rows[half:]
        high = (index & stride) != 0
        keep = jnp.where(high, upper, lower)
        send = jnp.where(high, lower, upper)
        pairs = [(source, source ^ stride) for source in range(count)]
        rows = keep + lax.ppermute(send, axis, pairs)
        stride //= 2
    return rows


def pair_sum(value, axis):
    count = lax.axis_size(axis)
    if count == 1:
        return value
    if count == 2:
        return value + lax.ppermute(value, axis, [(0, 1), (1, 0)])
    return lax.psum(value, axis)


def local(e_field, h_field, material, eps_table, sigma_table, angle_orders):
    comps, cells_x, cells_y, depth = e_field.shape
    f32 = jnp.float32
    field_shape = jax.ShapeDtypeStruct(e_field.shape, f32)
    xlo_shape = jax.ShapeDtypeStruct((5, cells_y, depth), f32)
    xhi_shape = jax.ShapeDtypeStruct((2, cells_y, depth), f32)
    rows_shape = jax.ShapeDtypeStruct((7, cells_x, depth), f32)
    angle_count = angle_orders.shape[0]
    sums_shape = jax.ShapeDtypeStruct((2, 1, 2 * angle_count), f32)
    step_call = pl.pallas_call(
        _step_kernel, out_shape=(field_shape, field_shape, rows_shape, sums_shape)
    )
    whole = pl.BlockSpec(memory_space=pltpu.VMEM)

    def field_plane(index):
        return pl.BlockSpec((comps, 1, cells_y, depth), lambda i: (0, index, 0, 0))

    def coef_plane(index):
        return pl.BlockSpec((1, cells_y, depth), lambda i: (index, 0, 0))

    first = 0
    last = cells_x - 1
    edge_call = pl.pallas_call(
        functools.partial(_edge_kernel, planes=cells_x),
        out_shape=(xlo_shape, xhi_shape),
        grid=(1,),
        in_specs=[field_plane(i) for i in (first, 1, last - 1, last)]
        + [field_plane(i) for i in (first, last - 1, last)]
        + [coef_plane(first), coef_plane(last), coef_plane(first), coef_plane(last)]
        + [whole] * 3,
        out_specs=(whole, whole),
    )
    slab = 8
    slabs = cells_y // slab

    def row_slab(index):
        return pl.BlockSpec((comps, cells_x, slab, depth), lambda i: (0, 0, index, 0))

    xlo, xhi, rows = pl.pallas_call(
        _halo_kernel,
        out_shape=(xlo_shape, xhi_shape, rows_shape),
        grid=(1,),
        in_specs=[field_plane(first), field_plane(last), field_plane(last),
                  row_slab(0), row_slab(slabs - 1), row_slab(slabs - 1)],
        out_specs=(whole, whole, whole),
    )(e_field, e_field, h_field, e_field, e_field, h_field)
    xlo, xhi = exchange_x(xlo, xhi)
    keep, drive = coefficients(material, eps_table, sigma_table)
    keep, drive, xlo, xhi = lax.optimization_barrier((keep, drive, xlo, xhi))
    rows = exchange_y(rows, xlo, xhi)
    basis = trig_basis(angle_orders, cells_x, cells_y)
    basis = basis.reshape(2 * angle_count, cells_x, cells_y).transpose(1, 0, 2)
    basis, rows = lax.optimization_barrier((basis, rows))
    elec = e_field
    magn = h_field
    columns = [[], []]
    for number in range(ITERS):
        if number + 1 < ITERS:
            edges = edge_call(
                elec, elec, elec, elec, magn, magn, magn, keep, keep, drive, drive, xlo, xhi, rows
            )
            next_xlo, next_xhi = exchange_x(*edges)
        elec, magn, new_rows, sums = step_call(elec, magn, keep, drive, xlo, xhi, rows, basis)
        if number + 1 < ITERS:
            xlo, xhi = next_xlo, next_xhi
            rows = exchange_y(new_rows, xlo, xhi)
        weight_cos = math.cos(PHASE_STEP * (number + 1))
        weight_sin = math.sin(PHASE_STEP * (number + 1))
        picked = sums[:, 0]
        for comp in range(2):
            cos_p = picked[comp, :angle_count]
            sin_p = picked[comp, angle_count:]
            columns[comp].append((weight_cos * cos_p - weight_sin * sin_p, -weight_sin * cos_p - weight_cos * sin_p))
    stacked = []
    for comp in range(2):
        real = columns[comp][0][0]
        imag = columns[comp][0][1]
        for more_real, more_imag in columns[comp][1:]:
            real = real + more_real
            imag = imag + more_imag
        stacked += [real, imag]
    columns = stacked
    terms = jnp.stack(columns, axis=1)
    owned = angle_count // lax.axis_size("gx")
    scale = 1.0 / math.sqrt(cells_x * lax.axis_size("gx") * cells_y * lax.axis_size("gy"))
    far_field = scatter_sum(terms, "gx", owned)
    far_field = pair_sum(far_field, "gy") * scale
    return (elec, magn, far_field)


def solution(mesh):
    return jax.shard_map(
        local,
        mesh=mesh,
        in_specs=(
            P(None, ("clip", "gx"), "gy", None),
            P(None, ("clip", "gx"), "gy", None),
            P(("clip", "gx"), "gy", None),
            P(),
            P(),
            P(),
        ),
        out_specs=(
            P(None, ("clip", "gx"), "gy", None),
            P(None, ("clip", "gx"), "gy", None),
            P(("clip", "gx"), None),
        ),
        check_vma=False,
    )
```

```python
import functools
import math

import jax
import jax.numpy as jnp
from jax import lax
from jax.experimental import pallas as pl
from jax.experimental.pallas import tpu as pltpu
from jax.sharding import PartitionSpec as P

ITERS = 4


TIME_STEP = 0.5
PHASE_STEP = 0.9


def shifted(value, axis, steps):
    count = lax.axis_size(axis)
    pairs = [(source, (source + steps) % count) for source in range(count)]
    return lax.ppermute(value, axis, pairs)


def _coef_kernel(eps_ref, sigma_ref, mat_ref, keep_out, drive_out):
    planes = mat_ref.shape[0]
    for x in range(planes):
        material = mat_ref[x]
        permit = jnp.zeros(material.shape, jnp.float32)
        conduct = jnp.zeros(material.shape, jnp.float32)
        for label in range(eps_ref.shape[0]):
            hit = material == label
            permit = jnp.where(hit, eps_ref[label], permit)
            conduct = jnp.where(hit, sigma_ref[label], conduct)
        loss = conduct * TIME_STEP / (2.0 * permit)
        keep_out[x] = (1.0 - loss) / (1.0 + loss)
        drive_out[x] = TIME_STEP / (permit * (1.0 + loss))


def coefficients(material, eps_table, sigma_table):
    scalar = pl.BlockSpec(memory_space=pltpu.SMEM)
    whole = pl.BlockSpec(memory_space=pltpu.VMEM)
    out = jax.ShapeDtypeStruct(material.shape, jnp.float32)
    return pl.pallas_call(
        _coef_kernel,
        out_shape=(out, out),
        in_specs=[scalar, scalar, whole],
        out_specs=(whole, whole),
    )(eps_table, sigma_table, material)


def _z_up(f):
    depth = f.shape[-1]
    lane = lax.broadcasted_iota(jnp.int32, f.shape, 1)
    up = pltpu.roll(f, depth - 1, 1)
    return jnp.where(lane == depth - 1, 0.0, up) - f


def _z_down(f):
    lane = lax.broadcasted_iota(jnp.int32, f.shape, 1)
    down = pltpu.roll(f, 1, 1)
    return f - jnp.where(lane == 0, 0.0, down)


def _y_up(f, row):
    cells = f.shape[0]
    index = lax.broadcasted_iota(jnp.int32, f.shape, 0)
    up = pltpu.roll(f, cells - 1, 0)
    return jnp.where(index == cells - 1, row, up) - f


def _y_down(f, row):
    index = lax.broadcasted_iota(jnp.int32, f.shape, 0)
    down = pltpu.roll(f, 1, 0)
    return f - jnp.where(index == 0, row, down)


def _magn_plane(elec, magn, x, planes, xhi_ref, yhi_ref):
    ex = elec(0, x)
    ey = elec(1, x)
    ez = elec(2, x)
    if x + 1 < planes:
        ey_next = elec(1, x + 1)
        ez_next = elec(2, x + 1)
    else:
        ey_next = xhi_ref[0]
        ez_next = xhi_ref[1]
    hx = magn(0, x) - TIME_STEP * (_y_up(ez, yhi_ref[1, x:x + 1]) - _z_up(ey))
    hy = magn(1, x) - TIME_STEP * (_z_up(ex) - (ez_next - ez))
    hz = magn(2, x) - TIME_STEP * ((ey_next - ey) - _y_up(ex, yhi_ref[0, x:x + 1]))
    return (ex, ey, ez, hx, hy, hz)


def _magn_before(elec, xlo_ref, c1_ref):
    ex_p = xlo_ref[0]
    ey_p = xlo_ref[1]
    ez_p = xlo_ref[2]
    hy = xlo_ref[3] - TIME_STEP * (_z_up(ex_p) - (elec(2, 0) - ez_p))
    hz = xlo_ref[4] - TIME_STEP * ((elec(1, 0) - ey_p) - _y_up(ex_p, c1_ref[...]))
    return (hy, hz)


def _elec_plane(x, planes, old, hy_prev, hz_prev, ylo_ref, c2_ref, keep, drive):
    ex, ey, ez, hx, hy, hz = old
    if x + 1 < planes:
        ey_m_next = ylo_ref[1, x + 1:x + 2]
    else:
        ey_m_next = c2_ref[...]
    ex_m = ylo_ref[0, x:x + 1]
    ey_m = ylo_ref[1, x:x + 1]
    ez_m = ylo_ref[2, x:x + 1]
    hx_r = ylo_ref[3, x:x + 1] - TIME_STEP * ((ez[0:1] - ez_m) - _z_up(ey_m))
    hz_r = ylo_ref[4, x:x + 1] - TIME_STEP * ((ey_m_next - ey_m) - (ex[0:1] - ex_m))
    ex_new = keep * ex + drive * (_y_down(hz, hz_r) - _z_down(hy))
    ey_new = keep * ey + drive * (_z_down(hx) - (hz - hz_prev))
    ez_new = keep * ez + drive * ((hy - hy_prev) - _y_down(hx, hx_r))
    return (ex_new, ey_new, ez_new)


def _step_kernel(e_ref, h_ref, keep_ref, drive_ref, xlo_ref, xhi_ref, y_ref, basis_ref,
                 e_out, h_out, y_out, g_out):
    c1_ref = y_ref.at[7, 0:1]
    c2_ref = y_ref.at[8, 0:1]
    yhi_ref = y_ref.at[5:7]
    planes = e_ref.shape[1]
    cells = e_ref.shape[2]
    elec = lambda comp, x: e_ref[comp, x]
    magn = lambda comp, x: h_ref[comp, x]
    hy_prev, hz_prev = _magn_before(elec, xlo_ref, c1_ref)
    sums = [None, None]
    pending = []
    for x in range(planes):
        old = _magn_plane(elec, magn, x, planes, xhi_ref, yhi_ref)
        ex_new, ey_new, ez_new = _elec_plane(
            x, planes, old, hy_prev, hz_prev, y_ref, c2_ref, keep_ref[x], drive_ref[x]
        )
        hx, hy, hz = old[3:]
        e_out[0, x] = ex_new
        e_out[1, x] = ey_new
        e_out[2, x] = ez_new
        h_out[0, x] = hx
        h_out[1, x] = hy
        h_out[2, x] = hz
        last = slice(cells - 1, cells)
        y_out[0, x:x + 1] = ex_new[last]
        y_out[1, x:x + 1] = ey_new[last]
        y_out[2, x:x + 1] = ez_new[last]
        y_out[3, x:x + 1] = hx[last]
        y_out[4, x:x + 1] = hz[last]
        y_out[5, x:x + 1] = ex_new[0:1]
        y_out[6, x:x + 1] = ez_new[0:1]
        hy_prev = hy
        hz_prev = hz
        group = basis_ref.shape[2] // cells
        pending.append((ex_new, ey_new))
        if len(pending) == group:
            for comp in range(2):
                fields = [planes_done[comp] for planes_done in pending]
                stacked = fields[0] if group == 1 else jnp.concatenate(fields, axis=0)
                part = jnp.dot(basis_ref[x // group], stacked, precision=lax.Precision.HIGHEST,
                               preferred_element_type=jnp.float32)
                sums[comp] = part if sums[comp] is None else sums[comp] + part
            pending = []
    depth = e_ref.shape[3]
    for comp in range(2):
        g_out[comp] = sums[comp].T[depth - 3:depth - 2]


def _edge_kernel(e_first, e_second, e_penult, e_last, h_first, h_penult, h_last,
                 keep_first, keep_last, drive_first, drive_last, xlo_ref, xhi_ref, y_ref,
                 xlo_out, xhi_out, *, planes):
    c1_ref = y_ref.at[7, 0:1]
    c2_ref = y_ref.at[8, 0:1]
    yhi_ref = y_ref.at[5:7]
    e_blocks = {0: e_first, 1: e_second, planes - 2: e_penult, planes - 1: e_last}
    h_blocks = {0: h_first, planes - 2: h_penult, planes - 1: h_last}
    elec = lambda comp, x: e_blocks[x][comp, 0]
    magn = lambda comp, x: h_blocks[x][comp, 0]
    hy_prev, hz_prev = _magn_before(elec, xlo_ref, c1_ref)
    old = _magn_plane(elec, magn, 0, planes, xhi_ref, yhi_ref)
    ex_new, ey_new, ez_new = _elec_plane(
        0, planes, old, hy_prev, hz_prev, y_ref, c2_ref, keep_first[0], drive_first[0]
    )
    xhi_out[0] = ey_new
    xhi_out[1] = ez_new
    penult = _magn_plane(elec, magn, planes - 2, planes, xhi_ref, yhi_ref)
    old = _magn_plane(elec, magn, planes - 1, planes, xhi_ref, yhi_ref)
    ex_new, ey_new, ez_new = _elec_plane(
        planes - 1, planes, old, penult[4], penult[5], y_ref, c2_ref, keep_last[0], drive_last[0]
    )
    xlo_out[0] = ex_new
    xlo_out[1] = ey_new
    xlo_out[2] = ez_new
    xlo_out[3] = old[4]
    xlo_out[4] = old[5]


def _halo_kernel(e_first, e_last, h_last, e_top, e_bottom, h_bottom, xlo_out, xhi_out, y_out):
    planes = e_top.shape[1]
    slab = e_top.shape[2]
    last = slice(slab - 1, slab)
    for x in range(planes):
        y_out[0, x:x + 1] = e_bottom[0, x][last]
        y_out[1, x:x + 1] = e_bottom[1, x][last]
        y_out[2, x:x + 1] = e_bottom[2, x][last]
        y_out[3, x:x + 1] = h_bottom[0, x][last]
        y_out[4, x:x + 1] = h_bottom[2, x][last]
        y_out[5, x:x + 1] = e_top[0, x][0:1]
        y_out[6, x:x + 1] = e_top[2, x][0:1]
    xhi_out[0] = e_first[1, 0]
    xhi_out[1] = e_first[2, 0]
    xlo_out[0] = e_last[0, 0]
    xlo_out[1] = e_last[1, 0]
    xlo_out[2] = e_last[2, 0]
    xlo_out[3] = h_last[1, 0]
    xlo_out[4] = h_last[2, 0]


def exchange_x(xlo, xhi):
    return (shifted(xlo, "gx", 1), shifted(xhi, "gx", -1))


def exchange_y(rows, xlo, xhi):
    cells = xhi.shape[1]
    corners = jnp.zeros((2,) + rows.shape[1:], rows.dtype)
    corners = corners.at[0, 0:1].set(xlo[0, 0:1]).at[1, 0:1].set(xhi[0, cells - 1:cells])
    message = jnp.concatenate([rows, corners])
    if lax.axis_size("gy") == 2:
        return shifted(message, "gy", 1)
    before = shifted(message, "gy", 1)
    after = shifted(message, "gy", -1)
    return jnp.concatenate([before[0:5], after[5:8], before[8:9]])


def trig_basis(angle_orders, cells_x, cells_y):
    size_x = lax.axis_size("gx")
    size_y = lax.axis_size("gy")
    total_x = cells_x * size_x
    total_y = cells_y * size_y
    pos_x = lax.axis_index("gx") * cells_x + jnp.arange(cells_x, dtype=jnp.int32)
    pos_y = lax.axis_index("gy") * cells_y + jnp.arange(cells_y, dtype=jnp.int32)
    order_x = angle_orders[:, 0]
    order_y = angle_orders[:, 1]
    phase_int = (
        order_x[:, None, None] * pos_x[None, :, None] * total_y
        + order_y[:, None, None] * pos_y[None, None, :] * total_x
    ) % (total_x * total_y)
    theta = phase_int.astype(jnp.float32) * (2.0 * math.pi / (total_x * total_y))
    theta = theta.reshape(angle_orders.shape[0], cells_x * cells_y)
    return jnp.concatenate([jnp.cos(theta), jnp.sin(theta)])


def transform(basis, columns):
    return jnp.dot(basis, columns, precision=lax.Precision.HIGHEST, preferred_element_type=jnp.float32)


def flat(plane):
    return plane.reshape(plane.shape[0], -1).T


def scatter_sum(rows, axis, owned):
    count = lax.axis_size(axis)
    index = lax.axis_index(axis)
    if count & (count - 1):
        return lax.psum_scatter(rows, axis, scatter_dimension=0, tiled=True)
    stride = count // 2
    while stride >= 1:
        half = rows.shape[0] // 2
        lower = rows[:half]
        upper = rows[half:]
        high = (index & stride) != 0
        keep = jnp.where(high, upper, lower)
        send = jnp.where(high, lower, upper)
        pairs = [(source, source ^ stride) for source in range(count)]
        rows = keep + lax.ppermute(send, axis, pairs)
        stride //= 2
    return rows


def pair_sum(value, axis):
    count = lax.axis_size(axis)
    if count == 1:
        return value
    if count == 2:
        return value + lax.ppermute(value, axis, [(0, 1), (1, 0)])
    return lax.psum(value, axis)


def local(e_field, h_field, material, eps_table, sigma_table, angle_orders):
    comps, cells_x, cells_y, depth = e_field.shape
    f32 = jnp.float32
    field_shape = jax.ShapeDtypeStruct(e_field.shape, f32)
    xlo_shape = jax.ShapeDtypeStruct((5, cells_y, depth), f32)
    xhi_shape = jax.ShapeDtypeStruct((2, cells_y, depth), f32)
    rows_shape = jax.ShapeDtypeStruct((7, cells_x, depth), f32)
    angle_count = angle_orders.shape[0]
    sums_shape = jax.ShapeDtypeStruct((2, 1, 2 * angle_count), f32)
    step_call = pl.pallas_call(
        _step_kernel, out_shape=(field_shape, field_shape, rows_shape, sums_shape)
    )
    whole = pl.BlockSpec(memory_space=pltpu.VMEM)

    def field_plane(index):
        return pl.BlockSpec((comps, 1, cells_y, depth), lambda i: (0, index, 0, 0))

    def coef_plane(index):
        return pl.BlockSpec((1, cells_y, depth), lambda i: (index, 0, 0))

    first = 0
    last = cells_x - 1
    edge_call = pl.pallas_call(
        functools.partial(_edge_kernel, planes=cells_x),
        out_shape=(xlo_shape, xhi_shape),
        grid=(1,),
        in_specs=[field_plane(i) for i in (first, 1, last - 1, last)]
        + [field_plane(i) for i in (first, last - 1, last)]
        + [coef_plane(first), coef_plane(last), coef_plane(first), coef_plane(last)]
        + [whole] * 3,
        out_specs=(whole, whole),
    )
    slab = 8
    slabs = cells_y // slab

    def row_slab(index):
        return pl.BlockSpec((comps, cells_x, slab, depth), lambda i: (0, 0, index, 0))

    xlo, xhi, rows = pl.pallas_call(
        _halo_kernel,
        out_shape=(xlo_shape, xhi_shape, rows_shape),
        grid=(1,),
        in_specs=[field_plane(first), field_plane(last), field_plane(last),
                  row_slab(0), row_slab(slabs - 1), row_slab(slabs - 1)],
        out_specs=(whole, whole, whole),
    )(e_field, e_field, h_field, e_field, e_field, h_field)
    xlo, xhi = exchange_x(xlo, xhi)
    keep, drive = coefficients(material, eps_table, sigma_table)
    keep, drive, xlo, xhi = lax.optimization_barrier((keep, drive, xlo, xhi))
    rows = exchange_y(rows, xlo, xhi)
    basis = trig_basis(angle_orders, cells_x, cells_y)
    group = 2 if cells_x % 2 == 0 else 1
    basis = basis.reshape(2 * angle_count, cells_x // group, group * cells_y).transpose(1, 0, 2)
    basis, rows = lax.optimization_barrier((basis, rows))
    elec = e_field
    magn = h_field
    columns = [[], []]
    for number in range(ITERS):
        if number + 1 < ITERS:
            edges = edge_call(
                elec, elec, elec, elec, magn, magn, magn, keep, keep, drive, drive, xlo, xhi, rows
            )
            next_xlo, next_xhi = exchange_x(*edges)
        elec, magn, new_rows, sums = step_call(elec, magn, keep, drive, xlo, xhi, rows, basis)
        if number + 1 < ITERS:
            xlo, xhi = next_xlo, next_xhi
            rows = exchange_y(new_rows, xlo, xhi)
        weight_cos = math.cos(PHASE_STEP * (number + 1))
        weight_sin = math.sin(PHASE_STEP * (number + 1))
        picked = sums[:, 0]
        for comp in range(2):
            cos_p = picked[comp, :angle_count]
            sin_p = picked[comp, angle_count:]
            columns[comp].append((weight_cos * cos_p - weight_sin * sin_p, -weight_sin * cos_p - weight_cos * sin_p))
    stacked = []
    for comp in range(2):
        real = columns[comp][0][0]
        imag = columns[comp][0][1]
        for more_real, more_imag in columns[comp][1:]:
            real = real + more_real
            imag = imag + more_imag
        stacked += [real, imag]
    columns = stacked
    terms = jnp.stack(columns, axis=1)
    owned = angle_count // lax.axis_size("gx")
    scale = 1.0 / math.sqrt(cells_x * lax.axis_size("gx") * cells_y * lax.axis_size("gy"))
    far_field = scatter_sum(terms, "gx", owned)
    far_field = pair_sum(far_field, "gy") * scale
    return (elec, magn, far_field)


def solution(mesh):
    return jax.shard_map(
        local,
        mesh=mesh,
        in_specs=(
            P(None, ("clip", "gx"), "gy", None),
            P(None, ("clip", "gx"), "gy", None),
            P(("clip", "gx"), "gy", None),
            P(),
            P(),
            P(),
        ),
        out_specs=(
            P(None, ("clip", "gx"), "gy", None),
            P(None, ("clip", "gx"), "gy", None),
            P(("clip", "gx"), None),
        ),
        check_vma=False,
    )
```

```python
import functools
import math

import jax
import jax.numpy as jnp
from jax import lax
from jax.experimental import pallas as pl
from jax.experimental.pallas import tpu as pltpu
from jax.sharding import PartitionSpec as P

ITERS = 4


TIME_STEP = 0.5
PHASE_STEP = 0.9


def shifted(value, axis, steps):
    count = lax.axis_size(axis)
    pairs = [(source, (source + steps) % count) for source in range(count)]
    return lax.ppermute(value, axis, pairs)


def _coef_kernel(eps_ref, sigma_ref, mat_ref, keep_out, drive_out):
    planes = mat_ref.shape[0]
    for x in range(planes):
        material = mat_ref[x]
        permit = jnp.zeros(material.shape, jnp.float32)
        conduct = jnp.zeros(material.shape, jnp.float32)
        for label in range(eps_ref.shape[0]):
            hit = material == label
            permit = jnp.where(hit, eps_ref[label], permit)
            conduct = jnp.where(hit, sigma_ref[label], conduct)
        loss = conduct * TIME_STEP / (2.0 * permit)
        keep_out[x] = (1.0 - loss) / (1.0 + loss)
        drive_out[x] = TIME_STEP / (permit * (1.0 + loss))


def coefficients(material, eps_table, sigma_table):
    scalar = pl.BlockSpec(memory_space=pltpu.SMEM)
    whole = pl.BlockSpec(memory_space=pltpu.VMEM)
    out = jax.ShapeDtypeStruct(material.shape, jnp.float32)
    return pl.pallas_call(
        _coef_kernel,
        out_shape=(out, out),
        in_specs=[scalar, scalar, whole],
        out_specs=(whole, whole),
    )(eps_table, sigma_table, material)


def _z_up(f):
    depth = f.shape[-1]
    lane = lax.broadcasted_iota(jnp.int32, f.shape, 1)
    up = pltpu.roll(f, depth - 1, 1)
    return jnp.where(lane == depth - 1, 0.0, up) - f


def _z_down(f):
    lane = lax.broadcasted_iota(jnp.int32, f.shape, 1)
    down = pltpu.roll(f, 1, 1)
    return f - jnp.where(lane == 0, 0.0, down)


def _y_up(f, row):
    cells = f.shape[0]
    index = lax.broadcasted_iota(jnp.int32, f.shape, 0)
    up = pltpu.roll(f, cells - 1, 0)
    return jnp.where(index == cells - 1, row, up) - f


def _y_down(f, row):
    index = lax.broadcasted_iota(jnp.int32, f.shape, 0)
    down = pltpu.roll(f, 1, 0)
    return f - jnp.where(index == 0, row, down)


def _magn_plane(elec, magn, x, planes, xhi_ref, yhi_ref):
    ex = elec(0, x)
    ey = elec(1, x)
    ez = elec(2, x)
    if x + 1 < planes:
        ey_next = elec(1, x + 1)
        ez_next = elec(2, x + 1)
    else:
        ey_next = xhi_ref[0]
        ez_next = xhi_ref[1]
    hx = magn(0, x) - TIME_STEP * (_y_up(ez, yhi_ref[1, x:x + 1]) - _z_up(ey))
    hy = magn(1, x) - TIME_STEP * (_z_up(ex) - (ez_next - ez))
    hz = magn(2, x) - TIME_STEP * ((ey_next - ey) - _y_up(ex, yhi_ref[0, x:x + 1]))
    return (ex, ey, ez, hx, hy, hz)


def _magn_before(elec, xlo_ref, c1_ref):
    ex_p = xlo_ref[0]
    ey_p = xlo_ref[1]
    ez_p = xlo_ref[2]
    hy = xlo_ref[3] - TIME_STEP * (_z_up(ex_p) - (elec(2, 0) - ez_p))
    hz = xlo_ref[4] - TIME_STEP * ((elec(1, 0) - ey_p) - _y_up(ex_p, c1_ref[...]))
    return (hy, hz)


def _elec_plane(x, planes, old, hy_prev, hz_prev, ylo_ref, c2_ref, keep, drive):
    ex, ey, ez, hx, hy, hz = old
    if x + 1 < planes:
        ey_m_next = ylo_ref[1, x + 1:x + 2]
    else:
        ey_m_next = c2_ref[...]
    ex_m = ylo_ref[0, x:x + 1]
    ey_m = ylo_ref[1, x:x + 1]
    ez_m = ylo_ref[2, x:x + 1]
    hx_r = ylo_ref[3, x:x + 1] - TIME_STEP * ((ez[0:1] - ez_m) - _z_up(ey_m))
    hz_r = ylo_ref[4, x:x + 1] - TIME_STEP * ((ey_m_next - ey_m) - (ex[0:1] - ex_m))
    ex_new = keep * ex + drive * (_y_down(hz, hz_r) - _z_down(hy))
    ey_new = keep * ey + drive * (_z_down(hx) - (hz - hz_prev))
    ez_new = keep * ez + drive * ((hy - hy_prev) - _y_down(hx, hx_r))
    return (ex_new, ey_new, ez_new)


def _step_kernel(e_ref, h_ref, keep_ref, drive_ref, xlo_ref, xhi_ref, y_ref, basis_ref,
                 e_out, h_out, y_out, g_out):
    c1_ref = y_ref.at[7, 0:1]
    c2_ref = y_ref.at[8, 0:1]
    yhi_ref = y_ref.at[5:7]
    planes = e_ref.shape[1]
    cells = e_ref.shape[2]
    elec = lambda comp, x: e_ref[comp, x]
    magn = lambda comp, x: h_ref[comp, x]
    hy_prev, hz_prev = _magn_before(elec, xlo_ref, c1_ref)
    sums = [None, None]
    pending = []
    for x in range(planes):
        old = _magn_plane(elec, magn, x, planes, xhi_ref, yhi_ref)
        ex_new, ey_new, ez_new = _elec_plane(
            x, planes, old, hy_prev, hz_prev, y_ref, c2_ref, keep_ref[x], drive_ref[x]
        )
        hx, hy, hz = old[3:]
        e_out[0, x] = ex_new
        e_out[1, x] = ey_new
        e_out[2, x] = ez_new
        h_out[0, x] = hx
        h_out[1, x] = hy
        h_out[2, x] = hz
        last = slice(cells - 1, cells)
        y_out[0, x:x + 1] = ex_new[last]
        y_out[1, x:x + 1] = ey_new[last]
        y_out[2, x:x + 1] = ez_new[last]
        y_out[3, x:x + 1] = hx[last]
        y_out[4, x:x + 1] = hz[last]
        y_out[5, x:x + 1] = ex_new[0:1]
        y_out[6, x:x + 1] = ez_new[0:1]
        hy_prev = hy
        hz_prev = hz
        group = basis_ref.shape[2] // cells
        pending.append((ex_new, ey_new))
        if len(pending) == group:
            for comp in range(2):
                fields = [planes_done[comp] for planes_done in pending]
                stacked = fields[0] if group == 1 else jnp.concatenate(fields, axis=0)
                part = jnp.dot(basis_ref[x // group], stacked, precision=lax.Precision.HIGHEST,
                               preferred_element_type=jnp.float32)
                sums[comp] = part if sums[comp] is None else sums[comp] + part
            pending = []
    depth = e_ref.shape[3]
    for comp in range(2):
        g_out[comp] = sums[comp].T[depth - 3:depth - 2]


def _edge_kernel(e_low, e_high, h_first, h_high,
                 keep_first, keep_last, drive_first, drive_last, xlo_ref, xhi_ref, y_ref,
                 xlo_out, xhi_out, *, planes):
    c1_ref = y_ref.at[7, 0:1]
    c2_ref = y_ref.at[8, 0:1]
    yhi_ref = y_ref.at[5:7]
    e_blocks = {0: (e_low, 0), 1: (e_low, 1), planes - 2: (e_high, 0), planes - 1: (e_high, 1)}
    h_blocks = {0: (h_first, 0), planes - 2: (h_high, 0), planes - 1: (h_high, 1)}
    elec = lambda comp, x: e_blocks[x][0][comp, e_blocks[x][1]]
    magn = lambda comp, x: h_blocks[x][0][comp, h_blocks[x][1]]
    hy_prev, hz_prev = _magn_before(elec, xlo_ref, c1_ref)
    old = _magn_plane(elec, magn, 0, planes, xhi_ref, yhi_ref)
    ex_new, ey_new, ez_new = _elec_plane(
        0, planes, old, hy_prev, hz_prev, y_ref, c2_ref, keep_first[0], drive_first[0]
    )
    xhi_out[0] = ey_new
    xhi_out[1] = ez_new
    penult = _magn_plane(elec, magn, planes - 2, planes, xhi_ref, yhi_ref)
    old = _magn_plane(elec, magn, planes - 1, planes, xhi_ref, yhi_ref)
    ex_new, ey_new, ez_new = _elec_plane(
        planes - 1, planes, old, penult[4], penult[5], y_ref, c2_ref, keep_last[0], drive_last[0]
    )
    xlo_out[0] = ex_new
    xlo_out[1] = ey_new
    xlo_out[2] = ez_new
    xlo_out[3] = old[4]
    xlo_out[4] = old[5]


def _halo_kernel(e_first, e_last, h_last, e_top, e_bottom, h_bottom, xlo_out, xhi_out, y_out):
    planes = e_top.shape[1]
    slab = e_top.shape[2]
    last = slice(slab - 1, slab)
    for x in range(planes):
        y_out[0, x:x + 1] = e_bottom[0, x][last]
        y_out[1, x:x + 1] = e_bottom[1, x][last]
        y_out[2, x:x + 1] = e_bottom[2, x][last]
        y_out[3, x:x + 1] = h_bottom[0, x][last]
        y_out[4, x:x + 1] = h_bottom[2, x][last]
        y_out[5, x:x + 1] = e_top[0, x][0:1]
        y_out[6, x:x + 1] = e_top[2, x][0:1]
    xhi_out[0] = e_first[1, 0]
    xhi_out[1] = e_first[2, 0]
    xlo_out[0] = e_last[0, 0]
    xlo_out[1] = e_last[1, 0]
    xlo_out[2] = e_last[2, 0]
    xlo_out[3] = h_last[1, 0]
    xlo_out[4] = h_last[2, 0]


def exchange_x(xlo, xhi):
    return (shifted(xlo, "gx", 1), shifted(xhi, "gx", -1))


def exchange_y(rows, xlo, xhi):
    cells = xhi.shape[1]
    corners = jnp.zeros((2,) + rows.shape[1:], rows.dtype)
    corners = corners.at[0, 0:1].set(xlo[0, 0:1]).at[1, 0:1].set(xhi[0, cells - 1:cells])
    message = jnp.concatenate([rows, corners])
    if lax.axis_size("gy") == 2:
        return shifted(message, "gy", 1)
    before = shifted(message, "gy", 1)
    after = shifted(message, "gy", -1)
    return jnp.concatenate([before[0:5], after[5:8], before[8:9]])


def trig_basis(angle_orders, cells_x, cells_y):
    size_x = lax.axis_size("gx")
    size_y = lax.axis_size("gy")
    total_x = cells_x * size_x
    total_y = cells_y * size_y
    pos_x = lax.axis_index("gx") * cells_x + jnp.arange(cells_x, dtype=jnp.int32)
    pos_y = lax.axis_index("gy") * cells_y + jnp.arange(cells_y, dtype=jnp.int32)
    order_x = angle_orders[:, 0]
    order_y = angle_orders[:, 1]
    phase_int = (
        order_x[:, None, None] * pos_x[None, :, None] * total_y
        + order_y[:, None, None] * pos_y[None, None, :] * total_x
    ) % (total_x * total_y)
    theta = phase_int.astype(jnp.float32) * (2.0 * math.pi / (total_x * total_y))
    theta = theta.reshape(angle_orders.shape[0], cells_x * cells_y)
    return jnp.concatenate([jnp.cos(theta), jnp.sin(theta)])


def transform(basis, columns):
    return jnp.dot(basis, columns, precision=lax.Precision.HIGHEST, preferred_element_type=jnp.float32)


def flat(plane):
    return plane.reshape(plane.shape[0], -1).T


def scatter_sum(rows, axis, owned):
    count = lax.axis_size(axis)
    index = lax.axis_index(axis)
    if count & (count - 1):
        return lax.psum_scatter(rows, axis, scatter_dimension=0, tiled=True)
    stride = count // 2
    while stride >= 1:
        half = rows.shape[0] // 2
        lower = rows[:half]
        upper = rows[half:]
        high = (index & stride) != 0
        keep = jnp.where(high, upper, lower)
        send = jnp.where(high, lower, upper)
        pairs = [(source, source ^ stride) for source in range(count)]
        rows = keep + lax.ppermute(send, axis, pairs)
        stride //= 2
    return rows


def pair_sum(value, axis):
    count = lax.axis_size(axis)
    if count == 1:
        return value
    if count == 2:
        return value + lax.ppermute(value, axis, [(0, 1), (1, 0)])
    return lax.psum(value, axis)


def local(e_field, h_field, material, eps_table, sigma_table, angle_orders):
    comps, cells_x, cells_y, depth = e_field.shape
    f32 = jnp.float32
    field_shape = jax.ShapeDtypeStruct(e_field.shape, f32)
    xlo_shape = jax.ShapeDtypeStruct((5, cells_y, depth), f32)
    xhi_shape = jax.ShapeDtypeStruct((2, cells_y, depth), f32)
    rows_shape = jax.ShapeDtypeStruct((7, cells_x, depth), f32)
    angle_count = angle_orders.shape[0]
    sums_shape = jax.ShapeDtypeStruct((2, 1, 2 * angle_count), f32)
    step_call = pl.pallas_call(
        _step_kernel, out_shape=(field_shape, field_shape, rows_shape, sums_shape)
    )
    whole = pl.BlockSpec(memory_space=pltpu.VMEM)

    def field_plane(index):
        return pl.BlockSpec((comps, 1, cells_y, depth), lambda i: (0, index, 0, 0))

    def field_pair(index):
        return pl.BlockSpec((comps, 2, cells_y, depth), lambda i: (0, index, 0, 0))

    def coef_plane(index):
        return pl.BlockSpec((1, cells_y, depth), lambda i: (index, 0, 0))

    first = 0
    last = cells_x - 1
    edge_call = pl.pallas_call(
        functools.partial(_edge_kernel, planes=cells_x),
        out_shape=(xlo_shape, xhi_shape),
        grid=(1,),
        in_specs=[field_pair(0), field_pair(cells_x // 2 - 1), field_plane(first),
                  field_pair(cells_x // 2 - 1)]
        + [coef_plane(first), coef_plane(last), coef_plane(first), coef_plane(last)]
        + [whole] * 3,
        out_specs=(whole, whole),
    )
    slab = 8
    slabs = cells_y // slab

    def row_slab(index):
        return pl.BlockSpec((comps, cells_x, slab, depth), lambda i: (0, 0, index, 0))

    xlo, xhi, rows = pl.pallas_call(
        _halo_kernel,
        out_shape=(xlo_shape, xhi_shape, rows_shape),
        grid=(1,),
        in_specs=[field_plane(first), field_plane(last), field_plane(last),
                  row_slab(0), row_slab(slabs - 1), row_slab(slabs - 1)],
        out_specs=(whole, whole, whole),
    )(e_field, e_field, h_field, e_field, e_field, h_field)
    xlo, xhi = exchange_x(xlo, xhi)
    keep, drive = coefficients(material, eps_table, sigma_table)
    keep, drive, xlo, xhi = lax.optimization_barrier((keep, drive, xlo, xhi))
    rows = exchange_y(rows, xlo, xhi)
    basis = trig_basis(angle_orders, cells_x, cells_y)
    group = 2 if cells_x % 2 == 0 else 1
    basis = basis.reshape(2 * angle_count, cells_x // group, group * cells_y).transpose(1, 0, 2)
    basis, rows = lax.optimization_barrier((basis, rows))
    elec = e_field
    magn = h_field
    columns = [[], []]
    for number in range(ITERS):
        if number + 1 < ITERS:
            edges = edge_call(
                elec, elec, magn, magn, keep, keep, drive, drive, xlo, xhi, rows
            )
            next_xlo, next_xhi = exchange_x(*edges)
        elec, magn, new_rows, sums = step_call(elec, magn, keep, drive, xlo, xhi, rows, basis)
        if number + 1 < ITERS:
            xlo, xhi = next_xlo, next_xhi
            rows = exchange_y(new_rows, xlo, xhi)
        weight_cos = math.cos(PHASE_STEP * (number + 1))
        weight_sin = math.sin(PHASE_STEP * (number + 1))
        picked = sums[:, 0]
        for comp in range(2):
            cos_p = picked[comp, :angle_count]
            sin_p = picked[comp, angle_count:]
            columns[comp].append((weight_cos * cos_p - weight_sin * sin_p, -weight_sin * cos_p - weight_cos * sin_p))
    stacked = []
    for comp in range(2):
        real = columns[comp][0][0]
        imag = columns[comp][0][1]
        for more_real, more_imag in columns[comp][1:]:
            real = real + more_real
            imag = imag + more_imag
        stacked += [real, imag]
    columns = stacked
    terms = jnp.stack(columns, axis=1)
    owned = angle_count // lax.axis_size("gx")
    scale = 1.0 / math.sqrt(cells_x * lax.axis_size("gx") * cells_y * lax.axis_size("gy"))
    far_field = scatter_sum(terms, "gx", owned)
    far_field = pair_sum(far_field, "gy") * scale
    return (elec, magn, far_field)


def solution(mesh):
    return jax.shard_map(
        local,
        mesh=mesh,
        in_specs=(
            P(None, ("clip", "gx"), "gy", None),
            P(None, ("clip", "gx"), "gy", None),
            P(("clip", "gx"), "gy", None),
            P(),
            P(),
            P(),
        ),
        out_specs=(
            P(None, ("clip", "gx"), "gy", None),
            P(None, ("clip", "gx"), "gy", None),
            P(("clip", "gx"), None),
        ),
        check_vma=False,
    )
```

```python
import functools
import math

import jax
import jax.numpy as jnp
from jax import lax
from jax.experimental import pallas as pl
from jax.experimental.pallas import tpu as pltpu
from jax.sharding import PartitionSpec as P

ITERS = 4


TIME_STEP = 0.5
PHASE_STEP = 0.9


def shifted(value, axis, steps):
    count = lax.axis_size(axis)
    pairs = [(source, (source + steps) % count) for source in range(count)]
    return lax.ppermute(value, axis, pairs)


def _coef_kernel(eps_ref, sigma_ref, mat_ref, keep_out, drive_out):
    planes = mat_ref.shape[0]
    for x in range(planes):
        material = mat_ref[x]
        permit = jnp.zeros(material.shape, jnp.float32)
        conduct = jnp.zeros(material.shape, jnp.float32)
        for label in range(eps_ref.shape[0]):
            hit = material == label
            permit = jnp.where(hit, eps_ref[label], permit)
            conduct = jnp.where(hit, sigma_ref[label], conduct)
        loss = conduct * TIME_STEP / (2.0 * permit)
        keep_out[x] = (1.0 - loss) / (1.0 + loss)
        drive_out[x] = TIME_STEP / (permit * (1.0 + loss))


def coefficients(material, eps_table, sigma_table):
    scalar = pl.BlockSpec(memory_space=pltpu.SMEM)
    whole = pl.BlockSpec(memory_space=pltpu.VMEM)
    out = jax.ShapeDtypeStruct(material.shape, jnp.float32)
    return pl.pallas_call(
        _coef_kernel,
        out_shape=(out, out),
        in_specs=[scalar, scalar, whole],
        out_specs=(whole, whole),
    )(eps_table, sigma_table, material)


def _z_up(f):
    depth = f.shape[-1]
    lane = lax.broadcasted_iota(jnp.int32, f.shape, 1)
    up = pltpu.roll(f, depth - 1, 1)
    return jnp.where(lane == depth - 1, 0.0, up) - f


def _z_down(f):
    lane = lax.broadcasted_iota(jnp.int32, f.shape, 1)
    down = pltpu.roll(f, 1, 1)
    return f - jnp.where(lane == 0, 0.0, down)


def _y_up(f, row):
    cells = f.shape[0]
    index = lax.broadcasted_iota(jnp.int32, f.shape, 0)
    up = pltpu.roll(f, cells - 1, 0)
    return jnp.where(index == cells - 1, row, up) - f


def _y_down(f, row):
    index = lax.broadcasted_iota(jnp.int32, f.shape, 0)
    down = pltpu.roll(f, 1, 0)
    return f - jnp.where(index == 0, row, down)


def _magn_plane(elec, magn, x, planes, xhi_ref, yhi_ref):
    ex = elec(0, x)
    ey = elec(1, x)
    ez = elec(2, x)
    if x + 1 < planes:
        ey_next = elec(1, x + 1)
        ez_next = elec(2, x + 1)
    else:
        ey_next = xhi_ref[0]
        ez_next = xhi_ref[1]
    hx = magn(0, x) - TIME_STEP * (_y_up(ez, yhi_ref[1, x:x + 1]) - _z_up(ey))
    hy = magn(1, x) - TIME_STEP * (_z_up(ex) - (ez_next - ez))
    hz = magn(2, x) - TIME_STEP * ((ey_next - ey) - _y_up(ex, yhi_ref[0, x:x + 1]))
    return (ex, ey, ez, hx, hy, hz)


def _magn_before(elec, xlo_ref, c1_ref):
    ex_p = xlo_ref[0]
    ey_p = xlo_ref[1]
    ez_p = xlo_ref[2]
    hy = xlo_ref[3] - TIME_STEP * (_z_up(ex_p) - (elec(2, 0) - ez_p))
    hz = xlo_ref[4] - TIME_STEP * ((elec(1, 0) - ey_p) - _y_up(ex_p, c1_ref[...]))
    return (hy, hz)


def _elec_plane(x, planes, old, hy_prev, hz_prev, ylo_ref, c2_ref, keep, drive):
    ex, ey, ez, hx, hy, hz = old
    if x + 1 < planes:
        ey_m_next = ylo_ref[1, x + 1:x + 2]
    else:
        ey_m_next = c2_ref[...]
    ex_m = ylo_ref[0, x:x + 1]
    ey_m = ylo_ref[1, x:x + 1]
    ez_m = ylo_ref[2, x:x + 1]
    hx_r = ylo_ref[3, x:x + 1] - TIME_STEP * ((ez[0:1] - ez_m) - _z_up(ey_m))
    hz_r = ylo_ref[4, x:x + 1] - TIME_STEP * ((ey_m_next - ey_m) - (ex[0:1] - ex_m))
    ex_new = keep * ex + drive * (_y_down(hz, hz_r) - _z_down(hy))
    ey_new = keep * ey + drive * (_z_down(hx) - (hz - hz_prev))
    ez_new = keep * ez + drive * ((hy - hy_prev) - _y_down(hx, hx_r))
    return (ex_new, ey_new, ez_new)


def _step_kernel(e_ref, h_ref, keep_ref, drive_ref, xlo_ref, xhi_ref, y_ref, corner_ref, basis_ref,
                 e_out, h_out, y_out, g_out):
    c1_ref = corner_ref.at[0, 0:1]
    c2_ref = corner_ref.at[1, 0:1]
    yhi_ref = y_ref.at[5:7]
    planes = e_ref.shape[1]
    cells = e_ref.shape[2]
    elec = lambda comp, x: e_ref[comp, x]
    magn = lambda comp, x: h_ref[comp, x]
    hy_prev, hz_prev = _magn_before(elec, xlo_ref, c1_ref)
    sums = [None, None]
    pending = []
    for x in range(planes):
        old = _magn_plane(elec, magn, x, planes, xhi_ref, yhi_ref)
        ex_new, ey_new, ez_new = _elec_plane(
            x, planes, old, hy_prev, hz_prev, y_ref, c2_ref, keep_ref[x], drive_ref[x]
        )
        hx, hy, hz = old[3:]
        e_out[0, x] = ex_new
        e_out[1, x] = ey_new
        e_out[2, x] = ez_new
        h_out[0, x] = hx
        h_out[1, x] = hy
        h_out[2, x] = hz
        last = slice(cells - 1, cells)
        y_out[0, x:x + 1] = ex_new[last]
        y_out[1, x:x + 1] = ey_new[last]
        y_out[2, x:x + 1] = ez_new[last]
        y_out[3, x:x + 1] = hx[last]
        y_out[4, x:x + 1] = hz[last]
        y_out[5, x:x + 1] = ex_new[0:1]
        y_out[6, x:x + 1] = ez_new[0:1]
        hy_prev = hy
        hz_prev = hz
        group = basis_ref.shape[2] // cells
        pending.append((ex_new, ey_new))
        if len(pending) == group:
            for comp in range(2):
                fields = [planes_done[comp] for planes_done in pending]
                stacked = fields[0] if group == 1 else jnp.concatenate(fields, axis=0)
                part = jnp.dot(basis_ref[x // group], stacked, precision=lax.Precision.HIGHEST,
                               preferred_element_type=jnp.float32)
                sums[comp] = part if sums[comp] is None else sums[comp] + part
            pending = []
    depth = e_ref.shape[3]
    for comp in range(2):
        g_out[comp] = sums[comp].T[depth - 3:depth - 2]


def _edge_kernel(e_first, e_second, e_penult, e_last, h_first, h_penult, h_last,
                 keep_first, keep_last, drive_first, drive_last, xlo_ref, xhi_ref, y_ref, corner_ref,
                 xlo_out, xhi_out, *, planes):
    c1_ref = corner_ref.at[0, 0:1]
    c2_ref = corner_ref.at[1, 0:1]
    yhi_ref = y_ref.at[5:7]
    e_blocks = {0: e_first, 1: e_second, planes - 2: e_penult, planes - 1: e_last}
    h_blocks = {0: h_first, planes - 2: h_penult, planes - 1: h_last}
    elec = lambda comp, x: e_blocks[x][comp, 0]
    magn = lambda comp, x: h_blocks[x][comp, 0]
    hy_prev, hz_prev = _magn_before(elec, xlo_ref, c1_ref)
    old = _magn_plane(elec, magn, 0, planes, xhi_ref, yhi_ref)
    ex_new, ey_new, ez_new = _elec_plane(
        0, planes, old, hy_prev, hz_prev, y_ref, c2_ref, keep_first[0], drive_first[0]
    )
    xhi_out[0] = ey_new
    xhi_out[1] = ez_new
    penult = _magn_plane(elec, magn, planes - 2, planes, xhi_ref, yhi_ref)
    old = _magn_plane(elec, magn, planes - 1, planes, xhi_ref, yhi_ref)
    ex_new, ey_new, ez_new = _elec_plane(
        planes - 1, planes, old, penult[4], penult[5], y_ref, c2_ref, keep_last[0], drive_last[0]
    )
    xlo_out[0] = ex_new
    xlo_out[1] = ey_new
    xlo_out[2] = ez_new
    xlo_out[3] = old[4]
    xlo_out[4] = old[5]


def _halo_kernel(e_first, e_last, h_last, e_top, e_bottom, h_bottom, xlo_out, xhi_out, y_out):
    planes = e_top.shape[1]
    slab = e_top.shape[2]
    last = slice(slab - 1, slab)
    for x in range(planes):
        y_out[0, x:x + 1] = e_bottom[0, x][last]
        y_out[1, x:x + 1] = e_bottom[1, x][last]
        y_out[2, x:x + 1] = e_bottom[2, x][last]
        y_out[3, x:x + 1] = h_bottom[0, x][last]
        y_out[4, x:x + 1] = h_bottom[2, x][last]
        y_out[5, x:x + 1] = e_top[0, x][0:1]
        y_out[6, x:x + 1] = e_top[2, x][0:1]
    xhi_out[0] = e_first[1, 0]
    xhi_out[1] = e_first[2, 0]
    xlo_out[0] = e_last[0, 0]
    xlo_out[1] = e_last[1, 0]
    xlo_out[2] = e_last[2, 0]
    xlo_out[3] = h_last[1, 0]
    xlo_out[4] = h_last[2, 0]


def exchange_x(xlo, xhi):
    return (shifted(xlo, "gx", 1), shifted(xhi, "gx", -1))


def exchange_y(rows):
    if lax.axis_size("gy") == 2:
        return shifted(rows, "gy", 1)
    before = shifted(rows, "gy", 1)
    after = shifted(rows, "gy", -1)
    return jnp.concatenate([before[0:5], after[5:7]])


def exchange_corners(xlo, xhi, like):
    cells = xhi.shape[1]
    corners = jnp.zeros((2,) + like.shape[1:], like.dtype)
    corners = corners.at[0, 0:1].set(xlo[0, 0:1]).at[1, 0:1].set(xhi[0, cells - 1:cells])
    if lax.axis_size("gy") == 2:
        return shifted(corners, "gy", 1)
    before = shifted(corners, "gy", 1)
    after = shifted(corners, "gy", -1)
    return jnp.concatenate([after[0:1], before[1:2]])


def trig_basis(angle_orders, cells_x, cells_y):
    size_x = lax.axis_size("gx")
    size_y = lax.axis_size("gy")
    total_x = cells_x * size_x
    total_y = cells_y * size_y
    pos_x = lax.axis_index("gx") * cells_x + jnp.arange(cells_x, dtype=jnp.int32)
    pos_y = lax.axis_index("gy") * cells_y + jnp.arange(cells_y, dtype=jnp.int32)
    order_x = angle_orders[:, 0]
    order_y = angle_orders[:, 1]
    phase_int = (
        order_x[:, None, None] * pos_x[None, :, None] * total_y
        + order_y[:, None, None] * pos_y[None, None, :] * total_x
    ) % (total_x * total_y)
    theta = phase_int.astype(jnp.float32) * (2.0 * math.pi / (total_x * total_y))
    theta = theta.reshape(angle_orders.shape[0], cells_x * cells_y)
    return jnp.concatenate([jnp.cos(theta), jnp.sin(theta)])


def transform(basis, columns):
    return jnp.dot(basis, columns, precision=lax.Precision.HIGHEST, preferred_element_type=jnp.float32)


def flat(plane):
    return plane.reshape(plane.shape[0], -1).T


def scatter_sum(rows, axis, owned):
    count = lax.axis_size(axis)
    index = lax.axis_index(axis)
    if count & (count - 1):
        return lax.psum_scatter(rows, axis, scatter_dimension=0, tiled=True)
    stride = count // 2
    while stride >= 1:
        half = rows.shape[0] // 2
        lower = rows[:half]
        upper = rows[half:]
        high = (index & stride) != 0
        keep = jnp.where(high, upper, lower)
        send = jnp.where(high, lower, upper)
        pairs = [(source, source ^ stride) for source in range(count)]
        rows = keep + lax.ppermute(send, axis, pairs)
        stride //= 2
    return rows


def pair_sum(value, axis):
    count = lax.axis_size(axis)
    if count == 1:
        return value
    if count == 2:
        return value + lax.ppermute(value, axis, [(0, 1), (1, 0)])
    return lax.psum(value, axis)


def local(e_field, h_field, material, eps_table, sigma_table, angle_orders):
    comps, cells_x, cells_y, depth = e_field.shape
    f32 = jnp.float32
    field_shape = jax.ShapeDtypeStruct(e_field.shape, f32)
    xlo_shape = jax.ShapeDtypeStruct((5, cells_y, depth), f32)
    xhi_shape = jax.ShapeDtypeStruct((2, cells_y, depth), f32)
    rows_shape = jax.ShapeDtypeStruct((7, cells_x, depth), f32)
    angle_count = angle_orders.shape[0]
    sums_shape = jax.ShapeDtypeStruct((2, 1, 2 * angle_count), f32)
    step_call = pl.pallas_call(
        _step_kernel, out_shape=(field_shape, field_shape, rows_shape, sums_shape)
    )
    whole = pl.BlockSpec(memory_space=pltpu.VMEM)

    def field_plane(index):
        return pl.BlockSpec((comps, 1, cells_y, depth), lambda i: (0, index, 0, 0))

    def coef_plane(index):
        return pl.BlockSpec((1, cells_y, depth), lambda i: (index, 0, 0))

    first = 0
    last = cells_x - 1
    edge_call = pl.pallas_call(
        functools.partial(_edge_kernel, planes=cells_x),
        out_shape=(xlo_shape, xhi_shape),
        grid=(1,),
        in_specs=[field_plane(i) for i in (first, 1, last - 1, last)]
        + [field_plane(i) for i in (first, last - 1, last)]
        + [coef_plane(first), coef_plane(last), coef_plane(first), coef_plane(last)]
        + [whole] * 4,
        out_specs=(whole, whole),
    )
    slab = 8
    slabs = cells_y // slab

    def row_slab(index):
        return pl.BlockSpec((comps, cells_x, slab, depth), lambda i: (0, 0, index, 0))

    xlo, xhi, rows = pl.pallas_call(
        _halo_kernel,
        out_shape=(xlo_shape, xhi_shape, rows_shape),
        grid=(1,),
        in_specs=[field_plane(first), field_plane(last), field_plane(last),
                  row_slab(0), row_slab(slabs - 1), row_slab(slabs - 1)],
        out_specs=(whole, whole, whole),
    )(e_field, e_field, h_field, e_field, e_field, h_field)
    xlo, xhi = exchange_x(xlo, xhi)
    keep, drive = coefficients(material, eps_table, sigma_table)
    keep, drive, xlo, xhi = lax.optimization_barrier((keep, drive, xlo, xhi))
    rows = exchange_y(rows)
    corners = exchange_corners(xlo, xhi, rows)
    basis = trig_basis(angle_orders, cells_x, cells_y)
    group = 2 if cells_x % 2 == 0 else 1
    basis = basis.reshape(2 * angle_count, cells_x // group, group * cells_y).transpose(1, 0, 2)
    basis, rows, corners = lax.optimization_barrier((basis, rows, corners))
    elec = e_field
    magn = h_field
    columns = [[], []]
    for number in range(ITERS):
        if number + 1 < ITERS:
            edges = edge_call(
                elec, elec, elec, elec, magn, magn, magn, keep, keep, drive, drive, xlo, xhi, rows, corners
            )
            next_xlo, next_xhi = exchange_x(*edges)
        elec, magn, new_rows, sums = step_call(elec, magn, keep, drive, xlo, xhi, rows, corners, basis)
        if number + 1 < ITERS:
            rows = exchange_y(new_rows)
            xlo, xhi = next_xlo, next_xhi
            corners = exchange_corners(xlo, xhi, rows)
        weight_cos = math.cos(PHASE_STEP * (number + 1))
        weight_sin = math.sin(PHASE_STEP * (number + 1))
        picked = sums[:, 0]
        for comp in range(2):
            cos_p = picked[comp, :angle_count]
            sin_p = picked[comp, angle_count:]
            columns[comp].append((weight_cos * cos_p - weight_sin * sin_p, -weight_sin * cos_p - weight_cos * sin_p))
    stacked = []
    for comp in range(2):
        real = columns[comp][0][0]
        imag = columns[comp][0][1]
        for more_real, more_imag in columns[comp][1:]:
            real = real + more_real
            imag = imag + more_imag
        stacked += [real, imag]
    columns = stacked
    terms = jnp.stack(columns, axis=1)
    owned = angle_count // lax.axis_size("gx")
    scale = 1.0 / math.sqrt(cells_x * lax.axis_size("gx") * cells_y * lax.axis_size("gy"))
    far_field = scatter_sum(terms, "gx", owned)
    far_field = pair_sum(far_field, "gy") * scale
    return (elec, magn, far_field)


def solution(mesh):
    return jax.shard_map(
        local,
        mesh=mesh,
        in_specs=(
            P(None, ("clip", "gx"), "gy", None),
            P(None, ("clip", "gx"), "gy", None),
            P(("clip", "gx"), "gy", None),
            P(),
            P(),
            P(),
        ),
        out_specs=(
            P(None, ("clip", "gx"), "gy", None),
            P(None, ("clip", "gx"), "gy", None),
            P(("clip", "gx"), None),
        ),
        check_vma=False,
    )
```

```python
import functools
import math

import jax
import jax.numpy as jnp
from jax import lax
from jax.experimental import pallas as pl
from jax.experimental.pallas import tpu as pltpu
from jax.sharding import PartitionSpec as P

ITERS = 4


TIME_STEP = 0.5
PHASE_STEP = 0.9


def shifted(value, axis, steps):
    count = lax.axis_size(axis)
    pairs = [(source, (source + steps) % count) for source in range(count)]
    return lax.ppermute(value, axis, pairs)


def _coef_kernel(eps_ref, sigma_ref, mat_ref, keep_out, drive_out):
    planes = mat_ref.shape[0]
    for x in range(planes):
        material = mat_ref[x]
        permit = jnp.zeros(material.shape, jnp.float32)
        conduct = jnp.zeros(material.shape, jnp.float32)
        for label in range(eps_ref.shape[0]):
            hit = material == label
            permit = jnp.where(hit, eps_ref[label], permit)
            conduct = jnp.where(hit, sigma_ref[label], conduct)
        loss = conduct * TIME_STEP / (2.0 * permit)
        keep_out[x] = (1.0 - loss) / (1.0 + loss)
        drive_out[x] = TIME_STEP / (permit * (1.0 + loss))


def coefficients(material, eps_table, sigma_table):
    scalar = pl.BlockSpec(memory_space=pltpu.SMEM)
    whole = pl.BlockSpec(memory_space=pltpu.VMEM)
    out = jax.ShapeDtypeStruct(material.shape, jnp.float32)
    return pl.pallas_call(
        _coef_kernel,
        out_shape=(out, out),
        in_specs=[scalar, scalar, whole],
        out_specs=(whole, whole),
    )(eps_table, sigma_table, material)


def _z_up(f):
    depth = f.shape[-1]
    lane = lax.broadcasted_iota(jnp.int32, f.shape, 1)
    up = pltpu.roll(f, depth - 1, 1)
    return jnp.where(lane == depth - 1, 0.0, up) - f


def _z_down(f):
    lane = lax.broadcasted_iota(jnp.int32, f.shape, 1)
    down = pltpu.roll(f, 1, 1)
    return f - jnp.where(lane == 0, 0.0, down)


def _y_up(f, row):
    cells = f.shape[0]
    index = lax.broadcasted_iota(jnp.int32, f.shape, 0)
    up = pltpu.roll(f, cells - 1, 0)
    return jnp.where(index == cells - 1, row, up) - f


def _y_down(f, row):
    index = lax.broadcasted_iota(jnp.int32, f.shape, 0)
    down = pltpu.roll(f, 1, 0)
    return f - jnp.where(index == 0, row, down)


def _magn_plane(elec, magn, x, planes, xhi_ref, yhi_ref):
    ex = elec(0, x)
    ey = elec(1, x)
    ez = elec(2, x)
    if x + 1 < planes:
        ey_next = elec(1, x + 1)
        ez_next = elec(2, x + 1)
    else:
        ey_next = xhi_ref[0]
        ez_next = xhi_ref[1]
    hx = magn(0, x) - TIME_STEP * (_y_up(ez, yhi_ref[1, x:x + 1]) - _z_up(ey))
    hy = magn(1, x) - TIME_STEP * (_z_up(ex) - (ez_next - ez))
    hz = magn(2, x) - TIME_STEP * ((ey_next - ey) - _y_up(ex, yhi_ref[0, x:x + 1]))
    return (ex, ey, ez, hx, hy, hz)


def _magn_before(elec, xlo_ref, c1_ref):
    ex_p = xlo_ref[0]
    ey_p = xlo_ref[1]
    ez_p = xlo_ref[2]
    hy = xlo_ref[3] - TIME_STEP * (_z_up(ex_p) - (elec(2, 0) - ez_p))
    hz = xlo_ref[4] - TIME_STEP * ((elec(1, 0) - ey_p) - _y_up(ex_p, c1_ref[...]))
    return (hy, hz)


def _elec_plane(x, planes, old, hy_prev, hz_prev, ylo_ref, c2_ref, keep, drive):
    ex, ey, ez, hx, hy, hz = old
    if x + 1 < planes:
        ey_m_next = ylo_ref[1, x + 1:x + 2]
    else:
        ey_m_next = c2_ref[...]
    ex_m = ylo_ref[0, x:x + 1]
    ey_m = ylo_ref[1, x:x + 1]
    ez_m = ylo_ref[2, x:x + 1]
    hx_r = ylo_ref[3, x:x + 1] - TIME_STEP * ((ez[0:1] - ez_m) - _z_up(ey_m))
    hz_r = ylo_ref[4, x:x + 1] - TIME_STEP * ((ey_m_next - ey_m) - (ex[0:1] - ex_m))
    ex_new = keep * ex + drive * (_y_down(hz, hz_r) - _z_down(hy))
    ey_new = keep * ey + drive * (_z_down(hx) - (hz - hz_prev))
    ez_new = keep * ez + drive * ((hy - hy_prev) - _y_down(hx, hx_r))
    return (ex_new, ey_new, ez_new)


def _step_kernel(e_ref, h_ref, keep_ref, drive_ref, xlo_ref, xhi_ref, y_ref, corner_ref, basis_ref,
                 e_out, h_out, y_out, g_out):
    c1_ref = corner_ref.at[0, 0:1]
    c2_ref = corner_ref.at[1, 0:1]
    yhi_ref = y_ref.at[5:7]
    planes = e_ref.shape[1]
    cells = e_ref.shape[2]
    elec = lambda comp, x: e_ref[comp, x]
    magn = lambda comp, x: h_ref[comp, x]
    hy_prev, hz_prev = _magn_before(elec, xlo_ref, c1_ref)
    sums = [None, None]
    pending = []
    for x in range(planes):
        old = _magn_plane(elec, magn, x, planes, xhi_ref, yhi_ref)
        ex_new, ey_new, ez_new = _elec_plane(
            x, planes, old, hy_prev, hz_prev, y_ref, c2_ref, keep_ref[x], drive_ref[x]
        )
        hx, hy, hz = old[3:]
        e_out[0, x] = ex_new
        e_out[1, x] = ey_new
        e_out[2, x] = ez_new
        h_out[0, x] = hx
        h_out[1, x] = hy
        h_out[2, x] = hz
        last = slice(cells - 1, cells)
        y_out[0, x:x + 1] = ex_new[last]
        y_out[1, x:x + 1] = ey_new[last]
        y_out[2, x:x + 1] = ez_new[last]
        y_out[3, x:x + 1] = hx[last]
        y_out[4, x:x + 1] = hz[last]
        y_out[5, x:x + 1] = ex_new[0:1]
        y_out[6, x:x + 1] = ez_new[0:1]
        hy_prev = hy
        hz_prev = hz
        group = basis_ref.shape[2] // cells
        pending.append((ex_new, ey_new))
        if len(pending) == group:
            for comp in range(2):
                fields = [planes_done[comp] for planes_done in pending]
                stacked = fields[0] if group == 1 else jnp.concatenate(fields, axis=0)
                part = jnp.dot(basis_ref[x // group], stacked, precision=lax.Precision.HIGHEST,
                               preferred_element_type=jnp.float32)
                sums[comp] = part if sums[comp] is None else sums[comp] + part
            pending = []
    depth = e_ref.shape[3]
    for comp in range(2):
        g_out[comp] = sums[comp].T[depth - 3:depth - 2]


def _edge_kernel(e_first, e_second, e_penult, e_last, h_first, h_penult, h_last,
                 keep_first, keep_last, drive_first, drive_last, xlo_ref, xhi_ref, y_ref, corner_ref,
                 xlo_out, xhi_out, *, planes):
    c1_ref = corner_ref.at[0, 0:1]
    c2_ref = corner_ref.at[1, 0:1]
    yhi_ref = y_ref.at[5:7]
    e_blocks = {0: e_first, 1: e_second, planes - 2: e_penult, planes - 1: e_last}
    h_blocks = {0: h_first, planes - 2: h_penult, planes - 1: h_last}
    elec = lambda comp, x: e_blocks[x][comp, 0]
    magn = lambda comp, x: h_blocks[x][comp, 0]
    hy_prev, hz_prev = _magn_before(elec, xlo_ref, c1_ref)
    old = _magn_plane(elec, magn, 0, planes, xhi_ref, yhi_ref)
    ex_new, ey_new, ez_new = _elec_plane(
        0, planes, old, hy_prev, hz_prev, y_ref, c2_ref, keep_first[0], drive_first[0]
    )
    xhi_out[0] = ey_new
    xhi_out[1] = ez_new
    penult = _magn_plane(elec, magn, planes - 2, planes, xhi_ref, yhi_ref)
    old = _magn_plane(elec, magn, planes - 1, planes, xhi_ref, yhi_ref)
    ex_new, ey_new, ez_new = _elec_plane(
        planes - 1, planes, old, penult[4], penult[5], y_ref, c2_ref, keep_last[0], drive_last[0]
    )
    xlo_out[0] = ex_new
    xlo_out[1] = ey_new
    xlo_out[2] = ez_new
    xlo_out[3] = old[4]
    xlo_out[4] = old[5]


def _edge_first_kernel(e_first, e_second, h_first, keep_first, drive_first, xlo_ref, y_ref,
                       corner_ref, xhi_out, *, planes):
    c1_ref = corner_ref.at[0, 0:1]
    c2_ref = corner_ref.at[1, 0:1]
    yhi_ref = y_ref.at[5:7]
    e_blocks = {0: e_first, 1: e_second}
    elec = lambda comp, x: e_blocks[x][comp, 0]
    magn = lambda comp, x: h_first[comp, 0]
    hy_prev, hz_prev = _magn_before(elec, xlo_ref, c1_ref)
    old = _magn_plane(elec, magn, 0, planes, None, yhi_ref)
    ex_new, ey_new, ez_new = _elec_plane(
        0, planes, old, hy_prev, hz_prev, y_ref, c2_ref, keep_first[0], drive_first[0]
    )
    xhi_out[0] = ey_new
    xhi_out[1] = ez_new


def _edge_last_kernel(e_penult, e_last, h_penult, h_last, keep_last, drive_last, xhi_ref, y_ref,
                      corner_ref, xlo_out, *, planes):
    c2_ref = corner_ref.at[1, 0:1]
    yhi_ref = y_ref.at[5:7]
    e_blocks = {planes - 2: e_penult, planes - 1: e_last}
    h_blocks = {planes - 2: h_penult, planes - 1: h_last}
    elec = lambda comp, x: e_blocks[x][comp, 0]
    magn = lambda comp, x: h_blocks[x][comp, 0]
    penult = _magn_plane(elec, magn, planes - 2, planes, xhi_ref, yhi_ref)
    old = _magn_plane(elec, magn, planes - 1, planes, xhi_ref, yhi_ref)
    ex_new, ey_new, ez_new = _elec_plane(
        planes - 1, planes, old, penult[4], penult[5], y_ref, c2_ref, keep_last[0], drive_last[0]
    )
    xlo_out[0] = ex_new
    xlo_out[1] = ey_new
    xlo_out[2] = ez_new
    xlo_out[3] = old[4]
    xlo_out[4] = old[5]


def _halo_kernel(e_first, e_last, h_last, e_top, e_bottom, h_bottom, xlo_out, xhi_out, y_out):
    planes = e_top.shape[1]
    slab = e_top.shape[2]
    last = slice(slab - 1, slab)
    for x in range(planes):
        y_out[0, x:x + 1] = e_bottom[0, x][last]
        y_out[1, x:x + 1] = e_bottom[1, x][last]
        y_out[2, x:x + 1] = e_bottom[2, x][last]
        y_out[3, x:x + 1] = h_bottom[0, x][last]
        y_out[4, x:x + 1] = h_bottom[2, x][last]
        y_out[5, x:x + 1] = e_top[0, x][0:1]
        y_out[6, x:x + 1] = e_top[2, x][0:1]
    xhi_out[0] = e_first[1, 0]
    xhi_out[1] = e_first[2, 0]
    xlo_out[0] = e_last[0, 0]
    xlo_out[1] = e_last[1, 0]
    xlo_out[2] = e_last[2, 0]
    xlo_out[3] = h_last[1, 0]
    xlo_out[4] = h_last[2, 0]


def exchange_x(xlo, xhi):
    return (shifted(xlo, "gx", 1), shifted(xhi, "gx", -1))


def exchange_y(rows):
    if lax.axis_size("gy") == 2:
        return shifted(rows, "gy", 1)
    before = shifted(rows, "gy", 1)
    after = shifted(rows, "gy", -1)
    return jnp.concatenate([before[0:5], after[5:7]])


def exchange_corners(xlo, xhi, like):
    cells = xhi.shape[1]
    corners = jnp.zeros((2,) + like.shape[1:], like.dtype)
    corners = corners.at[0, 0:1].set(xlo[0, 0:1]).at[1, 0:1].set(xhi[0, cells - 1:cells])
    if lax.axis_size("gy") == 2:
        return shifted(corners, "gy", 1)
    before = shifted(corners, "gy", 1)
    after = shifted(corners, "gy", -1)
    return jnp.concatenate([after[0:1], before[1:2]])


def trig_basis(angle_orders, cells_x, cells_y):
    size_x = lax.axis_size("gx")
    size_y = lax.axis_size("gy")
    total_x = cells_x * size_x
    total_y = cells_y * size_y
    pos_x = lax.axis_index("gx") * cells_x + jnp.arange(cells_x, dtype=jnp.int32)
    pos_y = lax.axis_index("gy") * cells_y + jnp.arange(cells_y, dtype=jnp.int32)
    order_x = angle_orders[:, 0]
    order_y = angle_orders[:, 1]
    phase_int = (
        order_x[:, None, None] * pos_x[None, :, None] * total_y
        + order_y[:, None, None] * pos_y[None, None, :] * total_x
    ) % (total_x * total_y)
    theta = phase_int.astype(jnp.float32) * (2.0 * math.pi / (total_x * total_y))
    theta = theta.reshape(angle_orders.shape[0], cells_x * cells_y)
    return jnp.concatenate([jnp.cos(theta), jnp.sin(theta)])


def transform(basis, columns):
    return jnp.dot(basis, columns, precision=lax.Precision.HIGHEST, preferred_element_type=jnp.float32)


def flat(plane):
    return plane.reshape(plane.shape[0], -1).T


def scatter_sum(rows, axis, owned):
    count = lax.axis_size(axis)
    index = lax.axis_index(axis)
    if count & (count - 1):
        return lax.psum_scatter(rows, axis, scatter_dimension=0, tiled=True)
    stride = count // 2
    while stride >= 1:
        half = rows.shape[0] // 2
        lower = rows[:half]
        upper = rows[half:]
        high = (index & stride) != 0
        keep = jnp.where(high, upper, lower)
        send = jnp.where(high, lower, upper)
        pairs = [(source, source ^ stride) for source in range(count)]
        rows = keep + lax.ppermute(send, axis, pairs)
        stride //= 2
    return rows


def pair_sum(value, axis):
    count = lax.axis_size(axis)
    if count == 1:
        return value
    if count == 2:
        return value + lax.ppermute(value, axis, [(0, 1), (1, 0)])
    return lax.psum(value, axis)


def local(e_field, h_field, material, eps_table, sigma_table, angle_orders):
    comps, cells_x, cells_y, depth = e_field.shape
    f32 = jnp.float32
    field_shape = jax.ShapeDtypeStruct(e_field.shape, f32)
    xlo_shape = jax.ShapeDtypeStruct((5, cells_y, depth), f32)
    xhi_shape = jax.ShapeDtypeStruct((2, cells_y, depth), f32)
    rows_shape = jax.ShapeDtypeStruct((7, cells_x, depth), f32)
    angle_count = angle_orders.shape[0]
    sums_shape = jax.ShapeDtypeStruct((2, 1, 2 * angle_count), f32)
    step_call = pl.pallas_call(
        _step_kernel, out_shape=(field_shape, field_shape, rows_shape, sums_shape)
    )
    whole = pl.BlockSpec(memory_space=pltpu.VMEM)

    def field_plane(index):
        return pl.BlockSpec((comps, 1, cells_y, depth), lambda i: (0, index, 0, 0))

    def coef_plane(index):
        return pl.BlockSpec((1, cells_y, depth), lambda i: (index, 0, 0))

    first = 0
    last = cells_x - 1
    edge_first_call = pl.pallas_call(
        functools.partial(_edge_first_kernel, planes=cells_x),
        out_shape=xhi_shape,
        grid=(1,),
        in_specs=[field_plane(first), field_plane(1), field_plane(first), coef_plane(first),
                  coef_plane(first)] + [whole] * 3,
        out_specs=whole,
    )
    edge_last_call = pl.pallas_call(
        functools.partial(_edge_last_kernel, planes=cells_x),
        out_shape=xlo_shape,
        grid=(1,),
        in_specs=[field_plane(last - 1), field_plane(last), field_plane(last - 1), field_plane(last),
                  coef_plane(last), coef_plane(last)] + [whole] * 3,
        out_specs=whole,
    )
    slab = 8
    slabs = cells_y // slab

    def row_slab(index):
        return pl.BlockSpec((comps, cells_x, slab, depth), lambda i: (0, 0, index, 0))

    xlo, xhi, rows = pl.pallas_call(
        _halo_kernel,
        out_shape=(xlo_shape, xhi_shape, rows_shape),
        grid=(1,),
        in_specs=[field_plane(first), field_plane(last), field_plane(last),
                  row_slab(0), row_slab(slabs - 1), row_slab(slabs - 1)],
        out_specs=(whole, whole, whole),
    )(e_field, e_field, h_field, e_field, e_field, h_field)
    xlo, xhi = exchange_x(xlo, xhi)
    keep, drive = coefficients(material, eps_table, sigma_table)
    keep, drive, xlo, xhi = lax.optimization_barrier((keep, drive, xlo, xhi))
    rows = exchange_y(rows)
    corners = exchange_corners(xlo, xhi, rows)
    basis = trig_basis(angle_orders, cells_x, cells_y)
    group = 2 if cells_x % 2 == 0 else 1
    basis = basis.reshape(2 * angle_count, cells_x // group, group * cells_y).transpose(1, 0, 2)
    basis, rows, corners = lax.optimization_barrier((basis, rows, corners))
    elec = e_field
    magn = h_field
    columns = [[], []]
    for number in range(ITERS):
        if number + 1 < ITERS:
            next_xhi = shifted(edge_first_call(elec, elec, magn, keep, drive, xlo, rows, corners), "gx", -1)
            next_xlo = shifted(
                edge_last_call(elec, elec, magn, magn, keep, drive, xhi, rows, corners), "gx", 1
            )
        elec, magn, new_rows, sums = step_call(elec, magn, keep, drive, xlo, xhi, rows, corners, basis)
        if number + 1 < ITERS:
            rows = exchange_y(new_rows)
            xlo, xhi = next_xlo, next_xhi
            corners = exchange_corners(xlo, xhi, rows)
        weight_cos = math.cos(PHASE_STEP * (number + 1))
        weight_sin = math.sin(PHASE_STEP * (number + 1))
        picked = sums[:, 0]
        for comp in range(2):
            cos_p = picked[comp, :angle_count]
            sin_p = picked[comp, angle_count:]
            columns[comp].append((weight_cos * cos_p - weight_sin * sin_p, -weight_sin * cos_p - weight_cos * sin_p))
    stacked = []
    for comp in range(2):
        real = columns[comp][0][0]
        imag = columns[comp][0][1]
        for more_real, more_imag in columns[comp][1:]:
            real = real + more_real
            imag = imag + more_imag
        stacked += [real, imag]
    columns = stacked
    terms = jnp.stack(columns, axis=1)
    owned = angle_count // lax.axis_size("gx")
    scale = 1.0 / math.sqrt(cells_x * lax.axis_size("gx") * cells_y * lax.axis_size("gy"))
    far_field = scatter_sum(terms, "gx", owned)
    far_field = pair_sum(far_field, "gy") * scale
    return (elec, magn, far_field)


def solution(mesh):
    return jax.shard_map(
        local,
        mesh=mesh,
        in_specs=(
            P(None, ("clip", "gx"), "gy", None),
            P(None, ("clip", "gx"), "gy", None),
            P(("clip", "gx"), "gy", None),
            P(),
            P(),
            P(),
        ),
        out_specs=(
            P(None, ("clip", "gx"), "gy", None),
            P(None, ("clip", "gx"), "gy", None),
            P(("clip", "gx"), None),
        ),
        check_vma=False,
    )
```
